32 devices in a mesh: side: 4 (over z), slab: 8 (over y, x, core).
Axes of the slice: x: 2, y: 2, z: 4, core: 2. Of those that a mesh axis runs over, the one named last changes fastest.
Arguments:
- flow_force: float32 [4, 64, 64, 512], P('side', 'slab'), may hold values from -6 to 6
- flow_coef: float32 [4, 64, 64, 512], P('side', 'slab'), may hold values from 0.1 to 1.5
- flow_init: float32 [4, 64, 64, 512], P('side', 'slab'), may hold values from -6 to 6
- compliance: float32 [64, 512, 512], P('slab')
- shell_load: float32 [64, 512], P('slab')
- disp_init: float32 [64, 512], P('slab'), may hold values from -3 to 3
- patch_len: int32 [64], P('slab'), may hold values from 256 to 512
- owner: int32 [64, 1], P('slab'), may hold values from 0 to 2; in each aligned block of 8 rows (0 to 7, 8 to 15, ...) at most 4 rows name the same one
- block_row: int32 [64], P('slab'), may hold values from 0 to 7
Outputs:
- disp_next: float32 [4, 64, 512], P('side', 'slab')
- residual: float32 [4, 64, 512], P('side', 'slab')
- flow_final: float32 [4, 64, 64, 512], P('side', 'slab')
The draws below stay inside these ranges and needn't reach their ends.
Inputs may be any that keep to these rules, and one draw needn't show every extreme that they name: Within the patch blocks of one shell device (aligned blocks of 8), no sector is the owner of more than 4 blocks.
All inputs are finite; a program needn't handle non-finite values.
Results may differ from the reference program's by a relative error of at most 0.0003.
Values sent between devices are 32-bit elements; how exact they have to be, the bound alone decides.
No kernel may reach another device: no remote copies, remote signals or barrier semaphores. Data moves between devices by JAX's collectives and lax.ppermute only.
A program may use at most 128 MiB of HBM per device.

```python
import math
import jax
import jax.numpy as jnp
import numpy as np
from jax import lax

CX = 8
NZF = 64
NY = 512
PB = 8
SWEEPS = 4
CAP = 4
NX = 64
PATCHES = 64
N_SIDE = 4


def draw_compliance(key, part):
    key_off = jax.random.fold_in(key, 11)
    key_dia = jax.random.fold_in(key, 12)
    offdiag = jax.random.normal(key_off, (PATCHES, NY, NY), jnp.float32)
    diagonal = jax.random.uniform(key_dia, (PATCHES, NY), jnp.float32, 0.4, 0.6)
    identity = jnp.eye(NY, dtype=jnp.float32)
    return identity[None, :, :] * diagonal[:, :, None] + offdiag * (0.4 / NY ** 0.5)


def draw_shell_load(key, part):
    key_base = jax.random.fold_in(key, 21)
    ramp = 1.0 + 2.0 * jnp.arange(PATCHES, dtype=jnp.float32) / max(PATCHES - 1, 1)
    base = jax.random.normal(key_base, (PATCHES, NY), jnp.float32)
    return base * ramp[:, None]


def draw_patch_len(key, part):
    key_len = jax.random.fold_in(key, 31)
    key_pos = jax.random.fold_in(key, 32)
    lengths = jax.random.randint(key_len, (PATCHES,), NY // 2, NY + 1)
    position = jax.random.randint(key_pos, (), 0, PATCHES)
    return jnp.where(jnp.arange(PATCHES) == position, NY, lengths).astype(jnp.int32)


def place_ends(drawn, key, low, top_value):
    dims = drawn.shape
    index_at = [jax.random.randint(jax.random.fold_in(key, axis), (), 0, dims[axis]) for axis in range(len(dims))]
    drawn = drawn.at[tuple(index_at)].set(low)
    longest = dims.index(max(dims))
    index_at[longest] = (index_at[longest] + 1) % dims[longest]
    return drawn.at[tuple(index_at)].set(top_value)


def shard_levels(own_key, extent, pieces, least, largest):
    def one(axis_at, shards_of):
        steps = jax.random.uniform(jax.random.fold_in(jax.random.fold_in(own_key, 6), axis_at), (shards_of,), jnp.float32, least / len(pieces), largest / len(pieces))
        return jnp.repeat(jnp.exp(steps), extent[axis_at] // shards_of).reshape((-1,) + (1,) * (len(extent) - axis_at - 1))

    level = one(*pieces[0])
    for cut in pieces[1:]:
        level = level * one(*cut)
    return level


def routed_block(key, own, number, rows, amount, top, most, lean):
    sequence = jax.random.permutation(key, amount)
    heavy_load, ordinary = portions_of(amount, rows * top, most, lean, True), portions_of(amount, rows * top, most, lean, False)
    places = jnp.arange(amount)

    def named(sizes, offset_by):
        used = int((sizes > 0).sum())
        fixed = max(1, used // 4)
        moved = fixed + (places - fixed + offset_by * (used - fixed)) % max(1, amount - fixed)
        return jnp.zeros((amount,), jnp.int32).at[sequence[jnp.where(places < fixed, places, moved)]].set(jnp.asarray(sizes, jnp.int32))

    sizes = jnp.where(number % 4 == 0, named(heavy_load, number // 4), named(ordinary, number - number // 4 - 1))
    mixed = jax.random.permutation(jax.random.fold_in(own, 3), amount)
    giver, receiver = mixed[0:amount // 2 * 2:2], mixed[1:amount // 2 * 2:2]
    room = jnp.minimum(sizes[giver] - 1, most - sizes[receiver]) // 2
    room = jnp.where((giver == sequence[0]) | (receiver == sequence[0]) | (sizes[receiver] == 0), 0, jnp.maximum(room, 0))
    moved = jax.random.randint(jax.random.fold_in(own, 4), (amount // 2,), 0, 1 << 20) % (room + 1)
    sizes = sizes.at[giver].add(-moved).at[receiver].add(moved)
    members = jnp.searchsorted(jnp.cumsum(sizes), jnp.arange(rows * top), side="right").astype(jnp.int32)
    listing = members.reshape(top, rows).T
    listing = listing[jax.random.permutation(jax.random.fold_in(own, 1), rows)]
    offset_by = jax.random.randint(jax.random.fold_in(own, 2), (rows, 1), 0, top)
    return jnp.take_along_axis(listing, (jnp.arange(top)[None, :] + offset_by) % top, axis=1)


def portions_of(amount, total, limit, slope, full):
    loads = [(1 << 20) // math.isqrt(rank ** slope) + 1 for rank in range(1, amount + 1)]
    largest = limit if full else min(limit, max(-(-total // amount), total * loads[0] // sum(loads)))
    least = 1 if total - largest >= amount - 1 else 0
    given, surplus = [largest] + [least] * (amount - 1), total - largest - least * (amount - 1)
    while surplus > 0:
        candidates = [i for i in range(1, amount) if given[i] < largest] or [i for i in range(1, amount) if given[i] < limit]
        pool, remaining = sum([loads[i] for i in candidates]), surplus
        for i in candidates:
            more = min(limit - given[i], max(1, remaining * loads[i] // pool), surplus)
            given[i] = given[i] + more
            surplus = surplus - more
    return np.array(given)


def scatter_about(rng, dims, scale, bound, split=(), kind=jnp.bfloat16):
    drawn = scale * jax.random.normal(rng, dims, jnp.float32)
    if split:
        drawn = drawn * shard_levels(rng, dims, split, -0.22, 0.18)
    return jnp.clip(drawn, -bound, bound).astype(kind)


def setup_inputs(seed: int = 0) -> dict:
    splits = jax.random.split(jax.random.key(seed), 10)
    flow_force = scatter_about(splits[0], (N_SIDE, NX, NZF, NY), 1.0, 6.0, ((0, 4), (1, 8)), jnp.float32)
    flow_coef = jnp.clip(jnp.exp(math.log(1.5) - 2.7080502 * jax.random.uniform(splits[1], (N_SIDE, NX, NZF, NY), jnp.float32) ** shard_levels(splits[1], (N_SIDE, NX, NZF, NY), ((0, 4), (1, 8)), -0.2, 0.2)), 0.1, 1.5)
    flow_init = scatter_about(splits[2], (N_SIDE, NX, NZF, NY), 1.0, 6.0, ((0, 4), (1, 8)), jnp.float32)
    compliance = draw_compliance(jax.random.fold_in(splits[9], 71), 0)
    shell_load = draw_shell_load(jax.random.fold_in(splits[9], 71), 0)
    disp_init = scatter_about(splits[5], (PATCHES, NY), 0.5, 3.0, ((0, 8),), jnp.float32)
    patch_len = draw_patch_len(jax.random.fold_in(splits[9], 71), 0)
    owner_keys = jax.random.split(jax.random.fold_in(splits[7], 1), PATCHES // PB)
    owner_turns = jax.random.permutation(jax.random.fold_in(splits[7], 3), PATCHES // PB)
    owner = jax.vmap(lambda own, number: routed_block(jax.random.fold_in(splits[7], 2), own, number, PB, N_SIDE - 1, 1, CAP, 1))(owner_keys, owner_turns).reshape((PATCHES, 1))
    block_row = place_ends(jax.random.randint(splits[8], (PATCHES,), 0, CX), jax.random.fold_in(splits[8], 1), 0, CX - 1).astype(jnp.int32)
    return {"flow_force": flow_force, "flow_coef": flow_coef, "flow_init": flow_init, "compliance": compliance, "shell_load": shell_load, "disp_init": disp_init, "patch_len": patch_len, "owner": owner, "block_row": block_row}


RELAX = 0.5
PENALTY = 3.0
HIGH = lax.Precision.HIGHEST


def neighbours(padded):
    total = padded[:, 2:, 1:-1, 1:-1] + padded[:, :-2, 1:-1, 1:-1]
    total = total + padded[:, 1:-1, 2:, 1:-1] + padded[:, 1:-1, :-2, 1:-1]
    total = total + padded[:, 1:-1, 1:-1, 2:] + padded[:, 1:-1, 1:-1, :-2]
    return total


def fluid_solve(disp, flow_force, flow_coef, flow_init, owner, block_row, live_mask):
    sector_of = owner[:, 0].astype(jnp.int32)
    global_row = ((jnp.arange(PATCHES) // PB) * CX).astype(jnp.int32) + block_row.astype(jnp.int32)
    plane = jnp.zeros((N_SIDE, NX, NY), jnp.float32).at[sector_of, global_row].add(live_mask * disp)
    right_side = flow_force.at[:, :, 0, :].add(plane)
    flow_state = flow_init
    for sweep_index in range(SWEEPS):
        padded = jnp.pad(flow_state, ((0, 0), (1, 1), (1, 1), (1, 1)))
        flow_state = (right_side + neighbours(padded)) / (6.0 + flow_coef)
    traction = PENALTY * flow_state[sector_of, global_row, 0, :]
    return traction, flow_state


def reference(flow_force, flow_coef, flow_init, compliance, shell_load, disp_init, patch_len, owner, block_row):
    live_mask = (jnp.arange(NY)[None, :] < patch_len[:, None]).astype(jnp.float32)

    def evaluate(disp):
        traction, flow_state = fluid_solve(disp, flow_force, flow_coef, flow_init, owner, block_row, live_mask)
        loaded = live_mask * (shell_load - traction)
        tilde = live_mask * jnp.einsum("pij,pj->pi", compliance, loaded, precision=HIGH)
        return tilde, flow_state

    disp_zero = live_mask * disp_init
    tilde_zero, flow_state = evaluate(disp_zero)
    resid_zero = tilde_zero - disp_zero
    disp_one = disp_zero + RELAX * resid_zero
    tilde_one, flow_state = evaluate(disp_one)
    resid_one = tilde_one - disp_one
    diff_one = resid_one - resid_zero
    gram_aa = jnp.sum(diff_one * diff_one)
    gram_ab = jnp.sum(diff_one * resid_one)
    coeff = -gram_ab / (gram_aa + (1e-3 * gram_aa + 1e-6))
    disp_two = tilde_one + coeff * (tilde_one - tilde_zero)
    tilde_two, flow_state = evaluate(disp_two)
    resid_two = tilde_two - disp_two
    newer = resid_two - resid_one
    gram_nn = jnp.sum(newer * newer)
    gram_no = jnp.sum(newer * diff_one)
    gram_oo = jnp.sum(diff_one * diff_one)
    proj_new = jnp.sum(newer * resid_two)
    proj_old = jnp.sum(diff_one * resid_two)
    shift_two = 1e-3 * (gram_nn + gram_oo) + 1e-6
    diag_new = gram_nn + shift_two
    diag_old = gram_oo + shift_two
    determ = diag_new * diag_old - gram_no * gram_no
    coeff_new = (-proj_new * diag_old + proj_old * gram_no) / determ
    coeff_old = (-proj_old * diag_new + proj_new * gram_no) / determ
    disp_three = tilde_two + coeff_new * (tilde_two - tilde_one) + coeff_old * (tilde_one - tilde_zero)
    disp_next = jnp.zeros((N_SIDE, PATCHES, NY), jnp.float32).at[N_SIDE - 1].set(disp_three)
    residual = jnp.zeros((N_SIDE, PATCHES, NY), jnp.float32).at[N_SIDE - 1].set(resid_two)
    flow_final = flow_state.at[N_SIDE - 1].set(0.0)
    return (disp_next, residual, flow_final)
```

```python
import jax
import jax.numpy as jnp
from jax import lax
from jax.sharding import PartitionSpec as P

SWEEPS = 4
RELAX = 0.5
PENALTY = 3.0
HALO = SWEEPS
BAND = 2 * SWEEPS


def shift_y(a):
    zero = jnp.zeros_like(a[..., :1])
    return (jnp.concatenate([a[..., 1:], zero], axis=-1), jnp.concatenate([zero, a[..., :-1]], axis=-1))


def stencil(rhs, coef, xp, xm, zp, zm, centre):
    yp, ym = shift_y(centre)
    total = ((((xp + xm) + zp) + zm) + yp) + ym
    return (rhs + total) / (6.0 + coef)


def band_solve(q, rhs, coef, row_ok):
    rows, planes = q.shape[0], q.shape[1]
    for k in range(1, SWEEPS + 1):
        centre = q[1:-1, :-1]
        zm = jnp.concatenate([jnp.zeros_like(centre[:, :1]), centre[:, :-1]], axis=1)
        new = stencil(
            rhs[k : rows - k, : planes - k],
            coef[k : rows - k, : planes - k],
            q[2:, :-1],
            q[:-2, :-1],
            q[1:-1, 1:],
            zm,
            centre,
        )
        q = jnp.where(row_ok[k : rows - k], new, 0.0)
    return q


def ring_pairs(count):
    forward = [(i, i + 1) for i in range(count - 1)]
    return forward, [(t, s) for s, t in forward]


def rims(block, width):
    count = lax.axis_size("slab")
    forward, backward = ring_pairs(count)
    low = lax.ppermute(block[block.shape[0] - width :], "slab", forward)
    high = lax.ppermute(block[:width], "slab", backward)
    return jnp.concatenate([low, block, high], axis=0)


def full_solve(q, rhs, coef):
    for k in range(SWEEPS):
        qx = rims(q, 1)
        zero = jnp.zeros_like(q[:, :1])
        q = stencil(
            rhs,
            coef,
            qx[2:],
            qx[:-2],
            jnp.concatenate([q[:, 1:], zero], axis=1),
            jnp.concatenate([zero, q[:, :-1]], axis=1),
            q,
        )
    return q


def allsum(v):
    for axis in ("slab", "side"):
        count = lax.axis_size(axis)
        step = 1
        while step < count:
            v = v + lax.ppermute(v, axis, [(i, i ^ step) for i in range(count)])
            step *= 2
    return v


def body(
    flow_force, flow_coef, flow_init, compliance, shell_load, disp_init, patch_len, owner, block_row
):
    force_here = flow_force[0]
    coef_here = flow_coef[0]
    start_here = flow_init[0]
    slab_rows, planes, line_cells = force_here.shape
    assert slab_rows >= HALO and planes >= BAND
    side_count = lax.axis_size("side")
    side_id = lax.axis_index("side")
    slab_id = lax.axis_index("slab")
    shell_flag = side_id == side_count - 1
    live = (jnp.arange(line_cells)[None, :] < patch_len[:, None]).astype(jnp.float32)
    own = (owner[:, 0] == side_id).astype(jnp.float32)[:, None]
    own_live = own * live
    onehot = (block_row[None, :] == jnp.arange(slab_rows)[:, None]).astype(jnp.float32) * own[:, 0][None, :]

    packed = jnp.stack([start_here[:, :BAND], force_here[:, :BAND], coef_here[:, :BAND]])
    packed = jnp.moveaxis(rims(jnp.moveaxis(packed, 1, 0), HALO), 0, 1)
    init_band, force_band, coef_band = packed[0], packed[1], packed[2]
    global_row = slab_id * slab_rows + jnp.arange(slab_rows + 2 * HALO) - HALO
    total_rows = slab_rows * lax.axis_size("slab")
    row_ok = ((global_row >= 0) & (global_row < total_rows))[:, None, None]

    def evaluate(disp):
        plane = jnp.sum(onehot[:, :, None] * (live * disp)[None], axis=1)
        rhs = force_band.at[:, 0, :].add(rims(plane, HALO))
        band = band_solve(init_band, rhs, coef_band, row_ok)
        traction = PENALTY * band[:, 0, :][block_row]
        loaded = live * (shell_load - traction)
        tilde = own_live * jnp.sum(compliance * loaded[:, None, :], axis=-1)
        return tilde, band

    disp_zero = own_live * disp_init
    tilde_zero, unused = evaluate(disp_zero)
    resid_zero = tilde_zero - disp_zero
    disp_one = disp_zero + RELAX * resid_zero
    tilde_one, unused = evaluate(disp_one)
    resid_one = tilde_one - disp_one
    diff_one = resid_one - resid_zero
    sums = allsum(jnp.stack([jnp.sum(diff_one * diff_one), jnp.sum(diff_one * resid_one)]))
    gram_aa, gram_ab = sums[0], sums[1]
    coeff = -gram_ab / (gram_aa + (0.001 * gram_aa + 1e-06))
    disp_two = tilde_one + coeff * (tilde_one - tilde_zero)
    tilde_two, band_two = evaluate(disp_two)
    resid_two = tilde_two - disp_two
    newer = resid_two - resid_one
    sums = allsum(
        jnp.stack(
            [
                jnp.sum(newer * newer),
                jnp.sum(newer * diff_one),
                jnp.sum(newer * resid_two),
                jnp.sum(diff_one * resid_two),
            ]
        )
    )
    gram_nn, gram_no, proj_new, proj_old = sums[0], sums[1], sums[2], sums[3]

    outgoing = jnp.stack([tilde_two, tilde_one, tilde_zero, resid_two])
    gathered = outgoing
    for source in range(side_count - 1):
        gathered = gathered + lax.ppermute(outgoing, "side", [(source, side_count - 1)])
    tilde_two, tilde_one, tilde_zero, resid_two = gathered[0], gathered[1], gathered[2], gathered[3]

    shift_two = 0.001 * (gram_nn + gram_aa) + 1e-06
    diag_new = gram_nn + shift_two
    diag_old = gram_aa + shift_two
    determ = diag_new * diag_old - gram_no * gram_no
    coeff_new = (-proj_new * diag_old + proj_old * gram_no) / determ
    coeff_old = (-proj_old * diag_new + proj_new * gram_no) / determ
    disp_three = (
        tilde_two + coeff_new * (tilde_two - tilde_one) + coeff_old * (tilde_one - tilde_zero)
    )

    deep = full_solve(start_here, force_here, coef_here)
    flow_state = jnp.concatenate([band_two, deep[:, band_two.shape[1] :]], axis=1)
    disp_next = jnp.where(shell_flag, disp_three, 0.0)[None]
    residual = jnp.where(shell_flag, resid_two, 0.0)[None]
    flow_final = jnp.where(shell_flag, 0.0, flow_state)[None]
    return (disp_next, residual, flow_final)


def solution(mesh):
    return jax.shard_map(
        body,
        mesh=mesh,
        in_specs=(
            P("side", "slab", None, None),
            P("side", "slab", None, None),
            P("side", "slab", None, None),
            P("slab", None, None),
            P("slab", None),
            P("slab", None),
            P("slab"),
            P("slab", None),
            P("slab"),
        ),
        out_specs=(P("side", "slab", None), P("side", "slab", None), P("side", "slab", None, None)),
        check_vma=False,
    )
```

```python
import jax
import jax.numpy as jnp
from jax import lax
from jax.sharding import PartitionSpec as P

SWEEPS = 4
RELAX = 0.5
PENALTY = 3.0
HALO = SWEEPS
BAND = 2 * SWEEPS


def shift_y(a):
    zero = jnp.zeros_like(a[..., :1])
    return (jnp.concatenate([a[..., 1:], zero], axis=-1), jnp.concatenate([zero, a[..., :-1]], axis=-1))


def stencil(rhs, coef, xp, xm, zp, zm, centre):
    yp, ym = shift_y(centre)
    total = ((((xp + xm) + zp) + zm) + yp) + ym
    return (rhs + total) / (6.0 + coef)


def band_solve(q, rhs, coef, row_ok):
    rows, planes = q.shape[0], q.shape[1]
    for k in range(1, SWEEPS + 1):
        centre = q[1:-1, :-1]
        zm = jnp.concatenate([jnp.zeros_like(centre[:, :1]), centre[:, :-1]], axis=1)
        new = stencil(
            rhs[k : rows - k, : planes - k],
            coef[k : rows - k, : planes - k],
            q[2:, :-1],
            q[:-2, :-1],
            q[1:-1, 1:],
            zm,
            centre,
        )
        q = jnp.where(row_ok[k : rows - k], new, 0.0)
    return q


def ring_pairs(count):
    forward = [(i, i + 1) for i in range(count - 1)]
    return forward, [(t, s) for s, t in forward]


def rims(block, width):
    count = lax.axis_size("slab")
    forward, backward = ring_pairs(count)
    low = lax.ppermute(block[block.shape[0] - width :], "slab", forward)
    high = lax.ppermute(block[:width], "slab", backward)
    return jnp.concatenate([low, block, high], axis=0)


def full_solve(q, rhs, coef):
    for k in range(SWEEPS):
        qx = rims(q, 1)
        zero = jnp.zeros_like(q[:, :1])
        q = stencil(
            rhs,
            coef,
            qx[2:],
            qx[:-2],
            jnp.concatenate([q[:, 1:], zero], axis=1),
            jnp.concatenate([zero, q[:, :-1]], axis=1),
            q,
        )
    return q


def allsum_axis(v, axis):
    count = lax.axis_size(axis)
    step = 1
    while step < count:
        v = v + lax.ppermute(v, axis, [(i, i ^ step) for i in range(count)])
        step *= 2
    return v


def allsum(v):
    return allsum_axis(allsum_axis(v, "slab"), "side")


def body(
    flow_force, flow_coef, flow_init, compliance, shell_load, disp_init, patch_len, owner, block_row
):
    force_here = flow_force[0]
    coef_here = flow_coef[0]
    start_here = flow_init[0]
    slab_rows, planes, line_cells = force_here.shape
    assert slab_rows >= HALO and planes >= BAND
    side_count = lax.axis_size("side")
    side_id = lax.axis_index("side")
    slab_id = lax.axis_index("slab")
    shell_flag = side_id == side_count - 1
    live = (jnp.arange(line_cells)[None, :] < patch_len[:, None]).astype(jnp.float32)
    own = (owner[:, 0] == side_id).astype(jnp.float32)[:, None]
    own_live = own * live
    onehot = (block_row[None, :] == jnp.arange(slab_rows)[:, None]).astype(jnp.float32) * own[:, 0][None, :]

    packed = rims(
        jnp.concatenate([start_here[:, :BAND], force_here[:, :BAND], coef_here[:, :BAND]], axis=1), HALO
    )
    init_band, force_band, coef_band = (
        packed[:, :BAND],
        packed[:, BAND : 2 * BAND],
        packed[:, 2 * BAND :],
    )
    global_row = slab_id * slab_rows + jnp.arange(slab_rows + 2 * HALO) - HALO
    total_rows = slab_rows * lax.axis_size("slab")
    row_ok = ((global_row >= 0) & (global_row < total_rows))[:, None, None]

    def evaluate(disp):
        plane = jnp.sum(onehot[:, :, None] * (live * disp)[None], axis=1)
        rhs = force_band.at[:, 0, :].add(rims(plane, HALO))
        band = band_solve(init_band, rhs, coef_band, row_ok)
        traction = PENALTY * band[:, 0, :][block_row]
        loaded = live * (shell_load - traction)
        tilde = own_live * jnp.sum(compliance * loaded[:, None, :], axis=-1)
        return tilde, band

    disp_zero = own_live * disp_init
    tilde_zero, unused = evaluate(disp_zero)
    resid_zero = tilde_zero - disp_zero
    disp_one = disp_zero + RELAX * resid_zero
    tilde_one, unused = evaluate(disp_one)
    resid_one = tilde_one - disp_one
    diff_one = resid_one - resid_zero
    sums = allsum(jnp.stack([jnp.sum(diff_one * diff_one), jnp.sum(diff_one * resid_one)]))
    gram_aa, gram_ab = sums[0], sums[1]
    coeff = -gram_ab / (gram_aa + (0.001 * gram_aa + 1e-06))
    disp_two = tilde_one + coeff * (tilde_one - tilde_zero)
    tilde_two, band_two = evaluate(disp_two)
    resid_two = tilde_two - disp_two
    newer = resid_two - resid_one
    partial = jnp.stack(
        [
            jnp.sum(newer * newer),
            jnp.sum(newer * diff_one),
            jnp.sum(newer * resid_two),
            jnp.sum(diff_one * resid_two),
        ]
    )
    patches_here = tilde_two.shape[0]
    outgoing = jnp.concatenate(
        [
            jnp.concatenate([tilde_two, tilde_one, tilde_zero, resid_two], axis=0),
            jnp.concatenate([partial, jnp.zeros((line_cells - 4,), jnp.float32)])[None],
        ],
        axis=0,
    )
    gathered = outgoing
    for source in range(side_count - 1):
        gathered = gathered + lax.ppermute(outgoing, "side", [(source, side_count - 1)])
    sums = allsum_axis(gathered[4 * patches_here, :4], "slab")
    gram_nn, gram_no, proj_new, proj_old = sums[0], sums[1], sums[2], sums[3]
    tilde_two, tilde_one, tilde_zero, resid_two = (
        gathered[k * patches_here : (k + 1) * patches_here] for k in range(4)
    )

    shift_two = 0.001 * (gram_nn + gram_aa) + 1e-06
    diag_new = gram_nn + shift_two
    diag_old = gram_aa + shift_two
    determ = diag_new * diag_old - gram_no * gram_no
    coeff_new = (-proj_new * diag_old + proj_old * gram_no) / determ
    coeff_old = (-proj_old * diag_new + proj_new * gram_no) / determ
    disp_three = (
        tilde_two + coeff_new * (tilde_two - tilde_one) + coeff_old * (tilde_one - tilde_zero)
    )

    deep = full_solve(start_here, force_here, coef_here)
    flow_state = jnp.concatenate([band_two, deep[:, band_two.shape[1] :]], axis=1)
    disp_next = jnp.where(shell_flag, disp_three, 0.0)[None]
    residual = jnp.where(shell_flag, resid_two, 0.0)[None]
    flow_final = jnp.where(shell_flag, 0.0, flow_state)[None]
    return (disp_next, residual, flow_final)


def solution(mesh):
    return jax.shard_map(
        body,
        mesh=mesh,
        in_specs=(
            P("side", "slab", None, None),
            P("side", "slab", None, None),
            P("side", "slab", None, None),
            P("slab", None, None),
            P("slab", None),
            P("slab", None),
            P("slab"),
            P("slab", None),
            P("slab"),
        ),
        out_specs=(P("side", "slab", None), P("side", "slab", None), P("side", "slab", None, None)),
        check_vma=False,
    )
```

```python
import jax
import jax.numpy as jnp
from jax import lax
from jax.sharding import PartitionSpec as P

SWEEPS = 4
RELAX = 0.5
PENALTY = 3.0
HALO = SWEEPS
BAND = 2 * SWEEPS


def shift_y(a):
    zero = jnp.zeros_like(a[..., :1])
    return (jnp.concatenate([a[..., 1:], zero], axis=-1), jnp.concatenate([zero, a[..., :-1]], axis=-1))


def stencil(rhs, coef, xp, xm, zp, zm, centre):
    yp, ym = shift_y(centre)
    total = ((((xp + xm) + zp) + zm) + yp) + ym
    return (rhs + total) / (6.0 + coef)


def band_solve(q, rhs, coef, row_ok):
    rows, planes = q.shape[0], q.shape[1]
    for k in range(1, SWEEPS + 1):
        centre = q[1:-1, :-1]
        zm = jnp.concatenate([jnp.zeros_like(centre[:, :1]), centre[:, :-1]], axis=1)
        new = stencil(
            rhs[k : rows - k, : planes - k],
            coef[k : rows - k, : planes - k],
            q[2:, :-1],
            q[:-2, :-1],
            q[1:-1, 1:],
            zm,
            centre,
        )
        q = jnp.where(row_ok[k : rows - k], new, 0.0)
    return q


def ring_pairs(count):
    forward = [(i, i + 1) for i in range(count - 1)]
    return forward, [(t, s) for s, t in forward]


def rims(block, width):
    count = lax.axis_size("slab")
    forward, backward = ring_pairs(count)
    low = lax.ppermute(block[block.shape[0] - width :], "slab", forward)
    high = lax.ppermute(block[:width], "slab", backward)
    return jnp.concatenate([low, block, high], axis=0)


def full_sweep(q, rhs, coef):
    qx = rims(q, 1)
    zero = jnp.zeros_like(q[:, :1])
    return stencil(
        rhs,
        coef,
        qx[2:],
        qx[:-2],
        jnp.concatenate([q[:, 1:], zero], axis=1),
        jnp.concatenate([zero, q[:, :-1]], axis=1),
        q,
    )


def allsum_axis(v, axis):
    count = lax.axis_size(axis)
    step = 1
    while step < count:
        v = v + lax.ppermute(v, axis, [(i, i ^ step) for i in range(count)])
        step *= 2
    return v


def allsum(v):
    return allsum_axis(allsum_axis(v, "slab"), "side")


def body(
    flow_force, flow_coef, flow_init, compliance, shell_load, disp_init, patch_len, owner, block_row
):
    force_here = flow_force[0]
    coef_here = flow_coef[0]
    start_here = flow_init[0]
    slab_rows, planes, line_cells = force_here.shape
    assert slab_rows >= HALO and planes >= BAND
    side_count = lax.axis_size("side")
    side_id = lax.axis_index("side")
    slab_id = lax.axis_index("slab")
    shell_flag = side_id == side_count - 1
    live = (jnp.arange(line_cells)[None, :] < patch_len[:, None]).astype(jnp.float32)
    own = (owner[:, 0] == side_id).astype(jnp.float32)[:, None]
    own_live = own * live
    onehot = (block_row[None, :] == jnp.arange(slab_rows)[:, None]).astype(jnp.float32) * own[:, 0][None, :]
    pick = (block_row[:, None] == jnp.arange(slab_rows)[None, :]).astype(jnp.float32)

    packed = rims(
        jnp.concatenate([start_here[:, :BAND], force_here[:, :BAND], coef_here[:, :BAND]], axis=1), HALO
    )
    init_band, force_band, coef_band = (
        packed[:, :BAND],
        packed[:, BAND : 2 * BAND],
        packed[:, 2 * BAND :],
    )
    global_row = slab_id * slab_rows + jnp.arange(slab_rows + 2 * HALO) - HALO
    total_rows = slab_rows * lax.axis_size("slab")
    row_ok = ((global_row >= 0) & (global_row < total_rows))[:, None, None]

    def evaluate(disp):
        plane = jnp.sum(onehot[:, :, None] * (live * disp)[None], axis=1)
        rhs = force_band.at[:, 0, :].add(rims(plane, HALO))
        band = band_solve(init_band, rhs, coef_band, row_ok)
        traction = PENALTY * jnp.sum(pick[:, :, None] * band[:, 0, :][None], axis=1)
        loaded = live * (shell_load - traction)
        tilde = own_live * jnp.sum(compliance * loaded[:, None, :], axis=-1)
        return tilde, band

    disp_zero = own_live * disp_init
    tilde_zero, unused = evaluate(disp_zero)
    resid_zero = tilde_zero - disp_zero
    disp_one = disp_zero + RELAX * resid_zero
    deep = start_here
    for k in range(SWEEPS // 2):
        deep = full_sweep(deep, force_here, coef_here)
    disp_one, deep = lax.optimization_barrier((disp_one, deep))
    tilde_one, unused = evaluate(disp_one)
    resid_one = tilde_one - disp_one
    diff_one = resid_one - resid_zero
    sums = allsum(jnp.stack([jnp.sum(diff_one * diff_one), jnp.sum(diff_one * resid_one)]))
    gram_aa, gram_ab = sums[0], sums[1]
    coeff = -gram_ab / (gram_aa + (0.001 * gram_aa + 1e-06))
    for k in range(SWEEPS // 2, SWEEPS):
        deep = full_sweep(deep, force_here, coef_here)
    coeff, deep = lax.optimization_barrier((coeff, deep))
    disp_two = tilde_one + coeff * (tilde_one - tilde_zero)
    tilde_two, band_two = evaluate(disp_two)
    resid_two = tilde_two - disp_two
    newer = resid_two - resid_one
    partial = jnp.stack(
        [
            jnp.sum(newer * newer),
            jnp.sum(newer * diff_one),
            jnp.sum(newer * resid_two),
            jnp.sum(diff_one * resid_two),
        ]
    )
    patches_here = tilde_two.shape[0]
    outgoing = jnp.concatenate(
        [
            jnp.concatenate([tilde_two, tilde_one, tilde_zero, resid_two], axis=0),
            sum(
                jnp.where(jnp.arange(line_cells) == k, partial[k], 0.0) for k in range(4)
            )[None],
        ],
        axis=0,
    )
    gathered = outgoing
    for source in range(side_count - 1):
        gathered = gathered + lax.ppermute(outgoing, "side", [(source, side_count - 1)])
    sums = allsum_axis(gathered[4 * patches_here, :4], "slab")
    gram_nn, gram_no, proj_new, proj_old = sums[0], sums[1], sums[2], sums[3]
    tilde_two, tilde_one, tilde_zero, resid_two = (
        gathered[k * patches_here : (k + 1) * patches_here] for k in range(4)
    )

    shift_two = 0.001 * (gram_nn + gram_aa) + 1e-06
    diag_new = gram_nn + shift_two
    diag_old = gram_aa + shift_two
    determ = diag_new * diag_old - gram_no * gram_no
    coeff_new = (-proj_new * diag_old + proj_old * gram_no) / determ
    coeff_old = (-proj_old * diag_new + proj_new * gram_no) / determ
    disp_three = (
        tilde_two + coeff_new * (tilde_two - tilde_one) + coeff_old * (tilde_one - tilde_zero)
    )

    flow_state = jnp.concatenate([band_two, deep[:, band_two.shape[1] :]], axis=1)
    disp_next = jnp.where(shell_flag, disp_three, 0.0)[None]
    residual = jnp.where(shell_flag, resid_two, 0.0)[None]
    flow_final = jnp.where(shell_flag, 0.0, flow_state)[None]
    return (disp_next, residual, flow_final)


def solution(mesh):
    return jax.shard_map(
        body,
        mesh=mesh,
        in_specs=(
            P("side", "slab", None, None),
            P("side", "slab", None, None),
            P("side", "slab", None, None),
            P("slab", None, None),
            P("slab", None),
            P("slab", None),
            P("slab"),
            P("slab", None),
            P("slab"),
        ),
        out_specs=(P("side", "slab", None), P("side", "slab", None), P("side", "slab", None, None)),
        check_vma=False,
    )
```

```python
import jax
import jax.numpy as jnp
from jax import lax
from jax.sharding import PartitionSpec as P

SWEEPS = 4
RELAX = 0.5
PENALTY = 3.0
HALO = SWEEPS
BAND = 2 * SWEEPS


def shift_y(a):
    zero = jnp.zeros_like(a[..., :1])
    return (jnp.concatenate([a[..., 1:], zero], axis=-1), jnp.concatenate([zero, a[..., :-1]], axis=-1))


def stencil(rhs, coef, xp, xm, zp, zm, centre):
    yp, ym = shift_y(centre)
    total = ((((xp + xm) + zp) + zm) + yp) + ym
    return (rhs + total) / (6.0 + coef)


def band_solve(q, rhs, coef, row_ok):
    rows, planes = q.shape[0], q.shape[1]
    for k in range(1, SWEEPS + 1):
        centre = q[1:-1, :-1]
        zm = jnp.concatenate([jnp.zeros_like(centre[:, :1]), centre[:, :-1]], axis=1)
        new = stencil(
            rhs[k : rows - k, : planes - k],
            coef[k : rows - k, : planes - k],
            q[2:, :-1],
            q[:-2, :-1],
            q[1:-1, 1:],
            zm,
            centre,
        )
        q = jnp.where(row_ok[k : rows - k], new, 0.0)
    return q


def ring_pairs(count):
    forward = [(i, i + 1) for i in range(count - 1)]
    return forward, [(t, s) for s, t in forward]


def rims(block, width):
    count = lax.axis_size("slab")
    forward, backward = ring_pairs(count)
    low = lax.ppermute(block[block.shape[0] - width :], "slab", forward)
    high = lax.ppermute(block[:width], "slab", backward)
    return jnp.concatenate([low, block, high], axis=0)


def deep_solve(q, rhs, coef, row_ok):
    rows = q.shape[0]
    for k in range(1, SWEEPS + 1):
        centre = q[1:-1]
        zero = jnp.zeros_like(centre[:, :1])
        new = stencil(
            rhs[k : rows - k],
            coef[k : rows - k],
            q[2:],
            q[:-2],
            jnp.concatenate([centre[:, 1:], zero], axis=1),
            jnp.concatenate([zero, centre[:, :-1]], axis=1),
            centre,
        )
        q = jnp.where(row_ok[k : rows - k], new, 0.0)
    return q


def allsum_axis(v, axis):
    count = lax.axis_size(axis)
    step = 1
    while step < count:
        v = v + lax.ppermute(v, axis, [(i, i ^ step) for i in range(count)])
        step *= 2
    return v


def allsum(v):
    return allsum_axis(allsum_axis(v, "slab"), "side")


def body(
    flow_force, flow_coef, flow_init, compliance, shell_load, disp_init, patch_len, owner, block_row
):
    force_here = flow_force[0]
    coef_here = flow_coef[0]
    start_here = flow_init[0]
    slab_rows, planes, line_cells = force_here.shape
    assert slab_rows >= HALO and planes >= BAND
    side_count = lax.axis_size("side")
    side_id = lax.axis_index("side")
    slab_id = lax.axis_index("slab")
    shell_flag = side_id == side_count - 1
    live = (jnp.arange(line_cells)[None, :] < patch_len[:, None]).astype(jnp.float32)
    own = (owner[:, 0] == side_id).astype(jnp.float32)[:, None]
    own_live = own * live
    onehot = (block_row[None, :] == jnp.arange(slab_rows)[:, None]).astype(jnp.float32) * own[:, 0][None, :]
    pick = (block_row[:, None] == jnp.arange(slab_rows)[None, :]).astype(jnp.float32)

    packed = rims(
        jnp.concatenate([start_here[:, :BAND], force_here[:, :BAND], coef_here[:, :BAND]], axis=1), HALO
    )
    init_band, force_band, coef_band = (
        packed[:, :BAND],
        packed[:, BAND : 2 * BAND],
        packed[:, 2 * BAND :],
    )
    global_row = slab_id * slab_rows + jnp.arange(slab_rows + 2 * HALO) - HALO
    total_rows = slab_rows * lax.axis_size("slab")
    row_ok = ((global_row >= 0) & (global_row < total_rows))[:, None, None]

    def evaluate(disp):
        plane = jnp.sum(onehot[:, :, None] * (live * disp)[None], axis=1)
        rhs = force_band.at[:, 0, :].add(rims(plane, HALO))
        band = band_solve(init_band, rhs, coef_band, row_ok)
        traction = PENALTY * jnp.sum(pick[:, :, None] * band[:, 0, :][None], axis=1)
        loaded = live * (shell_load - traction)
        tilde = own_live * jnp.sum(compliance * loaded[:, None, :], axis=-1)
        return tilde, band

    disp_zero = own_live * disp_init
    tilde_zero, unused = evaluate(disp_zero)
    resid_zero = tilde_zero - disp_zero
    disp_one = disp_zero + RELAX * resid_zero
    tilde_one, unused = evaluate(disp_one)
    resid_one = tilde_one - disp_one
    diff_one = resid_one - resid_zero
    sums = allsum(jnp.stack([jnp.sum(diff_one * diff_one), jnp.sum(diff_one * resid_one)]))
    gram_aa, gram_ab = sums[0], sums[1]
    coeff = -gram_ab / (gram_aa + (0.001 * gram_aa + 1e-06))
    deep_rims = rims(
        jnp.concatenate([start_here[:, BAND:], force_here[:, BAND:], coef_here[:, BAND:]], axis=1), HALO
    )
    rest = planes - BAND
    deep = deep_solve(
        jnp.concatenate([init_band, deep_rims[:, :rest]], axis=1),
        jnp.concatenate([force_band, deep_rims[:, rest : 2 * rest]], axis=1),
        jnp.concatenate([coef_band, deep_rims[:, 2 * rest :]], axis=1),
        row_ok,
    )
    coeff, deep = lax.optimization_barrier((coeff, deep))
    disp_two = tilde_one + coeff * (tilde_one - tilde_zero)
    tilde_two, band_two = evaluate(disp_two)
    resid_two = tilde_two - disp_two
    newer = resid_two - resid_one
    partial = jnp.stack(
        [
            jnp.sum(newer * newer),
            jnp.sum(newer * diff_one),
            jnp.sum(newer * resid_two),
            jnp.sum(diff_one * resid_two),
        ]
    )
    patches_here = tilde_two.shape[0]
    outgoing = jnp.concatenate(
        [
            jnp.concatenate([tilde_two, tilde_one, tilde_zero, resid_two], axis=0),
            sum(
                jnp.where(jnp.arange(line_cells) == k, partial[k], 0.0) for k in range(4)
            )[None],
        ],
        axis=0,
    )
    gathered = outgoing
    for source in range(side_count - 1):
        gathered = gathered + lax.ppermute(outgoing, "side", [(source, side_count - 1)])
    sums = allsum_axis(gathered[4 * patches_here, :4], "slab")
    gram_nn, gram_no, proj_new, proj_old = sums[0], sums[1], sums[2], sums[3]
    tilde_two, tilde_one, tilde_zero, resid_two = (
        gathered[k * patches_here : (k + 1) * patches_here] for k in range(4)
    )

    shift_two = 0.001 * (gram_nn + gram_aa) + 1e-06
    diag_new = gram_nn + shift_two
    diag_old = gram_aa + shift_two
    determ = diag_new * diag_old - gram_no * gram_no
    coeff_new = (-proj_new * diag_old + proj_old * gram_no) / determ
    coeff_old = (-proj_old * diag_new + proj_new * gram_no) / determ
    disp_three = (
        tilde_two + coeff_new * (tilde_two - tilde_one) + coeff_old * (tilde_one - tilde_zero)
    )

    flow_state = jnp.concatenate([band_two, deep[:, band_two.shape[1] :]], axis=1)
    disp_next = jnp.where(shell_flag, disp_three, 0.0)[None]
    residual = jnp.where(shell_flag, resid_two, 0.0)[None]
    flow_final = jnp.where(shell_flag, 0.0, flow_state)[None]
    return (disp_next, residual, flow_final)


def solution(mesh):
    return jax.shard_map(
        body,
        mesh=mesh,
        in_specs=(
            P("side", "slab", None, None),
            P("side", "slab", None, None),
            P("side", "slab", None, None),
            P("slab", None, None),
            P("slab", None),
            P("slab", None),
            P("slab"),
            P("slab", None),
            P("slab"),
        ),
        out_specs=(P("side", "slab", None), P("side", "slab", None), P("side", "slab", None, None)),
        check_vma=False,
    )
```

```python
import jax
import jax.numpy as jnp
from jax import lax
from jax.sharding import PartitionSpec as P

SWEEPS = 4
RELAX = 0.5
PENALTY = 3.0
HALO = SWEEPS
BAND = 2 * SWEEPS


def shift_y(a):
    zero = jnp.zeros_like(a[..., :1])
    return (jnp.concatenate([a[..., 1:], zero], axis=-1), jnp.concatenate([zero, a[..., :-1]], axis=-1))


def stencil(rhs, coef, xp, xm, zp, zm, centre):
    yp, ym = shift_y(centre)
    total = ((((xp + xm) + zp) + zm) + yp) + ym
    return (rhs + total) / (6.0 + coef)


def band_solve(q, rhs, coef, row_ok):
    rows, planes = q.shape[0], q.shape[1]
    for k in range(1, SWEEPS + 1):
        centre = q[1:-1, :-1]
        zm = jnp.concatenate([jnp.zeros_like(centre[:, :1]), centre[:, :-1]], axis=1)
        new = stencil(
            rhs[k : rows - k, : planes - k],
            coef[k : rows - k, : planes - k],
            q[2:, :-1],
            q[:-2, :-1],
            q[1:-1, 1:],
            zm,
            centre,
        )
        q = jnp.where(row_ok[k : rows - k], new, 0.0)
    return q


def ring_pairs(count):
    forward = [(i, i + 1) for i in range(count - 1)]
    return forward, [(t, s) for s, t in forward]


def rims(block, width):
    count = lax.axis_size("slab")
    forward, backward = ring_pairs(count)
    low = lax.ppermute(block[block.shape[0] - width :], "slab", forward)
    high = lax.ppermute(block[:width], "slab", backward)
    return jnp.concatenate([low, block, high], axis=0)


def deep_solve(q, rhs, coef, row_ok):
    rows = q.shape[0]
    for k in range(1, SWEEPS + 1):
        centre = q[1:-1]
        zero = jnp.zeros_like(centre[:, :1])
        new = stencil(
            rhs[k : rows - k],
            coef[k : rows - k],
            q[2:],
            q[:-2],
            jnp.concatenate([centre[:, 1:], zero], axis=1),
            jnp.concatenate([zero, centre[:, :-1]], axis=1),
            centre,
        )
        q = jnp.where(row_ok[k : rows - k], new, 0.0)
    return q


def allsum_axis(v, axis):
    count = lax.axis_size(axis)
    step = 1
    while step < count:
        v = v + lax.ppermute(v, axis, [(i, i ^ step) for i in range(count)])
        step *= 2
    return v


def allsum(v):
    return allsum_axis(allsum_axis(v, "slab"), "side")


def body(
    flow_force, flow_coef, flow_init, compliance, shell_load, disp_init, patch_len, owner, block_row
):
    force_here = flow_force[0]
    coef_here = flow_coef[0]
    start_here = flow_init[0]
    slab_rows, planes, line_cells = force_here.shape
    assert slab_rows >= HALO and planes >= BAND
    side_count = lax.axis_size("side")
    side_id = lax.axis_index("side")
    slab_id = lax.axis_index("slab")
    shell_flag = side_id == side_count - 1
    live = (jnp.arange(line_cells)[None, :] < patch_len[:, None]).astype(jnp.float32)
    own = (owner[:, 0] == side_id).astype(jnp.float32)[:, None]
    own_live = own * live
    onehot = (block_row[None, :] == jnp.arange(slab_rows)[:, None]).astype(jnp.float32) * own[:, 0][None, :]
    pick = (block_row[:, None] == jnp.arange(slab_rows)[None, :]).astype(jnp.float32)

    packed = rims(
        jnp.concatenate([start_here[:, :BAND], force_here[:, :BAND], coef_here[:, :BAND]], axis=1), HALO
    )
    init_band, force_band, coef_band = (
        packed[:, :BAND],
        packed[:, BAND : 2 * BAND],
        packed[:, 2 * BAND :],
    )
    global_row = slab_id * slab_rows + jnp.arange(slab_rows + 2 * HALO) - HALO
    total_rows = slab_rows * lax.axis_size("slab")
    row_ok = ((global_row >= 0) & (global_row < total_rows))[:, None, None]

    def evaluate(disp):
        plane = jnp.sum(onehot[:, :, None] * (live * disp)[None], axis=1)
        rhs = force_band.at[:, 0, :].add(rims(plane, HALO))
        band = band_solve(init_band, rhs, coef_band, row_ok)
        traction = PENALTY * jnp.sum(pick[:, :, None] * band[:, 0, :][None], axis=1)
        loaded = live * (shell_load - traction)
        tilde = own_live * jnp.sum(compliance * loaded[:, None, :], axis=-1)
        return tilde, band

    disp_zero = own_live * disp_init
    tilde_zero, unused = evaluate(disp_zero)
    resid_zero = tilde_zero - disp_zero
    disp_one = disp_zero + RELAX * resid_zero
    tilde_one, unused = evaluate(disp_one)
    resid_one = tilde_one - disp_one
    diff_one = resid_one - resid_zero
    sums = allsum(jnp.stack([jnp.sum(diff_one * diff_one), jnp.sum(diff_one * resid_one)]))
    gram_aa, gram_ab = sums[0], sums[1]
    coeff = -gram_ab / (gram_aa + (0.001 * gram_aa + 1e-06))
    deep_rims = rims(
        jnp.concatenate([start_here[:, BAND:], force_here[:, BAND:], coef_here[:, BAND:]], axis=1), HALO
    )
    rest = planes - BAND
    deep_rims, tilde_one = lax.optimization_barrier((deep_rims, tilde_one))
    deep = deep_solve(
        jnp.concatenate([init_band, deep_rims[:, :rest]], axis=1),
        jnp.concatenate([force_band, deep_rims[:, rest : 2 * rest]], axis=1),
        jnp.concatenate([coef_band, deep_rims[:, 2 * rest :]], axis=1),
        row_ok,
    )
    coeff, deep = lax.optimization_barrier((coeff, deep))
    disp_two = tilde_one + coeff * (tilde_one - tilde_zero)
    tilde_two, band_two = evaluate(disp_two)
    resid_two = tilde_two - disp_two
    newer = resid_two - resid_one
    partial = jnp.stack(
        [
            jnp.sum(newer * newer),
            jnp.sum(newer * diff_one),
            jnp.sum(newer * resid_two),
            jnp.sum(diff_one * resid_two),
        ]
    )
    patches_here = tilde_two.shape[0]
    outgoing = jnp.concatenate(
        [
            jnp.concatenate([tilde_two, tilde_one, tilde_zero, resid_two], axis=0),
            sum(
                jnp.where(jnp.arange(line_cells) == k, partial[k], 0.0) for k in range(4)
            )[None],
        ],
        axis=0,
    )
    gathered = outgoing
    for source in range(side_count - 1):
        gathered = gathered + lax.ppermute(outgoing, "side", [(source, side_count - 1)])
    sums = allsum_axis(gathered[4 * patches_here, :4], "slab")
    gram_nn, gram_no, proj_new, proj_old = sums[0], sums[1], sums[2], sums[3]
    tilde_two, tilde_one, tilde_zero, resid_two = (
        gathered[k * patches_here : (k + 1) * patches_here] for k in range(4)
    )

    shift_two = 0.001 * (gram_nn + gram_aa) + 1e-06
    diag_new = gram_nn + shift_two
    diag_old = gram_aa + shift_two
    determ = diag_new * diag_old - gram_no * gram_no
    coeff_new = (-proj_new * diag_old + proj_old * gram_no) / determ
    coeff_old = (-proj_old * diag_new + proj_new * gram_no) / determ
    disp_three = (
        tilde_two + coeff_new * (tilde_two - tilde_one) + coeff_old * (tilde_one - tilde_zero)
    )

    flow_state = jnp.concatenate([band_two, deep[:, band_two.shape[1] :]], axis=1)
    disp_next = jnp.where(shell_flag, disp_three, 0.0)[None]
    residual = jnp.where(shell_flag, resid_two, 0.0)[None]
    flow_final = jnp.where(shell_flag, 0.0, flow_state)[None]
    return (disp_next, residual, flow_final)


def solution(mesh):
    return jax.shard_map(
        body,
        mesh=mesh,
        in_specs=(
            P("side", "slab", None, None),
            P("side", "slab", None, None),
            P("side", "slab", None, None),
            P("slab", None, None),
            P("slab", None),
            P("slab", None),
            P("slab"),
            P("slab", None),
            P("slab"),
        ),
        out_specs=(P("side", "slab", None), P("side", "slab", None), P("side", "slab", None, None)),
        check_vma=False,
    )
```

```python
import jax
import jax.numpy as jnp
from jax import lax
from jax.sharding import PartitionSpec as P

SWEEPS = 4
RELAX = 0.5
PENALTY = 3.0
HALO = SWEEPS
BAND = 2 * SWEEPS


def shift_y(a):
    zero = jnp.zeros_like(a[..., :1])
    return (jnp.concatenate([a[..., 1:], zero], axis=-1), jnp.concatenate([zero, a[..., :-1]], axis=-1))


def stencil(rhs, coef, xp, xm, zp, zm, centre):
    yp, ym = shift_y(centre)
    total = ((((xp + xm) + zp) + zm) + yp) + ym
    return (rhs + total) / (6.0 + coef)


def band_solve(q, rhs, coef, row_ok):
    rows, planes = q.shape[0], q.shape[1]
    for k in range(1, SWEEPS + 1):
        centre = q[1:-1, :-1]
        zm = jnp.concatenate([jnp.zeros_like(centre[:, :1]), centre[:, :-1]], axis=1)
        new = stencil(
            rhs[k : rows - k, : planes - k],
            coef[k : rows - k, : planes - k],
            q[2:, :-1],
            q[:-2, :-1],
            q[1:-1, 1:],
            zm,
            centre,
        )
        q = jnp.where(row_ok[k : rows - k], new, 0.0)
    return q


def ring_pairs(count):
    forward = [(i, i + 1) for i in range(count - 1)]
    return forward, [(t, s) for s, t in forward]


def rims(block, width):
    count = lax.axis_size("slab")
    forward, backward = ring_pairs(count)
    low = lax.ppermute(block[block.shape[0] - width :], "slab", forward)
    high = lax.ppermute(block[:width], "slab", backward)
    return jnp.concatenate([low, block, high], axis=0)


def exchange(items):
    count = lax.axis_size("slab")
    forward, backward = ring_pairs(count)
    cells = items[0][0].shape[-1]
    sizes = [width * (a.size // a.shape[0]) // cells for a, width in items]
    up = jnp.concatenate([a[a.shape[0] - w :].reshape(-1, cells) for a, w in items], axis=0)
    down = jnp.concatenate([a[:w].reshape(-1, cells) for a, w in items], axis=0)
    low = lax.ppermute(up, "slab", forward)
    high = lax.ppermute(down, "slab", backward)
    out, at = [], 0
    for (a, w), n in zip(items, sizes):
        shape = (w,) + a.shape[1:]
        out.append(
            jnp.concatenate([low[at : at + n].reshape(shape), a, high[at : at + n].reshape(shape)], axis=0)
        )
        at += n
    return out


def deep_step(q, rhs, coef, ok):
    centre = q[1:-1]
    zero = jnp.zeros_like(centre[:, :1])
    new = stencil(
        rhs,
        coef,
        q[2:],
        q[:-2],
        jnp.concatenate([centre[:, 1:], zero], axis=1),
        jnp.concatenate([zero, centre[:, :-1]], axis=1),
        centre,
    )
    return jnp.where(ok, new, 0.0)


def deep_solve(q, rhs, coef, row_ok):
    rows = q.shape[0]
    for k in range(1, SWEEPS + 1):
        centre = q[1:-1]
        zero = jnp.zeros_like(centre[:, :1])
        new = stencil(
            rhs[k : rows - k],
            coef[k : rows - k],
            q[2:],
            q[:-2],
            jnp.concatenate([centre[:, 1:], zero], axis=1),
            jnp.concatenate([zero, centre[:, :-1]], axis=1),
            centre,
        )
        q = jnp.where(row_ok[k : rows - k], new, 0.0)
    return q


def allsum_axis(v, axis):
    count = lax.axis_size(axis)
    step = 1
    while step < count:
        v = v + lax.ppermute(v, axis, [(i, i ^ step) for i in range(count)])
        step *= 2
    return v


def allsum(v):
    return allsum_axis(allsum_axis(v, "slab"), "side")


def body(
    flow_force, flow_coef, flow_init, compliance, shell_load, disp_init, patch_len, owner, block_row
):
    force_here = flow_force[0]
    coef_here = flow_coef[0]
    start_here = flow_init[0]
    slab_rows, planes, line_cells = force_here.shape
    assert slab_rows >= HALO and planes >= BAND
    side_count = lax.axis_size("side")
    side_id = lax.axis_index("side")
    slab_id = lax.axis_index("slab")
    shell_flag = side_id == side_count - 1
    live = (jnp.arange(line_cells)[None, :] < patch_len[:, None]).astype(jnp.float32)
    own = (owner[:, 0] == side_id).astype(jnp.float32)[:, None]
    own_live = own * live
    onehot = (block_row[None, :] == jnp.arange(slab_rows)[:, None]).astype(jnp.float32) * own[:, 0][None, :]
    pick = (block_row[:, None] == jnp.arange(slab_rows)[None, :]).astype(jnp.float32)

    deep_planes = planes - BAND
    disp_zero = own_live * disp_init
    plane_zero = jnp.sum(onehot[:, :, None] * (live * disp_zero)[None], axis=1)
    packed, plane_zero_rims, init_deep, fc_deep = exchange(
        [
            (jnp.concatenate([start_here[:, :BAND], force_here[:, :BAND], coef_here[:, :BAND]], axis=1), HALO),
            (plane_zero, HALO),
            (start_here[:, BAND:], 2),
            (jnp.concatenate([force_here[:, BAND:], coef_here[:, BAND:]], axis=1), 1),
        ]
    )
    init_band, force_band, coef_band = (
        packed[:, :BAND],
        packed[:, BAND : 2 * BAND],
        packed[:, 2 * BAND :],
    )
    init_deep = jnp.concatenate([init_band[HALO - 2 : HALO + slab_rows + 2], init_deep], axis=1)
    force_deep = jnp.concatenate(
        [force_band[HALO - 1 : HALO + slab_rows + 1], fc_deep[:, :deep_planes]], axis=1
    )
    coef_deep = jnp.concatenate([coef_band[HALO - 1 : HALO + slab_rows + 1], fc_deep[:, deep_planes:]], axis=1)
    global_row = slab_id * slab_rows + jnp.arange(slab_rows + 2 * HALO) - HALO
    total_rows = slab_rows * lax.axis_size("slab")
    row_ok = ((global_row >= 0) & (global_row < total_rows))[:, None, None]

    ok_one = row_ok[HALO - 1 : HALO + slab_rows + 1]
    ok_two = row_ok[HALO : HALO + slab_rows]

    def evaluate(disp, plane_rims=None, extra=()):
        if plane_rims is None:
            plane = jnp.sum(onehot[:, :, None] * (live * disp)[None], axis=1)
            got = exchange([(plane, HALO)] + list(extra))
            plane_rims, extra = got[0], got[1:]
        rhs = force_band.at[:, 0, :].add(plane_rims)
        band = band_solve(init_band, rhs, coef_band, row_ok)
        traction = PENALTY * jnp.sum(pick[:, :, None] * band[:, 0, :][None], axis=1)
        loaded = live * (shell_load - traction)
        tilde = own_live * jnp.sum(compliance * loaded[:, None, :], axis=-1)
        return tilde, band, extra

    tilde_zero, unused, unused_extra = evaluate(disp_zero, plane_zero_rims)
    resid_zero = tilde_zero - disp_zero
    disp_one = disp_zero + RELAX * resid_zero
    tilde_one, unused, unused_extra = evaluate(disp_one)
    init_deep, tilde_one = lax.optimization_barrier((init_deep, tilde_one))
    deep = deep_step(init_deep, force_deep, coef_deep, ok_one)
    deep = deep_step(deep, force_deep[1:-1], coef_deep[1:-1], ok_two)
    resid_one = tilde_one - disp_one
    diff_one = resid_one - resid_zero
    sums = allsum(jnp.stack([jnp.sum(diff_one * diff_one), jnp.sum(diff_one * resid_one)]))
    gram_aa, gram_ab = sums[0], sums[1]
    coeff = -gram_ab / (gram_aa + (0.001 * gram_aa + 1e-06))
    disp_two = tilde_one + coeff * (tilde_one - tilde_zero)
    tilde_two, band_two, (deep,) = evaluate(disp_two, extra=[(deep, 2)])
    deep = deep_step(deep, force_deep, coef_deep, ok_one)
    deep = deep_step(deep, force_deep[1:-1], coef_deep[1:-1], ok_two)
    resid_two = tilde_two - disp_two
    newer = resid_two - resid_one
    partial = jnp.stack(
        [
            jnp.sum(newer * newer),
            jnp.sum(newer * diff_one),
            jnp.sum(newer * resid_two),
            jnp.sum(diff_one * resid_two),
        ]
    )
    patches_here = tilde_two.shape[0]
    outgoing = jnp.concatenate(
        [
            jnp.concatenate([tilde_two, tilde_one, tilde_zero, resid_two], axis=0),
            sum(
                jnp.where(jnp.arange(line_cells) == k, partial[k], 0.0) for k in range(4)
            )[None],
        ],
        axis=0,
    )
    gathered = outgoing
    for source in range(side_count - 1):
        gathered = gathered + lax.ppermute(outgoing, "side", [(source, side_count - 1)])
    sums = allsum_axis(gathered[4 * patches_here, :4], "slab")
    gram_nn, gram_no, proj_new, proj_old = sums[0], sums[1], sums[2], sums[3]
    tilde_two, tilde_one, tilde_zero, resid_two = (
        gathered[k * patches_here : (k + 1) * patches_here] for k in range(4)
    )

    shift_two = 0.001 * (gram_nn + gram_aa) + 1e-06
    diag_new = gram_nn + shift_two
    diag_old = gram_aa + shift_two
    determ = diag_new * diag_old - gram_no * gram_no
    coeff_new = (-proj_new * diag_old + proj_old * gram_no) / determ
    coeff_old = (-proj_old * diag_new + proj_new * gram_no) / determ
    disp_three = (
        tilde_two + coeff_new * (tilde_two - tilde_one) + coeff_old * (tilde_one - tilde_zero)
    )

    flow_state = jnp.concatenate([band_two, deep[:, band_two.shape[1] :]], axis=1)
    disp_next = jnp.where(shell_flag, disp_three, 0.0)[None]
    residual = jnp.where(shell_flag, resid_two, 0.0)[None]
    flow_final = jnp.where(shell_flag, 0.0, flow_state)[None]
    return (disp_next, residual, flow_final)


def solution(mesh):
    return jax.shard_map(
        body,
        mesh=mesh,
        in_specs=(
            P("side", "slab", None, None),
            P("side", "slab", None, None),
            P("side", "slab", None, None),
            P("slab", None, None),
            P("slab", None),
            P("slab", None),
            P("slab"),
            P("slab", None),
            P("slab"),
        ),
        out_specs=(P("side", "slab", None), P("side", "slab", None), P("side", "slab", None, None)),
        check_vma=False,
    )
```

```python
import jax
import jax.numpy as jnp
from jax import lax
from jax.sharding import PartitionSpec as P

SWEEPS = 4
RELAX = 0.5
PENALTY = 3.0
HALO = SWEEPS
BAND = 2 * SWEEPS


def shift_y(a):
    zero = jnp.zeros_like(a[..., :1])
    return (jnp.concatenate([a[..., 1:], zero], axis=-1), jnp.concatenate([zero, a[..., :-1]], axis=-1))


def stencil(rhs, coef, xp, xm, zp, zm, centre):
    yp, ym = shift_y(centre)
    total = ((((xp + xm) + zp) + zm) + yp) + ym
    return (rhs + total) / (6.0 + coef)


def band_solve(q, rhs, coef, row_ok):
    rows, planes = q.shape[0], q.shape[1]
    for k in range(1, SWEEPS + 1):
        centre = q[1:-1, :-1]
        zm = jnp.concatenate([jnp.zeros_like(centre[:, :1]), centre[:, :-1]], axis=1)
        new = stencil(
            rhs[k : rows - k, : planes - k],
            coef[k : rows - k, : planes - k],
            q[2:, :-1],
            q[:-2, :-1],
            q[1:-1, 1:],
            zm,
            centre,
        )
        q = jnp.where(row_ok[k : rows - k], new, 0.0)
    return q


def ring_pairs(count):
    forward = [(i, i + 1) for i in range(count - 1)]
    return forward, [(t, s) for s, t in forward]


def rims(block, width):
    count = lax.axis_size("slab")
    forward, backward = ring_pairs(count)
    low = lax.ppermute(block[block.shape[0] - width :], "slab", forward)
    high = lax.ppermute(block[:width], "slab", backward)
    return jnp.concatenate([low, block, high], axis=0)


def exchange(items):
    count = lax.axis_size("slab")
    forward, backward = ring_pairs(count)
    cells = items[0][0].shape[-1]
    sizes = [width * (a.size // a.shape[0]) // cells for a, width in items]
    up = jnp.concatenate([a[a.shape[0] - w :].reshape(-1, cells) for a, w in items], axis=0)
    down = jnp.concatenate([a[:w].reshape(-1, cells) for a, w in items], axis=0)
    low = lax.ppermute(up, "slab", forward)
    high = lax.ppermute(down, "slab", backward)
    out, at = [], 0
    for (a, w), n in zip(items, sizes):
        shape = (w,) + a.shape[1:]
        out.append(
            jnp.concatenate([low[at : at + n].reshape(shape), a, high[at : at + n].reshape(shape)], axis=0)
        )
        at += n
    return out


def deep_step(q, rhs, coef, ok):
    centre = q[1:-1]
    zero = jnp.zeros_like(centre[:, :1])
    new = stencil(
        rhs,
        coef,
        q[2:],
        q[:-2],
        jnp.concatenate([centre[:, 1:], zero], axis=1),
        jnp.concatenate([zero, centre[:, :-1]], axis=1),
        centre,
    )
    return jnp.where(ok, new, 0.0)


def deep_solve(q, rhs, coef, row_ok):
    rows = q.shape[0]
    for k in range(1, SWEEPS + 1):
        centre = q[1:-1]
        zero = jnp.zeros_like(centre[:, :1])
        new = stencil(
            rhs[k : rows - k],
            coef[k : rows - k],
            q[2:],
            q[:-2],
            jnp.concatenate([centre[:, 1:], zero], axis=1),
            jnp.concatenate([zero, centre[:, :-1]], axis=1),
            centre,
        )
        q = jnp.where(row_ok[k : rows - k], new, 0.0)
    return q


def allsum_axis(v, axis):
    count = lax.axis_size(axis)
    step = 1
    while step < count:
        v = v + lax.ppermute(v, axis, [(i, i ^ step) for i in range(count)])
        step *= 2
    return v


def shell_sum(v, side_count):
    count = lax.axis_size("slab")
    base = (side_count - 1) * count
    step = 1
    while step < count:
        pairs = [(base + i, base + (i ^ step)) for i in range(count)]
        v = v + lax.ppermute(v, ("side", "slab"), pairs)
        step *= 2
    return v


def allsum(v):
    return allsum_axis(allsum_axis(v, "slab"), "side")


def body(
    flow_force, flow_coef, flow_init, compliance, shell_load, disp_init, patch_len, owner, block_row
):
    force_here = flow_force[0]
    coef_here = flow_coef[0]
    start_here = flow_init[0]
    slab_rows, planes, line_cells = force_here.shape
    assert slab_rows >= HALO and planes >= BAND
    side_count = lax.axis_size("side")
    side_id = lax.axis_index("side")
    slab_id = lax.axis_index("slab")
    shell_flag = side_id == side_count - 1
    live = (jnp.arange(line_cells)[None, :] < patch_len[:, None]).astype(jnp.float32)
    own = (owner[:, 0] == side_id).astype(jnp.float32)[:, None]
    own_live = own * live
    onehot = (block_row[None, :] == jnp.arange(slab_rows)[:, None]).astype(jnp.float32) * own[:, 0][None, :]
    pick = (block_row[:, None] == jnp.arange(slab_rows)[None, :]).astype(jnp.float32)

    deep_planes = planes - BAND
    disp_zero = own_live * disp_init
    plane_zero = jnp.sum(onehot[:, :, None] * (live * disp_zero)[None], axis=1)
    packed, plane_zero_rims = exchange(
        [
            (jnp.concatenate([start_here[:, :BAND], force_here[:, :BAND], coef_here[:, :BAND]], axis=1), HALO),
            (plane_zero, HALO),
        ]
    )
    init_deep, fc_deep = exchange(
        [
            (start_here[:, BAND:], 2),
            (jnp.concatenate([force_here[:, BAND:], coef_here[:, BAND:]], axis=1), 1),
        ]
    )
    init_band, force_band, coef_band = (
        packed[:, :BAND],
        packed[:, BAND : 2 * BAND],
        packed[:, 2 * BAND :],
    )
    init_deep = jnp.concatenate([init_band[HALO - 2 : HALO + slab_rows + 2], init_deep], axis=1)
    force_deep = jnp.concatenate(
        [force_band[HALO - 1 : HALO + slab_rows + 1], fc_deep[:, :deep_planes]], axis=1
    )
    coef_deep = jnp.concatenate([coef_band[HALO - 1 : HALO + slab_rows + 1], fc_deep[:, deep_planes:]], axis=1)
    global_row = slab_id * slab_rows + jnp.arange(slab_rows + 2 * HALO) - HALO
    total_rows = slab_rows * lax.axis_size("slab")
    row_ok = ((global_row >= 0) & (global_row < total_rows))[:, None, None]

    ok_one = row_ok[HALO - 1 : HALO + slab_rows + 1]
    ok_two = row_ok[HALO : HALO + slab_rows]

    def evaluate(disp, plane_rims=None, extra=()):
        if plane_rims is None:
            plane = jnp.sum(onehot[:, :, None] * (live * disp)[None], axis=1)
            got = exchange([(plane, HALO)] + list(extra))
            plane_rims, extra = got[0], got[1:]
        rhs = force_band.at[:, 0, :].add(plane_rims)
        band = band_solve(init_band, rhs, coef_band, row_ok)
        traction = PENALTY * jnp.sum(pick[:, :, None] * band[:, 0, :][None], axis=1)
        loaded = live * (shell_load - traction)
        tilde = own_live * jnp.sum(compliance * loaded[:, None, :], axis=-1)
        return tilde, band, extra

    tilde_zero, unused, unused_extra = evaluate(disp_zero, plane_zero_rims)
    resid_zero = tilde_zero - disp_zero
    disp_one = disp_zero + RELAX * resid_zero
    tilde_one, unused, unused_extra = evaluate(disp_one)
    init_deep, tilde_one = lax.optimization_barrier((init_deep, tilde_one))
    deep = lax.cond(
        shell_flag,
        lambda: jnp.zeros((slab_rows,) + init_deep.shape[1:], jnp.float32),
        lambda: deep_step(
            deep_step(init_deep, force_deep, coef_deep, ok_one), force_deep[1:-1], coef_deep[1:-1], ok_two
        ),
    )
    resid_one = tilde_one - disp_one
    diff_one = resid_one - resid_zero
    sums = allsum(jnp.stack([jnp.sum(diff_one * diff_one), jnp.sum(diff_one * resid_one)]))
    gram_aa, gram_ab = sums[0], sums[1]
    coeff = -gram_ab / (gram_aa + (0.001 * gram_aa + 1e-06))
    disp_two = tilde_one + coeff * (tilde_one - tilde_zero)
    tilde_two, band_two, (deep,) = evaluate(disp_two, extra=[(deep, 2)])
    deep = lax.cond(
        shell_flag,
        lambda: jnp.zeros((slab_rows,) + deep.shape[1:], jnp.float32),
        lambda: deep_step(
            deep_step(deep, force_deep, coef_deep, ok_one), force_deep[1:-1], coef_deep[1:-1], ok_two
        ),
    )
    resid_two = tilde_two - disp_two
    newer = resid_two - resid_one
    partial = jnp.stack(
        [
            jnp.sum(newer * newer),
            jnp.sum(newer * diff_one),
            jnp.sum(newer * resid_two),
            jnp.sum(diff_one * resid_two),
        ]
    )
    patches_here = tilde_two.shape[0]
    outgoing = jnp.concatenate(
        [
            jnp.concatenate([tilde_two, tilde_one, tilde_zero, resid_two], axis=0),
            sum(
                jnp.where(jnp.arange(line_cells) == k, partial[k], 0.0) for k in range(4)
            )[None],
        ],
        axis=0,
    )
    gathered = outgoing
    for source in range(side_count - 1):
        gathered = gathered + lax.ppermute(outgoing, "side", [(source, side_count - 1)])
    sums = shell_sum(gathered[4 * patches_here, :4], side_count)
    gram_nn, gram_no, proj_new, proj_old = sums[0], sums[1], sums[2], sums[3]
    tilde_two, tilde_one, tilde_zero, resid_two = (
        gathered[k * patches_here : (k + 1) * patches_here] for k in range(4)
    )

    shift_two = 0.001 * (gram_nn + gram_aa) + 1e-06
    diag_new = gram_nn + shift_two
    diag_old = gram_aa + shift_two
    determ = diag_new * diag_old - gram_no * gram_no
    coeff_new = (-proj_new * diag_old + proj_old * gram_no) / determ
    coeff_old = (-proj_old * diag_new + proj_new * gram_no) / determ
    disp_three = (
        tilde_two + coeff_new * (tilde_two - tilde_one) + coeff_old * (tilde_one - tilde_zero)
    )

    flow_state = jnp.concatenate([band_two, deep[:, band_two.shape[1] :]], axis=1)
    disp_next = jnp.where(shell_flag, disp_three, 0.0)[None]
    residual = jnp.where(shell_flag, resid_two, 0.0)[None]
    flow_final = jnp.where(shell_flag, 0.0, flow_state)[None]
    return (disp_next, residual, flow_final)


def solution(mesh):
    return jax.shard_map(
        body,
        mesh=mesh,
        in_specs=(
            P("side", "slab", None, None),
            P("side", "slab", None, None),
            P("side", "slab", None, None),
            P("slab", None, None),
            P("slab", None),
            P("slab", None),
            P("slab"),
            P("slab", None),
            P("slab"),
        ),
        out_specs=(P("side", "slab", None), P("side", "slab", None), P("side", "slab", None, None)),
        check_vma=False,
    )
```

```python
import jax
import jax.numpy as jnp
from jax import lax
from jax.sharding import PartitionSpec as P

SWEEPS = 4
CAP = 4
RELAX = 0.5
PENALTY = 3.0
HALO = SWEEPS
BAND = 2 * SWEEPS


def shift_y(a):
    zero = jnp.zeros_like(a[..., :1])
    return (jnp.concatenate([a[..., 1:], zero], axis=-1), jnp.concatenate([zero, a[..., :-1]], axis=-1))


def stencil(rhs, coef, xp, xm, zp, zm, centre):
    yp, ym = shift_y(centre)
    total = ((((xp + xm) + zp) + zm) + yp) + ym
    return (rhs + total) / (6.0 + coef)


def band_solve(q, rhs, coef, row_ok):
    rows, planes = q.shape[0], q.shape[1]
    for k in range(1, SWEEPS + 1):
        centre = q[1:-1, :-1]
        zm = jnp.concatenate([jnp.zeros_like(centre[:, :1]), centre[:, :-1]], axis=1)
        new = stencil(
            rhs[k : rows - k, : planes - k],
            coef[k : rows - k, : planes - k],
            q[2:, :-1],
            q[:-2, :-1],
            q[1:-1, 1:],
            zm,
            centre,
        )
        q = jnp.where(row_ok[k : rows - k], new, 0.0)
    return q


def ring_pairs(count):
    forward = [(i, i + 1) for i in range(count - 1)]
    return forward, [(t, s) for s, t in forward]


def rims(block, width):
    count = lax.axis_size("slab")
    forward, backward = ring_pairs(count)
    low = lax.ppermute(block[block.shape[0] - width :], "slab", forward)
    high = lax.ppermute(block[:width], "slab", backward)
    return jnp.concatenate([low, block, high], axis=0)


def exchange(items):
    count = lax.axis_size("slab")
    forward, backward = ring_pairs(count)
    cells = items[0][0].shape[-1]
    sizes = [width * (a.size // a.shape[0]) // cells for a, width in items]
    up = jnp.concatenate([a[a.shape[0] - w :].reshape(-1, cells) for a, w in items], axis=0)
    down = jnp.concatenate([a[:w].reshape(-1, cells) for a, w in items], axis=0)
    low = lax.ppermute(up, "slab", forward)
    high = lax.ppermute(down, "slab", backward)
    out, at = [], 0
    for (a, w), n in zip(items, sizes):
        shape = (w,) + a.shape[1:]
        out.append(
            jnp.concatenate([low[at : at + n].reshape(shape), a, high[at : at + n].reshape(shape)], axis=0)
        )
        at += n
    return out


def deep_step(q, rhs, coef, ok):
    centre = q[1:-1]
    zero = jnp.zeros_like(centre[:, :1])
    new = stencil(
        rhs,
        coef,
        q[2:],
        q[:-2],
        jnp.concatenate([centre[:, 1:], zero], axis=1),
        jnp.concatenate([zero, centre[:, :-1]], axis=1),
        centre,
    )
    return jnp.where(ok, new, 0.0)


def deep_solve(q, rhs, coef, row_ok):
    rows = q.shape[0]
    for k in range(1, SWEEPS + 1):
        centre = q[1:-1]
        zero = jnp.zeros_like(centre[:, :1])
        new = stencil(
            rhs[k : rows - k],
            coef[k : rows - k],
            q[2:],
            q[:-2],
            jnp.concatenate([centre[:, 1:], zero], axis=1),
            jnp.concatenate([zero, centre[:, :-1]], axis=1),
            centre,
        )
        q = jnp.where(row_ok[k : rows - k], new, 0.0)
    return q


def allsum_axis(v, axis):
    count = lax.axis_size(axis)
    step = 1
    while step < count:
        v = v + lax.ppermute(v, axis, [(i, i ^ step) for i in range(count)])
        step *= 2
    return v


def shell_sum(v, side_count):
    count = lax.axis_size("slab")
    base = (side_count - 1) * count
    step = 1
    while step < count:
        pairs = [(base + i, base + (i ^ step)) for i in range(count)]
        v = v + lax.ppermute(v, ("side", "slab"), pairs)
        step *= 2
    return v


def allsum(v):
    return allsum_axis(allsum_axis(v, "slab"), "side")


def body(
    flow_force, flow_coef, flow_init, compliance, shell_load, disp_init, patch_len, owner, block_row
):
    force_here = flow_force[0]
    coef_here = flow_coef[0]
    start_here = flow_init[0]
    slab_rows, planes, line_cells = force_here.shape
    assert slab_rows >= HALO and planes >= BAND
    side_count = lax.axis_size("side")
    side_id = lax.axis_index("side")
    slab_id = lax.axis_index("slab")
    shell_flag = side_id == side_count - 1
    live = (jnp.arange(line_cells)[None, :] < patch_len[:, None]).astype(jnp.float32)
    own = (owner[:, 0] == side_id).astype(jnp.float32)[:, None]
    own_live = own * live
    onehot = (block_row[None, :] == jnp.arange(slab_rows)[:, None]).astype(jnp.float32) * own[:, 0][None, :]
    pick = (block_row[:, None] == jnp.arange(slab_rows)[None, :]).astype(jnp.float32)
    owned = (owner[:, 0] == side_id).astype(jnp.int32)
    rank = jnp.cumsum(owned) - 1
    slot_hit = (owned[None, :] == 1) & (rank[None, :] == jnp.arange(CAP)[:, None])
    slot_of = slot_hit.astype(jnp.float32)
    slot_patch = jnp.sum(slot_hit.astype(jnp.int32) * jnp.arange(owned.shape[0])[None, :], axis=1)

    deep_planes = planes - BAND
    disp_zero = own_live * disp_init
    plane_zero = jnp.sum(onehot[:, :, None] * (live * disp_zero)[None], axis=1)
    packed, plane_zero_rims = exchange(
        [
            (jnp.concatenate([start_here[:, :BAND], force_here[:, :BAND], coef_here[:, :BAND]], axis=1), HALO),
            (plane_zero, HALO),
        ]
    )
    init_band, force_band, coef_band = (
        packed[:, :BAND],
        packed[:, BAND : 2 * BAND],
        packed[:, 2 * BAND :],
    )
    global_row = slab_id * slab_rows + jnp.arange(slab_rows + 2 * HALO) - HALO
    total_rows = slab_rows * lax.axis_size("slab")
    row_ok = ((global_row >= 0) & (global_row < total_rows))[:, None, None]

    ok_one = row_ok[HALO - 1 : HALO + slab_rows + 1]
    ok_two = row_ok[HALO : HALO + slab_rows]

    def evaluate(disp, plane_rims=None, extra=()):
        if plane_rims is None:
            plane = jnp.sum(onehot[:, :, None] * (live * disp)[None], axis=1)
            got = exchange([(plane, HALO)] + list(extra))
            plane_rims, extra = got[0], got[1:]
        rhs = force_band.at[:, 0, :].add(plane_rims)
        band = band_solve(init_band, rhs, coef_band, row_ok)
        traction = PENALTY * jnp.sum(pick[:, :, None] * band[:, 0, :][None], axis=1)
        loaded = live * (shell_load - traction)
        picked = jnp.sum(slot_of[:, :, None] * loaded[None], axis=1)
        products = jnp.stack(
            [
                jnp.sum(lax.dynamic_index_in_dim(compliance, slot_patch[k], keepdims=False) * picked[k][None, :], axis=-1)
                for k in range(CAP)
            ]
        )
        tilde = own_live * jnp.sum(slot_of.T[:, :, None] * products[None], axis=1)
        return tilde, band, extra

    tilde_zero, unused, unused_extra = evaluate(disp_zero, plane_zero_rims)
    deep_init_src, deep_fc_src, tilde_zero = lax.optimization_barrier(
        (start_here[:, BAND:], jnp.concatenate([force_here[:, BAND:], coef_here[:, BAND:]], axis=1), tilde_zero)
    )
    init_deep, fc_deep = exchange([(deep_init_src, 2), (deep_fc_src, 1)])
    init_deep = jnp.concatenate([init_band[HALO - 2 : HALO + slab_rows + 2], init_deep], axis=1)
    force_deep = jnp.concatenate(
        [force_band[HALO - 1 : HALO + slab_rows + 1], fc_deep[:, :deep_planes]], axis=1
    )
    coef_deep = jnp.concatenate([coef_band[HALO - 1 : HALO + slab_rows + 1], fc_deep[:, deep_planes:]], axis=1)
    resid_zero = tilde_zero - disp_zero
    disp_one = disp_zero + RELAX * resid_zero
    tilde_one, unused, unused_extra = evaluate(disp_one)
    init_deep, tilde_one = lax.optimization_barrier((init_deep, tilde_one))
    deep = lax.cond(
        shell_flag,
        lambda: jnp.zeros((slab_rows,) + init_deep.shape[1:], jnp.float32),
        lambda: deep_step(
            deep_step(init_deep, force_deep, coef_deep, ok_one), force_deep[1:-1], coef_deep[1:-1], ok_two
        ),
    )
    resid_one = tilde_one - disp_one
    diff_one = resid_one - resid_zero
    sums = allsum(jnp.stack([jnp.sum(diff_one * diff_one), jnp.sum(diff_one * resid_one)]))
    gram_aa, gram_ab = sums[0], sums[1]
    coeff = -gram_ab / (gram_aa + (0.001 * gram_aa + 1e-06))
    disp_two = tilde_one + coeff * (tilde_one - tilde_zero)
    tilde_two, band_two, (deep,) = evaluate(disp_two, extra=[(deep, 2)])
    deep = lax.cond(
        shell_flag,
        lambda: jnp.zeros((slab_rows,) + deep.shape[1:], jnp.float32),
        lambda: deep_step(
            deep_step(deep, force_deep, coef_deep, ok_one), force_deep[1:-1], coef_deep[1:-1], ok_two
        ),
    )
    resid_two = tilde_two - disp_two
    newer = resid_two - resid_one
    partial = jnp.stack(
        [
            jnp.sum(newer * newer),
            jnp.sum(newer * diff_one),
            jnp.sum(newer * resid_two),
            jnp.sum(diff_one * resid_two),
        ]
    )
    patches_here = tilde_two.shape[0]
    outgoing = jnp.concatenate(
        [
            jnp.concatenate([tilde_two, tilde_one, tilde_zero, resid_two], axis=0),
            sum(
                jnp.where(jnp.arange(line_cells) == k, partial[k], 0.0) for k in range(4)
            )[None],
        ],
        axis=0,
    )
    gathered = outgoing
    for source in range(side_count - 1):
        gathered = gathered + lax.ppermute(outgoing, "side", [(source, side_count - 1)])
    sums = shell_sum(gathered[4 * patches_here, :4], side_count)
    gram_nn, gram_no, proj_new, proj_old = sums[0], sums[1], sums[2], sums[3]
    tilde_two, tilde_one, tilde_zero, resid_two = (
        gathered[k * patches_here : (k + 1) * patches_here] for k in range(4)
    )

    shift_two = 0.001 * (gram_nn + gram_aa) + 1e-06
    diag_new = gram_nn + shift_two
    diag_old = gram_aa + shift_two
    determ = diag_new * diag_old - gram_no * gram_no
    coeff_new = (-proj_new * diag_old + proj_old * gram_no) / determ
    coeff_old = (-proj_old * diag_new + proj_new * gram_no) / determ
    disp_three = (
        tilde_two + coeff_new * (tilde_two - tilde_one) + coeff_old * (tilde_one - tilde_zero)
    )

    flow_state = jnp.concatenate([band_two, deep[:, band_two.shape[1] :]], axis=1)
    disp_next = jnp.where(shell_flag, disp_three, 0.0)[None]
    residual = jnp.where(shell_flag, resid_two, 0.0)[None]
    flow_final = jnp.where(shell_flag, 0.0, flow_state)[None]
    return (disp_next, residual, flow_final)


def solution(mesh):
    return jax.shard_map(
        body,
        mesh=mesh,
        in_specs=(
            P("side", "slab", None, None),
            P("side", "slab", None, None),
            P("side", "slab", None, None),
            P("slab", None, None),
            P("slab", None),
            P("slab", None),
            P("slab"),
            P("slab", None),
            P("slab"),
        ),
        out_specs=(P("side", "slab", None), P("side", "slab", None), P("side", "slab", None, None)),
        check_vma=False,
    )
```

```python
import jax
import jax.numpy as jnp
from jax import lax
from jax.sharding import PartitionSpec as P

SWEEPS = 4
CAP = 4
RELAX = 0.5
PENALTY = 3.0
HALO = SWEEPS
BAND = 2 * SWEEPS


def shift_y(a):
    zero = jnp.zeros_like(a[..., :1])
    return (jnp.concatenate([a[..., 1:], zero], axis=-1), jnp.concatenate([zero, a[..., :-1]], axis=-1))


def stencil(rhs, coef, xp, xm, zp, zm, centre):
    yp, ym = shift_y(centre)
    total = ((((xp + xm) + zp) + zm) + yp) + ym
    return (rhs + total) / (6.0 + coef)


def band_solve(q, rhs, coef, row_ok):
    rows, planes = q.shape[0], q.shape[1]
    for k in range(1, SWEEPS + 1):
        centre = q[1:-1, :-1]
        zm = jnp.concatenate([jnp.zeros_like(centre[:, :1]), centre[:, :-1]], axis=1)
        new = stencil(
            rhs[k : rows - k, : planes - k],
            coef[k : rows - k, : planes - k],
            q[2:, :-1],
            q[:-2, :-1],
            q[1:-1, 1:],
            zm,
            centre,
        )
        q = jnp.where(row_ok[k : rows - k], new, 0.0)
    return q


def ring_pairs(count):
    forward = [(i, i + 1) for i in range(count - 1)]
    return forward, [(t, s) for s, t in forward]


def rims(block, width):
    count = lax.axis_size("slab")
    forward, backward = ring_pairs(count)
    low = lax.ppermute(block[block.shape[0] - width :], "slab", forward)
    high = lax.ppermute(block[:width], "slab", backward)
    return jnp.concatenate([low, block, high], axis=0)


def exchange(items):
    count = lax.axis_size("slab")
    forward, backward = ring_pairs(count)
    cells = items[0][0].shape[-1]
    sizes = [width * (a.size // a.shape[0]) // cells for a, width in items]
    up = jnp.concatenate([a[a.shape[0] - w :].reshape(-1, cells) for a, w in items], axis=0)
    down = jnp.concatenate([a[:w].reshape(-1, cells) for a, w in items], axis=0)
    low = lax.ppermute(up, "slab", forward)
    high = lax.ppermute(down, "slab", backward)
    out, at = [], 0
    for (a, w), n in zip(items, sizes):
        shape = (w,) + a.shape[1:]
        out.append(
            jnp.concatenate([low[at : at + n].reshape(shape), a, high[at : at + n].reshape(shape)], axis=0)
        )
        at += n
    return out


def deep_step(q, rhs, coef, ok):
    centre = q[1:-1]
    zero = jnp.zeros_like(centre[:, :1])
    new = stencil(
        rhs,
        coef,
        q[2:],
        q[:-2],
        jnp.concatenate([centre[:, 1:], zero], axis=1),
        jnp.concatenate([zero, centre[:, :-1]], axis=1),
        centre,
    )
    return jnp.where(ok, new, 0.0)


def deep_solve(q, rhs, coef, row_ok):
    rows = q.shape[0]
    for k in range(1, SWEEPS + 1):
        centre = q[1:-1]
        zero = jnp.zeros_like(centre[:, :1])
        new = stencil(
            rhs[k : rows - k],
            coef[k : rows - k],
            q[2:],
            q[:-2],
            jnp.concatenate([centre[:, 1:], zero], axis=1),
            jnp.concatenate([zero, centre[:, :-1]], axis=1),
            centre,
        )
        q = jnp.where(row_ok[k : rows - k], new, 0.0)
    return q


def allsum_axis(v, axis):
    count = lax.axis_size(axis)
    step = 1
    while step < count:
        v = v + lax.ppermute(v, axis, [(i, i ^ step) for i in range(count)])
        step *= 2
    return v


def shell_sum(v, side_count):
    count = lax.axis_size("slab")
    base = (side_count - 1) * count
    step = 1
    while step < count:
        pairs = [(base + i, base + (i ^ step)) for i in range(count)]
        v = v + lax.ppermute(v, ("side", "slab"), pairs)
        step *= 2
    return v


def allsum(v):
    return allsum_axis(allsum_axis(v, "slab"), "side")


def body(
    flow_force, flow_coef, flow_init, compliance, shell_load, disp_init, patch_len, owner, block_row
):
    force_here = flow_force[0]
    coef_here = flow_coef[0]
    start_here = flow_init[0]
    slab_rows, planes, line_cells = force_here.shape
    assert slab_rows >= HALO and planes >= BAND
    side_count = lax.axis_size("side")
    side_id = lax.axis_index("side")
    slab_id = lax.axis_index("slab")
    shell_flag = side_id == side_count - 1
    live = (jnp.arange(line_cells)[None, :] < patch_len[:, None]).astype(jnp.float32)
    own = (owner[:, 0] == side_id).astype(jnp.float32)[:, None]
    own_live = own * live
    onehot = (block_row[None, :] == jnp.arange(slab_rows)[:, None]).astype(jnp.float32) * own[:, 0][None, :]
    pick = (block_row[:, None] == jnp.arange(slab_rows)[None, :]).astype(jnp.float32)
    owned = (owner[:, 0] == side_id).astype(jnp.int32)
    rank = jnp.cumsum(owned) - 1
    slot_hit = (owned[None, :] == 1) & (rank[None, :] == jnp.arange(CAP)[:, None])
    slot_of = slot_hit.astype(jnp.float32)
    slot_patch = jnp.sum(slot_hit.astype(jnp.int32) * jnp.arange(owned.shape[0])[None, :], axis=1)

    deep_planes = planes - BAND
    disp_zero = own_live * disp_init
    plane_zero = jnp.sum(onehot[:, :, None] * (live * disp_zero)[None], axis=1)
    packed, plane_zero_rims = exchange(
        [
            (jnp.concatenate([start_here[:, :BAND], force_here[:, :BAND], coef_here[:, :BAND]], axis=1), HALO),
            (plane_zero, HALO),
        ]
    )
    init_deep, fc_deep = exchange(
        [
            (start_here[:, BAND:], 2),
            (jnp.concatenate([force_here[:, BAND:], coef_here[:, BAND:]], axis=1), 1),
        ]
    )
    init_band, force_band, coef_band = (
        packed[:, :BAND],
        packed[:, BAND : 2 * BAND],
        packed[:, 2 * BAND :],
    )
    init_deep = jnp.concatenate([init_band[HALO - 2 : HALO + slab_rows + 2], init_deep], axis=1)
    force_deep = jnp.concatenate(
        [force_band[HALO - 1 : HALO + slab_rows + 1], fc_deep[:, :deep_planes]], axis=1
    )
    coef_deep = jnp.concatenate([coef_band[HALO - 1 : HALO + slab_rows + 1], fc_deep[:, deep_planes:]], axis=1)
    global_row = slab_id * slab_rows + jnp.arange(slab_rows + 2 * HALO) - HALO
    total_rows = slab_rows * lax.axis_size("slab")
    row_ok = ((global_row >= 0) & (global_row < total_rows))[:, None, None]

    ok_one = row_ok[HALO - 1 : HALO + slab_rows + 1]
    ok_two = row_ok[HALO : HALO + slab_rows]

    def evaluate(disp, plane_rims=None, extra=()):
        if plane_rims is None:
            plane = jnp.sum(onehot[:, :, None] * (live * disp)[None], axis=1)
            got = exchange([(plane, HALO)] + list(extra))
            plane_rims, extra = got[0], got[1:]
        rhs = force_band.at[:, 0, :].add(plane_rims)
        band = band_solve(init_band, rhs, coef_band, row_ok)
        traction = PENALTY * jnp.sum(pick[:, :, None] * band[:, 0, :][None], axis=1)
        loaded = live * (shell_load - traction)
        picked = jnp.sum(slot_of[:, :, None] * loaded[None], axis=1)
        products = jnp.stack(
            [
                jnp.sum(lax.dynamic_index_in_dim(compliance, slot_patch[k], keepdims=False) * picked[k][None, :], axis=-1)
                for k in range(CAP)
            ]
        )
        tilde = own_live * jnp.sum(slot_of.T[:, :, None] * products[None], axis=1)
        return tilde, band, extra

    tilde_zero, unused, unused_extra = evaluate(disp_zero, plane_zero_rims)
    resid_zero = tilde_zero - disp_zero
    disp_one = disp_zero + RELAX * resid_zero
    tilde_one, unused, unused_extra = evaluate(disp_one)
    init_deep, tilde_one = lax.optimization_barrier((init_deep, tilde_one))
    deep = lax.cond(
        shell_flag,
        lambda: jnp.zeros((slab_rows,) + init_deep.shape[1:], jnp.float32),
        lambda: deep_step(
            deep_step(init_deep, force_deep, coef_deep, ok_one), force_deep[1:-1], coef_deep[1:-1], ok_two
        ),
    )
    resid_one = tilde_one - disp_one
    diff_one = resid_one - resid_zero
    sums = allsum(jnp.stack([jnp.sum(diff_one * diff_one), jnp.sum(diff_one * resid_one)]))
    gram_aa, gram_ab = sums[0], sums[1]
    coeff = -gram_ab / (gram_aa + (0.001 * gram_aa + 1e-06))
    disp_two = tilde_one + coeff * (tilde_one - tilde_zero)
    tilde_two, band_two, (deep,) = evaluate(disp_two, extra=[(deep, 2)])
    deep = lax.cond(
        shell_flag,
        lambda: jnp.zeros((slab_rows,) + deep.shape[1:], jnp.float32),
        lambda: deep_step(
            deep_step(deep, force_deep, coef_deep, ok_one), force_deep[1:-1], coef_deep[1:-1], ok_two
        ),
    )
    resid_two = tilde_two - disp_two
    newer = resid_two - resid_one
    partial = jnp.stack(
        [
            jnp.sum(newer * newer),
            jnp.sum(newer * diff_one),
            jnp.sum(newer * resid_two),
            jnp.sum(diff_one * resid_two),
        ]
    )
    patches_here = tilde_two.shape[0]
    outgoing = jnp.concatenate(
        [
            jnp.concatenate([tilde_two, tilde_one, tilde_zero, resid_two], axis=0),
            sum(
                jnp.where(jnp.arange(line_cells) == k, partial[k], 0.0) for k in range(4)
            )[None],
        ],
        axis=0,
    )
    gathered = outgoing
    for source in range(side_count - 1):
        gathered = gathered + lax.ppermute(outgoing, "side", [(source, side_count - 1)])
    sums = shell_sum(gathered[4 * patches_here, :4], side_count)
    gram_nn, gram_no, proj_new, proj_old = sums[0], sums[1], sums[2], sums[3]
    tilde_two, tilde_one, tilde_zero, resid_two = (
        gathered[k * patches_here : (k + 1) * patches_here] for k in range(4)
    )

    shift_two = 0.001 * (gram_nn + gram_aa) + 1e-06
    diag_new = gram_nn + shift_two
    diag_old = gram_aa + shift_two
    determ = diag_new * diag_old - gram_no * gram_no
    coeff_new = (-proj_new * diag_old + proj_old * gram_no) / determ
    coeff_old = (-proj_old * diag_new + proj_new * gram_no) / determ
    disp_three = (
        tilde_two + coeff_new * (tilde_two - tilde_one) + coeff_old * (tilde_one - tilde_zero)
    )

    flow_state = jnp.concatenate([band_two, deep[:, band_two.shape[1] :]], axis=1)
    disp_next = jnp.where(shell_flag, disp_three, 0.0)[None]
    residual = jnp.where(shell_flag, resid_two, 0.0)[None]
    flow_final = jnp.where(shell_flag, 0.0, flow_state)[None]
    return (disp_next, residual, flow_final)


def solution(mesh):
    return jax.shard_map(
        body,
        mesh=mesh,
        in_specs=(
            P("side", "slab", None, None),
            P("side", "slab", None, None),
            P("side", "slab", None, None),
            P("slab", None, None),
            P("slab", None),
            P("slab", None),
            P("slab"),
            P("slab", None),
            P("slab"),
        ),
        out_specs=(P("side", "slab", None), P("side", "slab", None), P("side", "slab", None, None)),
        check_vma=False,
    )
```

```python
import jax
import jax.numpy as jnp
from jax import lax
from jax.sharding import PartitionSpec as P

SWEEPS = 4
RELAX = 0.5
PENALTY = 3.0
HALO = SWEEPS
BAND = 2 * SWEEPS


def shift_y(a):
    zero = jnp.zeros_like(a[..., :1])
    return (jnp.concatenate([a[..., 1:], zero], axis=-1), jnp.concatenate([zero, a[..., :-1]], axis=-1))


def stencil(rhs, coef, xp, xm, zp, zm, centre):
    yp, ym = shift_y(centre)
    total = ((((xp + xm) + zp) + zm) + yp) + ym
    return (rhs + total) / (6.0 + coef)


def band_solve(q, rhs, coef, row_ok):
    rows, planes = q.shape[0], q.shape[1]
    for k in range(1, SWEEPS + 1):
        centre = q[1:-1, :-1]
        zm = jnp.concatenate([jnp.zeros_like(centre[:, :1]), centre[:, :-1]], axis=1)
        new = stencil(
            rhs[k : rows - k, : planes - k],
            coef[k : rows - k, : planes - k],
            q[2:, :-1],
            q[:-2, :-1],
            q[1:-1, 1:],
            zm,
            centre,
        )
        q = jnp.where(row_ok[k : rows - k], new, 0.0)
    return q


def ring_pairs(count):
    forward = [(i, i + 1) for i in range(count - 1)]
    return forward, [(t, s) for s, t in forward]


def rims(block, width):
    count = lax.axis_size("slab")
    forward, backward = ring_pairs(count)
    low = lax.ppermute(block[block.shape[0] - width :], "slab", forward)
    high = lax.ppermute(block[:width], "slab", backward)
    return jnp.concatenate([low, block, high], axis=0)


def exchange(items):
    count = lax.axis_size("slab")
    forward, backward = ring_pairs(count)
    cells = items[0][0].shape[-1]
    sizes = [width * (a.size // a.shape[0]) // cells for a, width in items]
    up = jnp.concatenate([a[a.shape[0] - w :].reshape(-1, cells) for a, w in items], axis=0)
    down = jnp.concatenate([a[:w].reshape(-1, cells) for a, w in items], axis=0)
    low = lax.ppermute(up, "slab", forward)
    high = lax.ppermute(down, "slab", backward)
    out, at = [], 0
    for (a, w), n in zip(items, sizes):
        shape = (w,) + a.shape[1:]
        out.append(
            jnp.concatenate([low[at : at + n].reshape(shape), a, high[at : at + n].reshape(shape)], axis=0)
        )
        at += n
    return out


def deep_step(q, rhs, coef, ok):
    centre = q[1:-1]
    zero = jnp.zeros_like(centre[:, :1])
    new = stencil(
        rhs,
        coef,
        q[2:],
        q[:-2],
        jnp.concatenate([centre[:, 1:], zero], axis=1),
        jnp.concatenate([zero, centre[:, :-1]], axis=1),
        centre,
    )
    return jnp.where(ok, new, 0.0)


def deep_solve(q, rhs, coef, row_ok):
    rows = q.shape[0]
    for k in range(1, SWEEPS + 1):
        centre = q[1:-1]
        zero = jnp.zeros_like(centre[:, :1])
        new = stencil(
            rhs[k : rows - k],
            coef[k : rows - k],
            q[2:],
            q[:-2],
            jnp.concatenate([centre[:, 1:], zero], axis=1),
            jnp.concatenate([zero, centre[:, :-1]], axis=1),
            centre,
        )
        q = jnp.where(row_ok[k : rows - k], new, 0.0)
    return q


def allsum_axis(v, axis):
    count = lax.axis_size(axis)
    step = 1
    while step < count:
        v = v + lax.ppermute(v, axis, [(i, i ^ step) for i in range(count)])
        step *= 2
    return v


def shell_sum(v, side_count):
    count = lax.axis_size("slab")
    base = (side_count - 1) * count
    step = 1
    while step < count:
        pairs = [(base + i, base + (i ^ step)) for i in range(count)]
        v = v + lax.ppermute(v, ("side", "slab"), pairs)
        step *= 2
    return v


def allsum(v):
    return allsum_axis(allsum_axis(v, "slab"), "side")


def body(
    flow_force, flow_coef, flow_init, compliance, shell_load, disp_init, patch_len, owner, block_row
):
    force_here = flow_force[0]
    coef_here = flow_coef[0]
    start_here = flow_init[0]
    slab_rows, planes, line_cells = force_here.shape
    assert slab_rows >= HALO and planes >= BAND
    side_count = lax.axis_size("side")
    side_id = lax.axis_index("side")
    slab_id = lax.axis_index("slab")
    shell_flag = side_id == side_count - 1
    live = (jnp.arange(line_cells)[None, :] < patch_len[:, None]).astype(jnp.float32)
    own = (owner[:, 0] == side_id).astype(jnp.float32)[:, None]
    own_live = own * live
    onehot = (block_row[None, :] == jnp.arange(slab_rows)[:, None]).astype(jnp.float32) * own[:, 0][None, :]
    pick = (block_row[:, None] == jnp.arange(slab_rows)[None, :]).astype(jnp.float32)

    deep_planes = planes - BAND
    disp_zero = own_live * disp_init
    plane_zero = jnp.sum(onehot[:, :, None] * (live * disp_zero)[None], axis=1)
    packed, plane_zero_rims = exchange(
        [
            (jnp.concatenate([start_here[:, :BAND], force_here[:, :BAND], coef_here[:, :BAND]], axis=1), HALO),
            (plane_zero, HALO),
        ]
    )
    init_deep, fc_deep = exchange(
        [
            (start_here[:, BAND:], 2),
            (jnp.concatenate([force_here[:, BAND:], coef_here[:, BAND:]], axis=1), 1),
        ]
    )
    init_band, force_band, coef_band = (
        packed[:, :BAND],
        packed[:, BAND : 2 * BAND],
        packed[:, 2 * BAND :],
    )
    init_deep = jnp.concatenate([init_band[HALO - 2 : HALO + slab_rows + 2], init_deep], axis=1)
    force_deep = jnp.concatenate(
        [force_band[HALO - 1 : HALO + slab_rows + 1], fc_deep[:, :deep_planes]], axis=1
    )
    coef_deep = jnp.concatenate([coef_band[HALO - 1 : HALO + slab_rows + 1], fc_deep[:, deep_planes:]], axis=1)
    global_row = slab_id * slab_rows + jnp.arange(slab_rows + 2 * HALO) - HALO
    total_rows = slab_rows * lax.axis_size("slab")
    row_ok = ((global_row >= 0) & (global_row < total_rows))[:, None, None]

    ok_one = row_ok[HALO - 1 : HALO + slab_rows + 1]
    ok_two = row_ok[HALO : HALO + slab_rows]

    def plane_of(disp):
        return jnp.sum(onehot[:, :, None] * (live * disp)[None], axis=1)

    def evaluate(disp, plane_rims=None, extra=()):
        if plane_rims is None:
            got = exchange([(plane_of(disp), HALO)] + list(extra))
            plane_rims, extra = got[0], got[1:]
        rhs = force_band.at[:, 0, :].add(plane_rims)
        band = band_solve(init_band, rhs, coef_band, row_ok)
        traction = PENALTY * jnp.sum(pick[:, :, None] * band[:, 0, :][None], axis=1)
        loaded = live * (shell_load - traction)
        tilde = own_live * jnp.sum(compliance * loaded[:, None, :], axis=-1)
        return tilde, band, extra

    tilde_zero, unused, unused_extra = evaluate(disp_zero, plane_zero_rims)
    resid_zero = tilde_zero - disp_zero
    disp_one = disp_zero + RELAX * resid_zero
    tilde_one, unused, unused_extra = evaluate(disp_one)
    init_deep, tilde_one = lax.optimization_barrier((init_deep, tilde_one))
    deep = lax.cond(
        shell_flag,
        lambda: jnp.zeros((slab_rows,) + init_deep.shape[1:], jnp.float32),
        lambda: deep_step(
            deep_step(init_deep, force_deep, coef_deep, ok_one), force_deep[1:-1], coef_deep[1:-1], ok_two
        ),
    )
    resid_one = tilde_one - disp_one
    diff_one = resid_one - resid_zero
    sums = allsum(jnp.stack([jnp.sum(diff_one * diff_one), jnp.sum(diff_one * resid_one)]))
    step_one = tilde_one - tilde_zero
    rims_base, rims_step, deep = exchange(
        [(plane_of(tilde_one), HALO), (plane_of(step_one), HALO), (deep, 2)]
    )
    band_base = band_solve(init_band, force_band.at[:, 0, :].add(rims_base), coef_band, row_ok)
    band_step = band_solve(
        jnp.zeros_like(init_band), jnp.zeros_like(force_band).at[:, 0, :].set(rims_step), coef_band, row_ok
    )
    both = jnp.stack([band_base[:, 0, :], band_step[:, 0, :]])
    traction = PENALTY * jnp.sum(pick[None, :, :, None] * both[:, None], axis=2)
    loaded = live[None] * (jnp.stack([shell_load, jnp.zeros_like(shell_load)]) - traction)
    applied = own_live[None] * jnp.sum(compliance[None] * loaded[:, :, None, :], axis=-1)
    tilde_base, tilde_step = applied[0], applied[1]
    gram_aa, gram_ab = sums[0], sums[1]
    coeff = -gram_ab / (gram_aa + (0.001 * gram_aa + 1e-06))
    disp_two = tilde_one + coeff * step_one
    tilde_two = tilde_base + coeff * tilde_step
    band_two = band_base + coeff * band_step
    deep = lax.cond(
        shell_flag,
        lambda: jnp.zeros((slab_rows,) + deep.shape[1:], jnp.float32),
        lambda: deep_step(
            deep_step(deep, force_deep, coef_deep, ok_one), force_deep[1:-1], coef_deep[1:-1], ok_two
        ),
    )
    resid_two = tilde_two - disp_two
    newer = resid_two - resid_one
    partial = jnp.stack(
        [
            jnp.sum(newer * newer),
            jnp.sum(newer * diff_one),
            jnp.sum(newer * resid_two),
            jnp.sum(diff_one * resid_two),
        ]
    )
    patches_here = tilde_two.shape[0]
    outgoing = jnp.concatenate(
        [
            jnp.concatenate([tilde_two, tilde_one, tilde_zero, resid_two], axis=0),
            sum(
                jnp.where(jnp.arange(line_cells) == k, partial[k], 0.0) for k in range(4)
            )[None],
        ],
        axis=0,
    )
    gathered = outgoing
    for source in range(side_count - 1):
        gathered = gathered + lax.ppermute(outgoing, "side", [(source, side_count - 1)])
    sums = shell_sum(gathered[4 * patches_here, :4], side_count)
    gram_nn, gram_no, proj_new, proj_old = sums[0], sums[1], sums[2], sums[3]
    tilde_two, tilde_one, tilde_zero, resid_two = (
        gathered[k * patches_here : (k + 1) * patches_here] for k in range(4)
    )

    shift_two = 0.001 * (gram_nn + gram_aa) + 1e-06
    diag_new = gram_nn + shift_two
    diag_old = gram_aa + shift_two
    determ = diag_new * diag_old - gram_no * gram_no
    coeff_new = (-proj_new * diag_old + proj_old * gram_no) / determ
    coeff_old = (-proj_old * diag_new + proj_new * gram_no) / determ
    disp_three = (
        tilde_two + coeff_new * (tilde_two - tilde_one) + coeff_old * (tilde_one - tilde_zero)
    )

    flow_state = jnp.concatenate([band_two, deep[:, band_two.shape[1] :]], axis=1)
    disp_next = jnp.where(shell_flag, disp_three, 0.0)[None]
    residual = jnp.where(shell_flag, resid_two, 0.0)[None]
    flow_final = jnp.where(shell_flag, 0.0, flow_state)[None]
    return (disp_next, residual, flow_final)


def solution(mesh):
    return jax.shard_map(
        body,
        mesh=mesh,
        in_specs=(
            P("side", "slab", None, None),
            P("side", "slab", None, None),
            P("side", "slab", None, None),
            P("slab", None, None),
            P("slab", None),
            P("slab", None),
            P("slab"),
            P("slab", None),
            P("slab"),
        ),
        out_specs=(P("side", "slab", None), P("side", "slab", None), P("side", "slab", None, None)),
        check_vma=False,
    )
```

```python
import jax
import jax.numpy as jnp
from jax import lax
from jax.sharding import PartitionSpec as P

SWEEPS = 4
RELAX = 0.5
PENALTY = 3.0
HALO = SWEEPS
BAND = 2 * SWEEPS


def shift_y(a):
    zero = jnp.zeros_like(a[..., :1])
    return (jnp.concatenate([a[..., 1:], zero], axis=-1), jnp.concatenate([zero, a[..., :-1]], axis=-1))


def stencil(rhs, coef, xp, xm, zp, zm, centre):
    yp, ym = shift_y(centre)
    total = ((((xp + xm) + zp) + zm) + yp) + ym
    return (rhs + total) / (6.0 + coef)


def band_solve(q, rhs, coef, row_ok):
    rows, planes = q.shape[0], q.shape[1]
    for k in range(1, SWEEPS + 1):
        centre = q[1:-1, :-1]
        zm = jnp.concatenate([jnp.zeros_like(centre[:, :1]), centre[:, :-1]], axis=1)
        new = stencil(
            rhs[k : rows - k, : planes - k],
            coef[k : rows - k, : planes - k],
            q[2:, :-1],
            q[:-2, :-1],
            q[1:-1, 1:],
            zm,
            centre,
        )
        q = jnp.where(row_ok[k : rows - k], new, 0.0)
    return q


def ring_pairs(count):
    forward = [(i, i + 1) for i in range(count - 1)]
    return forward, [(t, s) for s, t in forward]


def rims(block, width):
    count = lax.axis_size("slab")
    forward, backward = ring_pairs(count)
    low = lax.ppermute(block[block.shape[0] - width :], "slab", forward)
    high = lax.ppermute(block[:width], "slab", backward)
    return jnp.concatenate([low, block, high], axis=0)


def exchange(items):
    count = lax.axis_size("slab")
    forward, backward = ring_pairs(count)
    cells = items[0][0].shape[-1]
    sizes = [width * (a.size // a.shape[0]) // cells for a, width in items]
    up = jnp.concatenate([a[a.shape[0] - w :].reshape(-1, cells) for a, w in items], axis=0)
    down = jnp.concatenate([a[:w].reshape(-1, cells) for a, w in items], axis=0)
    low = lax.ppermute(up, "slab", forward)
    high = lax.ppermute(down, "slab", backward)
    out, at = [], 0
    for (a, w), n in zip(items, sizes):
        shape = (w,) + a.shape[1:]
        out.append(
            jnp.concatenate([low[at : at + n].reshape(shape), a, high[at : at + n].reshape(shape)], axis=0)
        )
        at += n
    return out


def deep_step(q, rhs, coef, ok):
    centre = q[1:-1]
    zero = jnp.zeros_like(centre[:, :1])
    new = stencil(
        rhs,
        coef,
        q[2:],
        q[:-2],
        jnp.concatenate([centre[:, 1:], zero], axis=1),
        jnp.concatenate([zero, centre[:, :-1]], axis=1),
        centre,
    )
    return jnp.where(ok, new, 0.0)


def deep_solve(q, rhs, coef, row_ok):
    rows = q.shape[0]
    for k in range(1, SWEEPS + 1):
        centre = q[1:-1]
        zero = jnp.zeros_like(centre[:, :1])
        new = stencil(
            rhs[k : rows - k],
            coef[k : rows - k],
            q[2:],
            q[:-2],
            jnp.concatenate([centre[:, 1:], zero], axis=1),
            jnp.concatenate([zero, centre[:, :-1]], axis=1),
            centre,
        )
        q = jnp.where(row_ok[k : rows - k], new, 0.0)
    return q


def allsum_axis(v, axis):
    count = lax.axis_size(axis)
    step = 1
    while step < count:
        v = v + lax.ppermute(v, axis, [(i, i ^ step) for i in range(count)])
        step *= 2
    return v


def shell_sum(v, side_count):
    count = lax.axis_size("slab")
    base = (side_count - 1) * count
    step = 1
    while step < count:
        pairs = [(base + i, base + (i ^ step)) for i in range(count)]
        v = v + lax.ppermute(v, ("side", "slab"), pairs)
        step *= 2
    return v


def allsum(v):
    return allsum_axis(allsum_axis(v, "slab"), "side")


def body(
    flow_force, flow_coef, flow_init, compliance, shell_load, disp_init, patch_len, owner, block_row
):
    force_here = flow_force[0]
    coef_here = flow_coef[0]
    start_here = flow_init[0]
    slab_rows, planes, line_cells = force_here.shape
    assert slab_rows >= HALO and planes >= BAND
    side_count = lax.axis_size("side")
    side_id = lax.axis_index("side")
    slab_id = lax.axis_index("slab")
    shell_flag = side_id == side_count - 1
    live = (jnp.arange(line_cells)[None, :] < patch_len[:, None]).astype(jnp.float32)
    own = (owner[:, 0] == side_id).astype(jnp.float32)[:, None]
    own_live = own * live
    onehot = (block_row[None, :] == jnp.arange(slab_rows)[:, None]).astype(jnp.float32) * own[:, 0][None, :]
    pick = (block_row[:, None] == jnp.arange(slab_rows)[None, :]).astype(jnp.float32)

    deep_planes = planes - BAND
    disp_zero = own_live * disp_init
    plane_zero = jnp.sum(onehot[:, :, None] * (live * disp_zero)[None], axis=1)
    packed, plane_zero_rims = exchange(
        [
            (jnp.concatenate([start_here[:, :BAND], force_here[:, :BAND], coef_here[:, :BAND]], axis=1), HALO),
            (plane_zero, HALO),
        ]
    )
    after_band = 0.0 * packed[0, 0, 0]
    init_deep, fc_deep = exchange(
        [
            (start_here[:, BAND:] + after_band, 2),
            (jnp.concatenate([force_here[:, BAND:], coef_here[:, BAND:]], axis=1) + after_band, 1),
        ]
    )
    init_band, force_band, coef_band = (
        packed[:, :BAND],
        packed[:, BAND : 2 * BAND],
        packed[:, 2 * BAND :],
    )
    init_deep = jnp.concatenate([init_band[HALO - 2 : HALO + slab_rows + 2], init_deep], axis=1)
    force_deep = jnp.concatenate(
        [force_band[HALO - 1 : HALO + slab_rows + 1], fc_deep[:, :deep_planes]], axis=1
    )
    coef_deep = jnp.concatenate([coef_band[HALO - 1 : HALO + slab_rows + 1], fc_deep[:, deep_planes:]], axis=1)
    global_row = slab_id * slab_rows + jnp.arange(slab_rows + 2 * HALO) - HALO
    total_rows = slab_rows * lax.axis_size("slab")
    row_ok = ((global_row >= 0) & (global_row < total_rows))[:, None, None]

    ok_one = row_ok[HALO - 1 : HALO + slab_rows + 1]
    ok_two = row_ok[HALO : HALO + slab_rows]

    def plane_of(disp):
        return jnp.sum(onehot[:, :, None] * (live * disp)[None], axis=1)

    def evaluate(disp, plane_rims=None, extra=()):
        if plane_rims is None:
            got = exchange([(plane_of(disp), HALO)] + list(extra))
            plane_rims, extra = got[0], got[1:]
        rhs = force_band.at[:, 0, :].add(plane_rims)
        band = band_solve(init_band, rhs, coef_band, row_ok)
        traction = PENALTY * jnp.sum(pick[:, :, None] * band[:, 0, :][None], axis=1)
        loaded = live * (shell_load - traction)
        tilde = own_live * jnp.sum(compliance * loaded[:, None, :], axis=-1)
        return tilde, band, extra

    tilde_zero, unused, unused_extra = evaluate(disp_zero, plane_zero_rims)
    resid_zero = tilde_zero - disp_zero
    disp_one = disp_zero + RELAX * resid_zero
    tilde_one, unused, unused_extra = evaluate(disp_one)
    init_deep, tilde_one = lax.optimization_barrier((init_deep, tilde_one))
    deep = lax.cond(
        shell_flag,
        lambda: jnp.zeros((slab_rows,) + init_deep.shape[1:], jnp.float32),
        lambda: deep_step(
            deep_step(init_deep, force_deep, coef_deep, ok_one), force_deep[1:-1], coef_deep[1:-1], ok_two
        ),
    )
    resid_one = tilde_one - disp_one
    diff_one = resid_one - resid_zero
    sums = allsum(jnp.stack([jnp.sum(diff_one * diff_one), jnp.sum(diff_one * resid_one)]))
    step_one = tilde_one - tilde_zero
    rims_base, rims_step, deep = exchange(
        [(plane_of(tilde_one), HALO), (plane_of(step_one), HALO), (deep, 2)]
    )
    band_base = band_solve(init_band, force_band.at[:, 0, :].add(rims_base), coef_band, row_ok)
    band_step = band_solve(
        jnp.zeros_like(init_band), jnp.zeros_like(force_band).at[:, 0, :].set(rims_step), coef_band, row_ok
    )
    both = jnp.stack([band_base[:, 0, :], band_step[:, 0, :]])
    traction = PENALTY * jnp.sum(pick[None, :, :, None] * both[:, None], axis=2)
    loaded = live[None] * (jnp.stack([shell_load, jnp.zeros_like(shell_load)]) - traction)
    applied = own_live[None] * jnp.sum(compliance[None] * loaded[:, :, None, :], axis=-1)
    tilde_base, tilde_step = applied[0], applied[1]
    gram_aa, gram_ab = sums[0], sums[1]
    coeff = -gram_ab / (gram_aa + (0.001 * gram_aa + 1e-06))
    disp_two = tilde_one + coeff * step_one
    tilde_two = tilde_base + coeff * tilde_step
    band_two = band_base + coeff * band_step
    deep = lax.cond(
        shell_flag,
        lambda: jnp.zeros((slab_rows,) + deep.shape[1:], jnp.float32),
        lambda: deep_step(
            deep_step(deep, force_deep, coef_deep, ok_one), force_deep[1:-1], coef_deep[1:-1], ok_two
        ),
    )
    resid_two = tilde_two - disp_two
    newer = resid_two - resid_one
    partial = jnp.stack(
        [
            jnp.sum(newer * newer),
            jnp.sum(newer * diff_one),
            jnp.sum(newer * resid_two),
            jnp.sum(diff_one * resid_two),
        ]
    )
    patches_here = tilde_two.shape[0]
    outgoing = jnp.concatenate(
        [
            jnp.concatenate([tilde_two, tilde_one, tilde_zero, resid_two], axis=0),
            sum(
                jnp.where(jnp.arange(line_cells) == k, partial[k], 0.0) for k in range(4)
            )[None],
        ],
        axis=0,
    )
    gathered = outgoing
    for source in range(side_count - 1):
        gathered = gathered + lax.ppermute(outgoing, "side", [(source, side_count - 1)])
    sums = shell_sum(gathered[4 * patches_here, :4], side_count)
    gram_nn, gram_no, proj_new, proj_old = sums[0], sums[1], sums[2], sums[3]
    tilde_two, tilde_one, tilde_zero, resid_two = (
        gathered[k * patches_here : (k + 1) * patches_here] for k in range(4)
    )

    shift_two = 0.001 * (gram_nn + gram_aa) + 1e-06
    diag_new = gram_nn + shift_two
    diag_old = gram_aa + shift_two
    determ = diag_new * diag_old - gram_no * gram_no
    coeff_new = (-proj_new * diag_old + proj_old * gram_no) / determ
    coeff_old = (-proj_old * diag_new + proj_new * gram_no) / determ
    disp_three = (
        tilde_two + coeff_new * (tilde_two - tilde_one) + coeff_old * (tilde_one - tilde_zero)
    )

    flow_state = jnp.concatenate([band_two, deep[:, band_two.shape[1] :]], axis=1)
    disp_next = jnp.where(shell_flag, disp_three, 0.0)[None]
    residual = jnp.where(shell_flag, resid_two, 0.0)[None]
    flow_final = jnp.where(shell_flag, 0.0, flow_state)[None]
    return (disp_next, residual, flow_final)


def solution(mesh):
    return jax.shard_map(
        body,
        mesh=mesh,
        in_specs=(
            P("side", "slab", None, None),
            P("side", "slab", None, None),
            P("side", "slab", None, None),
            P("slab", None, None),
            P("slab", None),
            P("slab", None),
            P("slab"),
            P("slab", None),
            P("slab"),
        ),
        out_specs=(P("side", "slab", None), P("side", "slab", None), P("side", "slab", None, None)),
        check_vma=False,
    )
```

```python
import jax
import jax.numpy as jnp
from jax import lax
from jax.sharding import PartitionSpec as P

SWEEPS = 4
RELAX = 0.5
PENALTY = 3.0
HALO = SWEEPS
BAND = 2 * SWEEPS


def shift_y(a):
    zero = jnp.zeros_like(a[..., :1])
    return (jnp.concatenate([a[..., 1:], zero], axis=-1), jnp.concatenate([zero, a[..., :-1]], axis=-1))


def stencil(rhs, coef, xp, xm, zp, zm, centre):
    yp, ym = shift_y(centre)
    total = ((((xp + xm) + zp) + zm) + yp) + ym
    return (rhs + total) / (6.0 + coef)


def band_solve(q, rhs, coef, row_ok):
    rows, planes = q.shape[0], q.shape[1]
    for k in range(1, SWEEPS + 1):
        centre = q[1:-1, :-1]
        zm = jnp.concatenate([jnp.zeros_like(centre[:, :1]), centre[:, :-1]], axis=1)
        new = stencil(
            rhs[k : rows - k, : planes - k],
            coef[k : rows - k, : planes - k],
            q[2:, :-1],
            q[:-2, :-1],
            q[1:-1, 1:],
            zm,
            centre,
        )
        q = jnp.where(row_ok[k : rows - k], new, 0.0)
    return q


def ring_pairs(count):
    forward = [(i, i + 1) for i in range(count - 1)]
    return forward, [(t, s) for s, t in forward]


def rims(block, width):
    count = lax.axis_size("slab")
    forward, backward = ring_pairs(count)
    low = lax.ppermute(block[block.shape[0] - width :], "slab", forward)
    high = lax.ppermute(block[:width], "slab", backward)
    return jnp.concatenate([low, block, high], axis=0)


def exchange(items):
    count = lax.axis_size("slab")
    forward, backward = ring_pairs(count)
    cells = items[0][0].shape[-1]
    sizes = [width * (a.size // a.shape[0]) // cells for a, width in items]
    up = jnp.concatenate([a[a.shape[0] - w :].reshape(-1, cells) for a, w in items], axis=0)
    down = jnp.concatenate([a[:w].reshape(-1, cells) for a, w in items], axis=0)
    low = lax.ppermute(up, "slab", forward)
    high = lax.ppermute(down, "slab", backward)
    out, at = [], 0
    for (a, w), n in zip(items, sizes):
        shape = (w,) + a.shape[1:]
        out.append(
            jnp.concatenate([low[at : at + n].reshape(shape), a, high[at : at + n].reshape(shape)], axis=0)
        )
        at += n
    return out


def deep_step(q, rhs, coef, ok):
    centre = q[1:-1]
    zero = jnp.zeros_like(centre[:, :1])
    new = stencil(
        rhs,
        coef,
        q[2:],
        q[:-2],
        jnp.concatenate([centre[:, 1:], zero], axis=1),
        jnp.concatenate([zero, centre[:, :-1]], axis=1),
        centre,
    )
    return jnp.where(ok, new, 0.0)


def deep_solve(q, rhs, coef, row_ok):
    rows = q.shape[0]
    for k in range(1, SWEEPS + 1):
        centre = q[1:-1]
        zero = jnp.zeros_like(centre[:, :1])
        new = stencil(
            rhs[k : rows - k],
            coef[k : rows - k],
            q[2:],
            q[:-2],
            jnp.concatenate([centre[:, 1:], zero], axis=1),
            jnp.concatenate([zero, centre[:, :-1]], axis=1),
            centre,
        )
        q = jnp.where(row_ok[k : rows - k], new, 0.0)
    return q


def allsum_axis(v, axis):
    count = lax.axis_size(axis)
    step = 1
    while step < count:
        v = v + lax.ppermute(v, axis, [(i, i ^ step) for i in range(count)])
        step *= 2
    return v


def shell_sum(v, side_count):
    count = lax.axis_size("slab")
    base = (side_count - 1) * count
    step = 1
    while step < count:
        pairs = [(base + i, base + (i ^ step)) for i in range(count)]
        v = v + lax.ppermute(v, ("side", "slab"), pairs)
        step *= 2
    return v


def fluid_sum(v, side_id, sectors):
    count = lax.axis_size("slab")
    got = [v]
    for k in range(1, sectors):
        pairs = [(s * count + j, ((s + k) % sectors) * count + j) for s in range(sectors) for j in range(count)]
        got.append(lax.ppermute(v, ("side", "slab"), pairs))
    total = None
    for t in range(sectors):
        term = got[0]
        for k in range(1, sectors):
            term = jnp.where(side_id == (t + k) % sectors, got[k], term)
        term = jnp.where(side_id == t, got[0], term)
        total = term if total is None else total + term
    return total


def allsum(v):
    return allsum_axis(allsum_axis(v, "slab"), "side")


def body(
    flow_force, flow_coef, flow_init, compliance, shell_load, disp_init, patch_len, owner, block_row
):
    force_here = flow_force[0]
    coef_here = flow_coef[0]
    start_here = flow_init[0]
    slab_rows, planes, line_cells = force_here.shape
    assert slab_rows >= HALO and planes >= BAND
    side_count = lax.axis_size("side")
    side_id = lax.axis_index("side")
    slab_id = lax.axis_index("slab")
    shell_flag = side_id == side_count - 1
    live = (jnp.arange(line_cells)[None, :] < patch_len[:, None]).astype(jnp.float32)
    own = (owner[:, 0] == side_id).astype(jnp.float32)[:, None]
    own_live = own * live
    onehot = (block_row[None, :] == jnp.arange(slab_rows)[:, None]).astype(jnp.float32) * own[:, 0][None, :]
    pick = (block_row[:, None] == jnp.arange(slab_rows)[None, :]).astype(jnp.float32)

    deep_planes = planes - BAND
    disp_zero = own_live * disp_init
    plane_zero = jnp.sum(onehot[:, :, None] * (live * disp_zero)[None], axis=1)
    packed, plane_zero_rims = exchange(
        [
            (jnp.concatenate([start_here[:, :BAND], force_here[:, :BAND], coef_here[:, :BAND]], axis=1), HALO),
            (plane_zero, HALO),
        ]
    )
    after_band = 0.0 * packed[0, 0, 0]
    init_deep, fc_deep = exchange(
        [
            (start_here[:, BAND:] + after_band, 2),
            (jnp.concatenate([force_here[:, BAND:], coef_here[:, BAND:]], axis=1) + after_band, 1),
        ]
    )
    init_band, force_band, coef_band = (
        packed[:, :BAND],
        packed[:, BAND : 2 * BAND],
        packed[:, 2 * BAND :],
    )
    init_deep = jnp.concatenate([init_band[HALO - 2 : HALO + slab_rows + 2], init_deep], axis=1)
    force_deep = jnp.concatenate(
        [force_band[HALO - 1 : HALO + slab_rows + 1], fc_deep[:, :deep_planes]], axis=1
    )
    coef_deep = jnp.concatenate([coef_band[HALO - 1 : HALO + slab_rows + 1], fc_deep[:, deep_planes:]], axis=1)
    global_row = slab_id * slab_rows + jnp.arange(slab_rows + 2 * HALO) - HALO
    total_rows = slab_rows * lax.axis_size("slab")
    row_ok = ((global_row >= 0) & (global_row < total_rows))[:, None, None]

    ok_one = row_ok[HALO - 1 : HALO + slab_rows + 1]
    ok_two = row_ok[HALO : HALO + slab_rows]

    def plane_of(disp):
        return jnp.sum(onehot[:, :, None] * (live * disp)[None], axis=1)

    def evaluate(disp, plane_rims=None, extra=()):
        if plane_rims is None:
            got = exchange([(plane_of(disp), HALO)] + list(extra))
            plane_rims, extra = got[0], got[1:]
        rhs = force_band.at[:, 0, :].add(plane_rims)
        band = band_solve(init_band, rhs, coef_band, row_ok)
        traction = PENALTY * jnp.sum(pick[:, :, None] * band[:, 0, :][None], axis=1)
        loaded = live * (shell_load - traction)
        tilde = own_live * jnp.sum(compliance * loaded[:, None, :], axis=-1)
        return tilde, band, extra

    tilde_zero, unused, unused_extra = evaluate(disp_zero, plane_zero_rims)
    resid_zero = tilde_zero - disp_zero
    disp_one = disp_zero + RELAX * resid_zero
    tilde_one, unused, unused_extra = evaluate(disp_one)
    init_deep, tilde_one = lax.optimization_barrier((init_deep, tilde_one))
    deep = lax.cond(
        shell_flag,
        lambda: jnp.zeros((slab_rows,) + init_deep.shape[1:], jnp.float32),
        lambda: deep_step(
            deep_step(init_deep, force_deep, coef_deep, ok_one), force_deep[1:-1], coef_deep[1:-1], ok_two
        ),
    )
    resid_one = tilde_one - disp_one
    diff_one = resid_one - resid_zero
    sums = fluid_sum(
        allsum_axis(jnp.stack([jnp.sum(diff_one * diff_one), jnp.sum(diff_one * resid_one)]), "slab"),
        side_id,
        side_count - 1,
    )
    step_one = tilde_one - tilde_zero
    rims_base, rims_step, deep = exchange(
        [(plane_of(tilde_one), HALO), (plane_of(step_one), HALO), (deep, 2)]
    )
    band_base = band_solve(init_band, force_band.at[:, 0, :].add(rims_base), coef_band, row_ok)
    band_step = band_solve(
        jnp.zeros_like(init_band), jnp.zeros_like(force_band).at[:, 0, :].set(rims_step), coef_band, row_ok
    )
    both = jnp.stack([band_base[:, 0, :], band_step[:, 0, :]])
    traction = PENALTY * jnp.sum(pick[None, :, :, None] * both[:, None], axis=2)
    loaded = live[None] * (jnp.stack([shell_load, jnp.zeros_like(shell_load)]) - traction)
    applied = own_live[None] * jnp.sum(compliance[None] * loaded[:, :, None, :], axis=-1)
    tilde_base, tilde_step = applied[0], applied[1]
    gram_aa, gram_ab = sums[0], sums[1]
    coeff = -gram_ab / (gram_aa + (0.001 * gram_aa + 1e-06))
    disp_two = tilde_one + coeff * step_one
    tilde_two = tilde_base + coeff * tilde_step
    band_two = band_base + coeff * band_step
    deep = lax.cond(
        shell_flag,
        lambda: jnp.zeros((slab_rows,) + deep.shape[1:], jnp.float32),
        lambda: deep_step(
            deep_step(deep, force_deep, coef_deep, ok_one), force_deep[1:-1], coef_deep[1:-1], ok_two
        ),
    )
    resid_two = tilde_two - disp_two
    newer = resid_two - resid_one
    partial = jnp.stack(
        [
            jnp.sum(newer * newer),
            jnp.sum(newer * diff_one),
            jnp.sum(newer * resid_two),
            jnp.sum(diff_one * resid_two),
        ]
    )
    patches_here = tilde_two.shape[0]
    outgoing = jnp.concatenate(
        [
            jnp.concatenate([tilde_two, tilde_one, tilde_zero, resid_two], axis=0),
            sum(
                jnp.where(jnp.arange(line_cells) == k, partial[k], 0.0) for k in range(4)
            )[None]
            + jnp.where((jnp.arange(line_cells) == 4) & (side_id == 0), gram_aa, 0.0)[None],
        ],
        axis=0,
    )
    gathered = outgoing
    for source in range(side_count - 1):
        gathered = gathered + lax.ppermute(outgoing, "side", [(source, side_count - 1)])
    sums = shell_sum(gathered[4 * patches_here, :4], side_count)
    gram_aa = gathered[4 * patches_here, 4]
    gram_nn, gram_no, proj_new, proj_old = sums[0], sums[1], sums[2], sums[3]
    tilde_two, tilde_one, tilde_zero, resid_two = (
        gathered[k * patches_here : (k + 1) * patches_here] for k in range(4)
    )

    shift_two = 0.001 * (gram_nn + gram_aa) + 1e-06
    diag_new = gram_nn + shift_two
    diag_old = gram_aa + shift_two
    determ = diag_new * diag_old - gram_no * gram_no
    coeff_new = (-proj_new * diag_old + proj_old * gram_no) / determ
    coeff_old = (-proj_old * diag_new + proj_new * gram_no) / determ
    disp_three = (
        tilde_two + coeff_new * (tilde_two - tilde_one) + coeff_old * (tilde_one - tilde_zero)
    )

    flow_state = jnp.concatenate([band_two, deep[:, band_two.shape[1] :]], axis=1)
    disp_next = jnp.where(shell_flag, disp_three, 0.0)[None]
    residual = jnp.where(shell_flag, resid_two, 0.0)[None]
    flow_final = jnp.where(shell_flag, 0.0, flow_state)[None]
    return (disp_next, residual, flow_final)


def solution(mesh):
    return jax.shard_map(
        body,
        mesh=mesh,
        in_specs=(
            P("side", "slab", None, None),
            P("side", "slab", None, None),
            P("side", "slab", None, None),
            P("slab", None, None),
            P("slab", None),
            P("slab", None),
            P("slab"),
            P("slab", None),
            P("slab"),
        ),
        out_specs=(P("side", "slab", None), P("side", "slab", None), P("side", "slab", None, None)),
        check_vma=False,
    )
```

```python
import jax
import jax.numpy as jnp
from jax import lax
from jax.sharding import PartitionSpec as P

SWEEPS = 4
RELAX = 0.5
PENALTY = 3.0
HALO = SWEEPS
BAND = 2 * SWEEPS


def shift_y(a):
    zero = jnp.zeros_like(a[..., :1])
    return (jnp.concatenate([a[..., 1:], zero], axis=-1), jnp.concatenate([zero, a[..., :-1]], axis=-1))


def stencil(rhs, coef, xp, xm, zp, zm, centre):
    yp, ym = shift_y(centre)
    total = ((((xp + xm) + zp) + zm) + yp) + ym
    return (rhs + total) / (6.0 + coef)


def band_solve(q, rhs, coef, row_ok):
    rows, planes = q.shape[0], q.shape[1]
    for k in range(1, SWEEPS + 1):
        centre = q[1:-1, :-1]
        zm = jnp.concatenate([jnp.zeros_like(centre[:, :1]), centre[:, :-1]], axis=1)
        new = stencil(
            rhs[k : rows - k, : planes - k],
            coef[k : rows - k, : planes - k],
            q[2:, :-1],
            q[:-2, :-1],
            q[1:-1, 1:],
            zm,
            centre,
        )
        q = jnp.where(row_ok[k : rows - k], new, 0.0)
    return q


def ring_pairs(count):
    forward = [(i, i + 1) for i in range(count - 1)]
    return forward, [(t, s) for s, t in forward]


def rims(block, width):
    count = lax.axis_size("slab")
    forward, backward = ring_pairs(count)
    low = lax.ppermute(block[block.shape[0] - width :], "slab", forward)
    high = lax.ppermute(block[:width], "slab", backward)
    return jnp.concatenate([low, block, high], axis=0)


def exchange(items):
    count = lax.axis_size("slab")
    forward, backward = ring_pairs(count)
    cells = items[0][0].shape[-1]
    sizes = [width * (a.size // a.shape[0]) // cells for a, width in items]
    up = jnp.concatenate([a[a.shape[0] - w :].reshape(-1, cells) for a, w in items], axis=0)
    down = jnp.concatenate([a[:w].reshape(-1, cells) for a, w in items], axis=0)
    low = lax.ppermute(up, "slab", forward)
    high = lax.ppermute(down, "slab", backward)
    out, at = [], 0
    for (a, w), n in zip(items, sizes):
        shape = (w,) + a.shape[1:]
        out.append(
            jnp.concatenate([low[at : at + n].reshape(shape), a, high[at : at + n].reshape(shape)], axis=0)
        )
        at += n
    return out


def deep_step(q, rhs, coef, ok):
    centre = q[1:-1]
    zero = jnp.zeros_like(centre[:, :1])
    new = stencil(
        rhs,
        coef,
        q[2:],
        q[:-2],
        jnp.concatenate([centre[:, 1:], zero], axis=1),
        jnp.concatenate([zero, centre[:, :-1]], axis=1),
        centre,
    )
    return jnp.where(ok, new, 0.0)


def deep_solve(q, rhs, coef, row_ok):
    rows = q.shape[0]
    for k in range(1, SWEEPS + 1):
        centre = q[1:-1]
        zero = jnp.zeros_like(centre[:, :1])
        new = stencil(
            rhs[k : rows - k],
            coef[k : rows - k],
            q[2:],
            q[:-2],
            jnp.concatenate([centre[:, 1:], zero], axis=1),
            jnp.concatenate([zero, centre[:, :-1]], axis=1),
            centre,
        )
        q = jnp.where(row_ok[k : rows - k], new, 0.0)
    return q


def allsum_axis(v, axis):
    count = lax.axis_size(axis)
    step = 1
    while step < count:
        v = v + lax.ppermute(v, axis, [(i, i ^ step) for i in range(count)])
        step *= 2
    return v


def shell_sum(v, side_count):
    count = lax.axis_size("slab")
    base = (side_count - 1) * count
    step = 1
    while step < count:
        pairs = [(base + i, base + (i ^ step)) for i in range(count)]
        v = v + lax.ppermute(v, ("side", "slab"), pairs)
        step *= 2
    return v


def fluid_sum(v, side_id, sectors):
    count = lax.axis_size("slab")
    got = [v]
    for k in range(1, sectors):
        pairs = [(s * count + j, ((s + k) % sectors) * count + j) for s in range(sectors) for j in range(count)]
        got.append(lax.ppermute(v, ("side", "slab"), pairs))
    total = None
    for t in range(sectors):
        term = got[0]
        for k in range(1, sectors):
            term = jnp.where(side_id == (t + k) % sectors, got[k], term)
        term = jnp.where(side_id == t, got[0], term)
        total = term if total is None else total + term
    return total


def allsum(v):
    return allsum_axis(allsum_axis(v, "slab"), "side")


def body(
    flow_force, flow_coef, flow_init, compliance, shell_load, disp_init, patch_len, owner, block_row
):
    force_here = flow_force[0]
    coef_here = flow_coef[0]
    start_here = flow_init[0]
    slab_rows, planes, line_cells = force_here.shape
    assert slab_rows >= HALO and planes >= BAND
    side_count = lax.axis_size("side")
    side_id = lax.axis_index("side")
    slab_id = lax.axis_index("slab")
    shell_flag = side_id == side_count - 1
    live = (jnp.arange(line_cells)[None, :] < patch_len[:, None]).astype(jnp.float32)
    own = (owner[:, 0] == side_id).astype(jnp.float32)[:, None]
    own_live = own * live
    onehot = (block_row[None, :] == jnp.arange(slab_rows)[:, None]).astype(jnp.float32) * own[:, 0][None, :]
    pick = (block_row[:, None] == jnp.arange(slab_rows)[None, :]).astype(jnp.float32)

    deep_planes = planes - BAND
    disp_zero = own_live * disp_init
    plane_zero = jnp.sum(onehot[:, :, None] * (live * disp_zero)[None], axis=1)
    packed, plane_zero_rims = exchange(
        [
            (jnp.concatenate([start_here[:, :BAND], force_here[:, :BAND], coef_here[:, :BAND]], axis=1), HALO),
            (plane_zero, HALO),
        ]
    )
    after_band = 0.0 * packed[0, 0, 0]
    init_deep, fc_deep = exchange(
        [
            (start_here[:, BAND:] + after_band, 2),
            (jnp.concatenate([force_here[:, BAND:], coef_here[:, BAND:]], axis=1) + after_band, 1),
        ]
    )
    init_band, force_band, coef_band = (
        packed[:, :BAND],
        packed[:, BAND : 2 * BAND],
        packed[:, 2 * BAND :],
    )
    init_deep = jnp.concatenate([init_band[HALO - 2 : HALO + slab_rows + 2], init_deep], axis=1)
    force_deep = jnp.concatenate(
        [force_band[HALO - 1 : HALO + slab_rows + 1], fc_deep[:, :deep_planes]], axis=1
    )
    coef_deep = jnp.concatenate([coef_band[HALO - 1 : HALO + slab_rows + 1], fc_deep[:, deep_planes:]], axis=1)
    global_row = slab_id * slab_rows + jnp.arange(slab_rows + 2 * HALO) - HALO
    total_rows = slab_rows * lax.axis_size("slab")
    row_ok = ((global_row >= 0) & (global_row < total_rows))[:, None, None]

    ok_one = row_ok[HALO - 1 : HALO + slab_rows + 1]
    ok_two = row_ok[HALO : HALO + slab_rows]

    def plane_of(disp):
        return jnp.sum(onehot[:, :, None] * (live * disp)[None], axis=1)

    def evaluate(disp, plane_rims=None, extra=()):
        if plane_rims is None:
            got = exchange([(plane_of(disp), HALO)] + list(extra))
            plane_rims, extra = got[0], got[1:]
        rhs = force_band.at[:, 0, :].add(plane_rims)
        band = band_solve(init_band, rhs, coef_band, row_ok)
        traction = PENALTY * jnp.sum(pick[:, :, None] * band[:, 0, :][None], axis=1)
        loaded = live * (shell_load - traction)
        tilde = own_live * jnp.sum(compliance * loaded[:, None, :], axis=-1)
        return tilde, band, extra

    tilde_zero, unused, unused_extra = evaluate(disp_zero, plane_zero_rims)
    resid_zero = tilde_zero - disp_zero
    disp_one = disp_zero + RELAX * resid_zero
    tilde_one, unused, unused_extra = evaluate(disp_one)
    init_deep, tilde_one = lax.optimization_barrier((init_deep, tilde_one))
    deep = lax.cond(
        shell_flag,
        lambda: jnp.zeros((slab_rows,) + init_deep.shape[1:], jnp.float32),
        lambda: deep_step(
            deep_step(init_deep, force_deep, coef_deep, ok_one), force_deep[1:-1], coef_deep[1:-1], ok_two
        ),
    )
    resid_one = tilde_one - disp_one
    diff_one = resid_one - resid_zero
    sums = fluid_sum(
        allsum_axis(jnp.stack([jnp.sum(diff_one * diff_one), jnp.sum(diff_one * resid_one)]), "slab"),
        side_id,
        side_count - 1,
    )
    step_one = tilde_one - tilde_zero
    rims_base, rims_step, deep = exchange(
        [(plane_of(tilde_one), HALO), (plane_of(step_one), HALO), (deep, 2)]
    )
    band_base = band_solve(init_band, force_band.at[:, 0, :].add(rims_base), coef_band, row_ok)
    band_step = band_solve(
        jnp.zeros_like(init_band), jnp.zeros_like(force_band).at[:, 0, :].set(rims_step), coef_band, row_ok
    )
    both = jnp.stack([band_base[:, 0, :], band_step[:, 0, :]])
    traction = PENALTY * jnp.sum(pick[None, :, :, None] * both[:, None], axis=2)
    loaded = live[None] * (jnp.stack([shell_load, jnp.zeros_like(shell_load)]) - traction)
    applied = own_live[None] * jnp.sum(compliance[None] * loaded[:, :, None, :], axis=-1)
    tilde_base, tilde_step = applied[0], applied[1]
    gram_aa, gram_ab = sums[0], sums[1]
    coeff = -gram_ab / (gram_aa + (0.001 * gram_aa + 1e-06))
    disp_two = tilde_one + coeff * step_one
    tilde_two = tilde_base + coeff * tilde_step
    band_two = band_base + coeff * band_step
    deep = lax.cond(
        shell_flag,
        lambda: jnp.zeros((slab_rows,) + deep.shape[1:], jnp.float32),
        lambda: deep_step(
            deep_step(deep, force_deep, coef_deep, ok_one), force_deep[1:-1], coef_deep[1:-1], ok_two
        ),
    )
    resid_two = tilde_two - disp_two
    newer = resid_two - resid_one
    partial = jnp.stack(
        [
            jnp.sum(newer * newer, axis=0),
            jnp.sum(newer * diff_one, axis=0),
            jnp.sum(newer * resid_two, axis=0),
            jnp.sum(diff_one * resid_two, axis=0),
        ]
    )
    patches_here = tilde_two.shape[0]
    outgoing = jnp.concatenate(
        [
            tilde_two,
            tilde_one,
            tilde_zero,
            resid_two,
            partial,
            jnp.where((jnp.arange(line_cells) == 0) & (side_id == 0), gram_aa, 0.0)[None],
        ],
        axis=0,
    )
    gathered = outgoing
    for source in range(side_count - 1):
        gathered = gathered + lax.ppermute(outgoing, "side", [(source, side_count - 1)])
    sums = shell_sum(jnp.sum(gathered[4 * patches_here : 4 * patches_here + 4], axis=1), side_count)
    gram_aa = gathered[4 * patches_here + 4, 0]
    gram_nn, gram_no, proj_new, proj_old = sums[0], sums[1], sums[2], sums[3]
    tilde_two, tilde_one, tilde_zero, resid_two = (
        gathered[k * patches_here : (k + 1) * patches_here] for k in range(4)
    )

    shift_two = 0.001 * (gram_nn + gram_aa) + 1e-06
    diag_new = gram_nn + shift_two
    diag_old = gram_aa + shift_two
    determ = diag_new * diag_old - gram_no * gram_no
    coeff_new = (-proj_new * diag_old + proj_old * gram_no) / determ
    coeff_old = (-proj_old * diag_new + proj_new * gram_no) / determ
    disp_three = (
        tilde_two + coeff_new * (tilde_two - tilde_one) + coeff_old * (tilde_one - tilde_zero)
    )

    flow_state = jnp.concatenate([band_two, deep[:, band_two.shape[1] :]], axis=1)
    disp_next = jnp.where(shell_flag, disp_three, 0.0)[None]
    residual = jnp.where(shell_flag, resid_two, 0.0)[None]
    flow_final = jnp.where(shell_flag, 0.0, flow_state)[None]
    return (disp_next, residual, flow_final)


def solution(mesh):
    return jax.shard_map(
        body,
        mesh=mesh,
        in_specs=(
            P("side", "slab", None, None),
            P("side", "slab", None, None),
            P("side", "slab", None, None),
            P("slab", None, None),
            P("slab", None),
            P("slab", None),
            P("slab"),
            P("slab", None),
            P("slab"),
        ),
        out_specs=(P("side", "slab", None), P("side", "slab", None), P("side", "slab", None, None)),
        check_vma=False,
    )
```

```python
import jax
import jax.numpy as jnp
from jax import lax
from jax.sharding import PartitionSpec as P

SWEEPS = 4
RELAX = 0.5
PENALTY = 3.0
HALO = SWEEPS
BAND = 2 * SWEEPS


def shift_y(a):
    zero = jnp.zeros_like(a[..., :1])
    return (jnp.concatenate([a[..., 1:], zero], axis=-1), jnp.concatenate([zero, a[..., :-1]], axis=-1))


def stencil(rhs, coef, xp, xm, zp, zm, centre):
    yp, ym = shift_y(centre)
    total = ((((xp + xm) + zp) + zm) + yp) + ym
    return (rhs + total) / (6.0 + coef)


def band_solve(q, rhs, coef, row_ok):
    rows, planes = q.shape[0], q.shape[1]
    for k in range(1, SWEEPS + 1):
        centre = q[1:-1, :-1]
        zm = jnp.concatenate([jnp.zeros_like(centre[:, :1]), centre[:, :-1]], axis=1)
        new = stencil(
            rhs[k : rows - k, : planes - k],
            coef[k : rows - k, : planes - k],
            q[2:, :-1],
            q[:-2, :-1],
            q[1:-1, 1:],
            zm,
            centre,
        )
        q = jnp.where(row_ok[k : rows - k], new, 0.0)
    return q


def ring_pairs(count):
    forward = [(i, i + 1) for i in range(count - 1)]
    return forward, [(t, s) for s, t in forward]


def rims(block, width):
    count = lax.axis_size("slab")
    forward, backward = ring_pairs(count)
    low = lax.ppermute(block[block.shape[0] - width :], "slab", forward)
    high = lax.ppermute(block[:width], "slab", backward)
    return jnp.concatenate([low, block, high], axis=0)


def exchange(items):
    count = lax.axis_size("slab")
    forward, backward = ring_pairs(count)
    cells = items[0][0].shape[-1]
    sizes = [width * (a.size // a.shape[0]) // cells for a, width in items]
    up = jnp.concatenate([a[a.shape[0] - w :].reshape(-1, cells) for a, w in items], axis=0)
    down = jnp.concatenate([a[:w].reshape(-1, cells) for a, w in items], axis=0)
    low = lax.ppermute(up, "slab", forward)
    high = lax.ppermute(down, "slab", backward)
    out, at = [], 0
    for (a, w), n in zip(items, sizes):
        shape = (w,) + a.shape[1:]
        out.append(
            jnp.concatenate([low[at : at + n].reshape(shape), a, high[at : at + n].reshape(shape)], axis=0)
        )
        at += n
    return out


def deep_step(q, rhs, coef, ok):
    centre = q[1:-1]
    zero = jnp.zeros_like(centre[:, :1])
    new = stencil(
        rhs,
        coef,
        q[2:],
        q[:-2],
        jnp.concatenate([centre[:, 1:], zero], axis=1),
        jnp.concatenate([zero, centre[:, :-1]], axis=1),
        centre,
    )
    return jnp.where(ok, new, 0.0)


def deep_solve(q, rhs, coef, row_ok):
    rows = q.shape[0]
    for k in range(1, SWEEPS + 1):
        centre = q[1:-1]
        zero = jnp.zeros_like(centre[:, :1])
        new = stencil(
            rhs[k : rows - k],
            coef[k : rows - k],
            q[2:],
            q[:-2],
            jnp.concatenate([centre[:, 1:], zero], axis=1),
            jnp.concatenate([zero, centre[:, :-1]], axis=1),
            centre,
        )
        q = jnp.where(row_ok[k : rows - k], new, 0.0)
    return q


def allsum_axis(v, axis):
    count = lax.axis_size(axis)
    step = 1
    while step < count:
        v = v + lax.ppermute(v, axis, [(i, i ^ step) for i in range(count)])
        step *= 2
    return v


def shell_sum(v, side_count):
    count = lax.axis_size("slab")
    base = (side_count - 1) * count
    step = 1
    while step < count:
        pairs = [(base + i, base + (i ^ step)) for i in range(count)]
        v = v + lax.ppermute(v, ("side", "slab"), pairs)
        step *= 2
    return v


def fluid_sum(v, side_id, sectors):
    count = lax.axis_size("slab")
    got = [v]
    for k in range(1, sectors):
        pairs = [(s * count + j, ((s + k) % sectors) * count + j) for s in range(sectors) for j in range(count)]
        got.append(lax.ppermute(v, ("side", "slab"), pairs))
    total = None
    for t in range(sectors):
        term = got[0]
        for k in range(1, sectors):
            term = jnp.where(side_id == (t + k) % sectors, got[k], term)
        term = jnp.where(side_id == t, got[0], term)
        total = term if total is None else total + term
    return total


def allsum(v):
    return allsum_axis(allsum_axis(v, "slab"), "side")


def body(
    flow_force, flow_coef, flow_init, compliance, shell_load, disp_init, patch_len, owner, block_row
):
    force_here = flow_force[0]
    coef_here = flow_coef[0]
    start_here = flow_init[0]
    slab_rows, planes, line_cells = force_here.shape
    assert slab_rows >= HALO and planes >= BAND
    side_count = lax.axis_size("side")
    side_id = lax.axis_index("side")
    slab_id = lax.axis_index("slab")
    shell_flag = side_id == side_count - 1
    live = (jnp.arange(line_cells)[None, :] < patch_len[:, None]).astype(jnp.float32)
    own = (owner[:, 0] == side_id).astype(jnp.float32)[:, None]
    own_live = own * live
    onehot = (block_row[None, :] == jnp.arange(slab_rows)[:, None]).astype(jnp.float32) * own[:, 0][None, :]
    pick = (block_row[:, None] == jnp.arange(slab_rows)[None, :]).astype(jnp.float32)

    deep_planes = planes - BAND
    disp_zero = own_live * disp_init
    plane_zero = jnp.sum(onehot[:, :, None] * (live * disp_zero)[None], axis=1)
    packed, plane_zero_rims = exchange(
        [
            (jnp.concatenate([start_here[:, :BAND], force_here[:, :BAND], coef_here[:, :BAND]], axis=1), HALO),
            (plane_zero, HALO),
        ]
    )
    after_band = 0.0 * packed[0, 0, 0]
    init_deep, fc_deep = exchange(
        [
            (start_here[:, BAND:] + after_band, 2),
            (jnp.concatenate([force_here[:, BAND:], coef_here[:, BAND:]], axis=1) + after_band, 1),
        ]
    )
    init_band, force_band, coef_band = (
        packed[:, :BAND],
        packed[:, BAND : 2 * BAND],
        packed[:, 2 * BAND :],
    )
    init_deep = jnp.concatenate([init_band[HALO - 2 : HALO + slab_rows + 2], init_deep], axis=1)
    force_deep = jnp.concatenate(
        [force_band[HALO - 1 : HALO + slab_rows + 1], fc_deep[:, :deep_planes]], axis=1
    )
    coef_deep = jnp.concatenate([coef_band[HALO - 1 : HALO + slab_rows + 1], fc_deep[:, deep_planes:]], axis=1)
    global_row = slab_id * slab_rows + jnp.arange(slab_rows + 2 * HALO) - HALO
    total_rows = slab_rows * lax.axis_size("slab")
    row_ok = ((global_row >= 0) & (global_row < total_rows))[:, None, None]

    ok_one = row_ok[HALO - 1 : HALO + slab_rows + 1]
    ok_two = row_ok[HALO : HALO + slab_rows]

    def plane_of(disp):
        return jnp.sum(onehot[:, :, None] * (live * disp)[None], axis=1)

    def evaluate(disp, plane_rims=None, extra=()):
        if plane_rims is None:
            got = exchange([(plane_of(disp), HALO)] + list(extra))
            plane_rims, extra = got[0], got[1:]
        rhs = force_band.at[:, 0, :].add(plane_rims)
        band = band_solve(init_band, rhs, coef_band, row_ok)
        traction = PENALTY * jnp.sum(pick[:, :, None] * band[:, 0, :][None], axis=1)
        loaded = live * (shell_load - traction)
        tilde = own_live * jnp.sum(compliance * loaded[:, None, :], axis=-1)
        return tilde, band, extra

    tilde_zero, unused, unused_extra = evaluate(disp_zero, plane_zero_rims)
    resid_zero = tilde_zero - disp_zero
    disp_one = disp_zero + RELAX * resid_zero
    tilde_one, unused, unused_extra = evaluate(disp_one)
    init_deep, tilde_one = lax.optimization_barrier((init_deep, tilde_one))
    deep = lax.cond(
        shell_flag,
        lambda: jnp.zeros((slab_rows,) + init_deep.shape[1:], jnp.float32),
        lambda: deep_step(
            deep_step(init_deep, force_deep, coef_deep, ok_one), force_deep[1:-1], coef_deep[1:-1], ok_two
        ),
    )
    resid_one = tilde_one - disp_one
    diff_one = resid_one - resid_zero
    sums = fluid_sum(
        allsum_axis(jnp.stack([jnp.sum(diff_one * diff_one), jnp.sum(diff_one * resid_one)]), "slab"),
        side_id,
        side_count - 1,
    )
    step_one = tilde_one - tilde_zero
    rims_base, rims_step = exchange([(plane_of(tilde_one), HALO), (plane_of(step_one), HALO)])
    band_base = band_solve(init_band, force_band.at[:, 0, :].add(rims_base), coef_band, row_ok)
    band_step = band_solve(
        jnp.zeros_like(init_band), jnp.zeros_like(force_band).at[:, 0, :].set(rims_step), coef_band, row_ok
    )
    both = jnp.stack([band_base[:, 0, :], band_step[:, 0, :]])
    traction = PENALTY * jnp.sum(pick[None, :, :, None] * both[:, None], axis=2)
    loaded = live[None] * (jnp.stack([shell_load, jnp.zeros_like(shell_load)]) - traction)
    applied = own_live[None] * jnp.sum(compliance[None] * loaded[:, :, None, :], axis=-1)
    tilde_base, tilde_step = applied[0], applied[1]
    gram_aa, gram_ab = sums[0], sums[1]
    coeff = -gram_ab / (gram_aa + (0.001 * gram_aa + 1e-06))
    disp_two = tilde_one + coeff * step_one
    tilde_two = tilde_base + coeff * tilde_step
    band_two = band_base + coeff * band_step
    resid_two = tilde_two - disp_two
    newer = resid_two - resid_one
    partial = jnp.stack(
        [
            jnp.sum(newer * newer, axis=0),
            jnp.sum(newer * diff_one, axis=0),
            jnp.sum(newer * resid_two, axis=0),
            jnp.sum(diff_one * resid_two, axis=0),
        ]
    )
    patches_here = tilde_two.shape[0]
    outgoing = jnp.concatenate(
        [
            tilde_two,
            tilde_one,
            tilde_zero,
            resid_two,
            partial,
            jnp.where((jnp.arange(line_cells) == 0) & (side_id == 0), gram_aa, 0.0)[None],
        ],
        axis=0,
    )
    (deep,) = exchange([(deep + 0.0 * outgoing[0, 0], 2)])
    deep = lax.cond(
        shell_flag,
        lambda: jnp.zeros((slab_rows,) + deep.shape[1:], jnp.float32),
        lambda: deep_step(
            deep_step(deep, force_deep, coef_deep, ok_one), force_deep[1:-1], coef_deep[1:-1], ok_two
        ),
    )
    gathered = outgoing
    for source in range(side_count - 1):
        gathered = gathered + lax.ppermute(outgoing, "side", [(source, side_count - 1)])
    sums = shell_sum(jnp.sum(gathered[4 * patches_here : 4 * patches_here + 4], axis=1), side_count)
    gram_aa = gathered[4 * patches_here + 4, 0]
    gram_nn, gram_no, proj_new, proj_old = sums[0], sums[1], sums[2], sums[3]
    tilde_two, tilde_one, tilde_zero, resid_two = (
        gathered[k * patches_here : (k + 1) * patches_here] for k in range(4)
    )

    shift_two = 0.001 * (gram_nn + gram_aa) + 1e-06
    diag_new = gram_nn + shift_two
    diag_old = gram_aa + shift_two
    determ = diag_new * diag_old - gram_no * gram_no
    coeff_new = (-proj_new * diag_old + proj_old * gram_no) / determ
    coeff_old = (-proj_old * diag_new + proj_new * gram_no) / determ
    disp_three = (
        tilde_two + coeff_new * (tilde_two - tilde_one) + coeff_old * (tilde_one - tilde_zero)
    )

    flow_state = jnp.concatenate([band_two, deep[:, band_two.shape[1] :]], axis=1)
    disp_next = jnp.where(shell_flag, disp_three, 0.0)[None]
    residual = jnp.where(shell_flag, resid_two, 0.0)[None]
    flow_final = jnp.where(shell_flag, 0.0, flow_state)[None]
    return (disp_next, residual, flow_final)


def solution(mesh):
    return jax.shard_map(
        body,
        mesh=mesh,
        in_specs=(
            P("side", "slab", None, None),
            P("side", "slab", None, None),
            P("side", "slab", None, None),
            P("slab", None, None),
            P("slab", None),
            P("slab", None),
            P("slab"),
            P("slab", None),
            P("slab"),
        ),
        out_specs=(P("side", "slab", None), P("side", "slab", None), P("side", "slab", None, None)),
        check_vma=False,
    )
```

```python
import jax
import jax.numpy as jnp
from jax import lax
from jax.sharding import PartitionSpec as P

SWEEPS = 4
RELAX = 0.5
PENALTY = 3.0
HALO = SWEEPS
BAND = 2 * SWEEPS


def shift_y(a):
    zero = jnp.zeros_like(a[..., :1])
    return (jnp.concatenate([a[..., 1:], zero], axis=-1), jnp.concatenate([zero, a[..., :-1]], axis=-1))


def stencil(rhs, coef, xp, xm, zp, zm, centre):
    yp, ym = shift_y(centre)
    total = ((((xp + xm) + zp) + zm) + yp) + ym
    return (rhs + total) / (6.0 + coef)


def band_solve(q, rhs, coef, row_ok):
    rows, planes = q.shape[0], q.shape[1]
    for k in range(1, SWEEPS + 1):
        centre = q[1:-1, :-1]
        zm = jnp.concatenate([jnp.zeros_like(centre[:, :1]), centre[:, :-1]], axis=1)
        new = stencil(
            rhs[k : rows - k, : planes - k],
            coef[k : rows - k, : planes - k],
            q[2:, :-1],
            q[:-2, :-1],
            q[1:-1, 1:],
            zm,
            centre,
        )
        q = jnp.where(row_ok[k : rows - k], new, 0.0)
    return q


def ring_pairs(count):
    forward = [(i, i + 1) for i in range(count - 1)]
    return forward, [(t, s) for s, t in forward]


def rims(block, width):
    count = lax.axis_size("slab")
    forward, backward = ring_pairs(count)
    low = lax.ppermute(block[block.shape[0] - width :], "slab", forward)
    high = lax.ppermute(block[:width], "slab", backward)
    return jnp.concatenate([low, block, high], axis=0)


def exchange(items):
    count = lax.axis_size("slab")
    forward, backward = ring_pairs(count)
    cells = items[0][0].shape[-1]
    sizes = [width * (a.size // a.shape[0]) // cells for a, width in items]
    up = jnp.concatenate([a[a.shape[0] - w :].reshape(-1, cells) for a, w in items], axis=0)
    down = jnp.concatenate([a[:w].reshape(-1, cells) for a, w in items], axis=0)
    low = lax.ppermute(up, "slab", forward)
    high = lax.ppermute(down, "slab", backward)
    out, at = [], 0
    for (a, w), n in zip(items, sizes):
        shape = (w,) + a.shape[1:]
        out.append(
            jnp.concatenate([low[at : at + n].reshape(shape), a, high[at : at + n].reshape(shape)], axis=0)
        )
        at += n
    return out


def deep_step(q, rhs, coef, ok):
    centre = q[1:-1]
    zero = jnp.zeros_like(centre[:, :1])
    new = stencil(
        rhs,
        coef,
        q[2:],
        q[:-2],
        jnp.concatenate([centre[:, 1:], zero], axis=1),
        jnp.concatenate([zero, centre[:, :-1]], axis=1),
        centre,
    )
    return jnp.where(ok, new, 0.0)


def deep_solve(q, rhs, coef, row_ok):
    rows = q.shape[0]
    for k in range(1, SWEEPS + 1):
        centre = q[1:-1]
        zero = jnp.zeros_like(centre[:, :1])
        new = stencil(
            rhs[k : rows - k],
            coef[k : rows - k],
            q[2:],
            q[:-2],
            jnp.concatenate([centre[:, 1:], zero], axis=1),
            jnp.concatenate([zero, centre[:, :-1]], axis=1),
            centre,
        )
        q = jnp.where(row_ok[k : rows - k], new, 0.0)
    return q


def allsum_axis(v, axis):
    count = lax.axis_size(axis)
    step = 1
    while step < count:
        v = v + lax.ppermute(v, axis, [(i, i ^ step) for i in range(count)])
        step *= 2
    return v


def shell_sum(v, side_count):
    count = lax.axis_size("slab")
    base = (side_count - 1) * count
    step = 1
    while step < count:
        pairs = [(base + i, base + (i ^ step)) for i in range(count)]
        v = v + lax.ppermute(v, ("side", "slab"), pairs)
        step *= 2
    return v


def fluid_sum(v, side_id, sectors):
    count = lax.axis_size("slab")
    got = [v]
    for k in range(1, sectors):
        pairs = [(s * count + j, ((s + k) % sectors) * count + j) for s in range(sectors) for j in range(count)]
        got.append(lax.ppermute(v, ("side", "slab"), pairs))
    total = None
    for t in range(sectors):
        term = got[0]
        for k in range(1, sectors):
            term = jnp.where(side_id == (t + k) % sectors, got[k], term)
        term = jnp.where(side_id == t, got[0], term)
        total = term if total is None else total + term
    return total


def allsum(v):
    return allsum_axis(allsum_axis(v, "slab"), "side")


def body(
    flow_force, flow_coef, flow_init, compliance, shell_load, disp_init, patch_len, owner, block_row
):
    force_here = flow_force[0]
    coef_here = flow_coef[0]
    start_here = flow_init[0]
    slab_rows, planes, line_cells = force_here.shape
    assert slab_rows >= HALO and planes >= BAND
    side_count = lax.axis_size("side")
    side_id = lax.axis_index("side")
    slab_id = lax.axis_index("slab")
    shell_flag = side_id == side_count - 1
    live = (jnp.arange(line_cells)[None, :] < patch_len[:, None]).astype(jnp.float32)
    own = (owner[:, 0] == side_id).astype(jnp.float32)[:, None]
    own_live = own * live
    onehot = (block_row[None, :] == jnp.arange(slab_rows)[:, None]).astype(jnp.float32) * own[:, 0][None, :]
    pick = (block_row[:, None] == jnp.arange(slab_rows)[None, :]).astype(jnp.float32)

    deep_planes = planes - BAND
    disp_zero = own_live * disp_init
    plane_zero = jnp.sum(onehot[:, :, None] * (live * disp_zero)[None], axis=1)
    packed, plane_zero_rims = exchange(
        [
            (jnp.concatenate([start_here[:, :BAND], force_here[:, :BAND], coef_here[:, :BAND]], axis=1), HALO),
            (plane_zero, HALO),
        ]
    )
    after_band = 0.0 * packed[0, 0, 0]
    init_deep, fc_deep = exchange(
        [
            (start_here[:, BAND:] + after_band, 2),
            (jnp.concatenate([force_here[:, BAND:], coef_here[:, BAND:]], axis=1) + after_band, 1),
        ]
    )
    init_band, force_band, coef_band = (
        packed[:, :BAND],
        packed[:, BAND : 2 * BAND],
        packed[:, 2 * BAND :],
    )
    init_deep = jnp.concatenate([init_band[HALO - 2 : HALO + slab_rows + 2], init_deep], axis=1)
    force_deep = jnp.concatenate(
        [force_band[HALO - 1 : HALO + slab_rows + 1], fc_deep[:, :deep_planes]], axis=1
    )
    coef_deep = jnp.concatenate([coef_band[HALO - 1 : HALO + slab_rows + 1], fc_deep[:, deep_planes:]], axis=1)
    global_row = slab_id * slab_rows + jnp.arange(slab_rows + 2 * HALO) - HALO
    total_rows = slab_rows * lax.axis_size("slab")
    row_ok = ((global_row >= 0) & (global_row < total_rows))[:, None, None]

    ok_one = row_ok[HALO - 1 : HALO + slab_rows + 1]
    ok_two = row_ok[HALO : HALO + slab_rows]

    def plane_of(disp):
        return jnp.sum(onehot[:, :, None] * (live * disp)[None], axis=1)

    def evaluate(disp, plane_rims=None, extra=()):
        if plane_rims is None:
            got = exchange([(plane_of(disp), HALO)] + list(extra))
            plane_rims, extra = got[0], got[1:]
        rhs = force_band.at[:, 0, :].add(plane_rims)
        band = band_solve(init_band, rhs, coef_band, row_ok)
        traction = PENALTY * jnp.sum(pick[:, :, None] * band[:, 0, :][None], axis=1)
        loaded = live * (shell_load - traction)
        tilde = own_live * jnp.sum(compliance * loaded[:, None, :], axis=-1)
        return tilde, band, extra

    tilde_zero, unused, unused_extra = evaluate(disp_zero, plane_zero_rims)
    resid_zero = tilde_zero - disp_zero
    disp_one = disp_zero + RELAX * resid_zero
    tilde_one, unused, unused_extra = evaluate(disp_one)
    init_deep, tilde_one = lax.optimization_barrier((init_deep, tilde_one))

    def face_rows():
        r = slab_rows
        low = deep_step(init_deep[0:6], force_deep[0:4], coef_deep[0:4], ok_one[0:4])
        low = deep_step(low, force_deep[1:3], coef_deep[1:3], ok_two[0:2])
        high = deep_step(init_deep[r - 2 : r + 4], force_deep[r - 2 : r + 2], coef_deep[r - 2 : r + 2], ok_one[r - 2 : r + 2])
        high = deep_step(high, force_deep[r - 1 : r + 1], coef_deep[r - 1 : r + 1], ok_two[r - 2 : r])
        return jnp.concatenate([low, high], axis=0)

    faces = lax.cond(
        shell_flag, lambda: jnp.zeros((4,) + init_deep.shape[1:], jnp.float32), face_rows
    )
    resid_one = tilde_one - disp_one
    diff_one = resid_one - resid_zero
    sums = fluid_sum(
        allsum_axis(jnp.stack([jnp.sum(diff_one * diff_one), jnp.sum(diff_one * resid_one)]), "slab"),
        side_id,
        side_count - 1,
    )
    step_one = tilde_one - tilde_zero
    rims_base, rims_step, faces = exchange(
        [(plane_of(tilde_one), HALO), (plane_of(step_one), HALO), (faces, 2)]
    )
    band_base = band_solve(init_band, force_band.at[:, 0, :].add(rims_base), coef_band, row_ok)
    band_step = band_solve(
        jnp.zeros_like(init_band), jnp.zeros_like(force_band).at[:, 0, :].set(rims_step), coef_band, row_ok
    )
    both = jnp.stack([band_base[:, 0, :], band_step[:, 0, :]])
    traction = PENALTY * jnp.sum(pick[None, :, :, None] * both[:, None], axis=2)
    loaded = live[None] * (jnp.stack([shell_load, jnp.zeros_like(shell_load)]) - traction)
    applied = own_live[None] * jnp.sum(compliance[None] * loaded[:, :, None, :], axis=-1)
    tilde_base, tilde_step = applied[0], applied[1]
    gram_aa, gram_ab = sums[0], sums[1]
    coeff = -gram_ab / (gram_aa + (0.001 * gram_aa + 1e-06))
    disp_two = tilde_one + coeff * step_one
    tilde_two = tilde_base + coeff * tilde_step
    band_two = band_base + coeff * band_step
    resid_two = tilde_two - disp_two
    newer = resid_two - resid_one
    partial = jnp.stack(
        [
            jnp.sum(newer * newer, axis=0),
            jnp.sum(newer * diff_one, axis=0),
            jnp.sum(newer * resid_two, axis=0),
            jnp.sum(diff_one * resid_two, axis=0),
        ]
    )
    patches_here = tilde_two.shape[0]
    outgoing = jnp.concatenate(
        [
            tilde_two,
            tilde_one,
            tilde_zero,
            resid_two,
            partial,
            jnp.where((jnp.arange(line_cells) == 0) & (side_id == 0), gram_aa, 0.0)[None],
        ],
        axis=0,
    )
    late_init = init_deep + 0.0 * outgoing[0, 0]

    def deep_rest():
        q = deep_step(
            deep_step(late_init, force_deep, coef_deep, ok_one), force_deep[1:-1], coef_deep[1:-1], ok_two
        )
        q = jnp.concatenate([faces[:2], q, faces[-2:]], axis=0)
        return deep_step(
            deep_step(q, force_deep, coef_deep, ok_one), force_deep[1:-1], coef_deep[1:-1], ok_two
        )

    deep = lax.cond(
        shell_flag, lambda: jnp.zeros((slab_rows,) + init_deep.shape[1:], jnp.float32), deep_rest
    )
    gathered = outgoing
    for source in range(side_count - 1):
        gathered = gathered + lax.ppermute(outgoing, "side", [(source, side_count - 1)])
    sums = shell_sum(jnp.sum(gathered[4 * patches_here : 4 * patches_here + 4], axis=1), side_count)
    gram_aa = gathered[4 * patches_here + 4, 0]
    gram_nn, gram_no, proj_new, proj_old = sums[0], sums[1], sums[2], sums[3]
    tilde_two, tilde_one, tilde_zero, resid_two = (
        gathered[k * patches_here : (k + 1) * patches_here] for k in range(4)
    )

    shift_two = 0.001 * (gram_nn + gram_aa) + 1e-06
    diag_new = gram_nn + shift_two
    diag_old = gram_aa + shift_two
    determ = diag_new * diag_old - gram_no * gram_no
    coeff_new = (-proj_new * diag_old + proj_old * gram_no) / determ
    coeff_old = (-proj_old * diag_new + proj_new * gram_no) / determ
    disp_three = (
        tilde_two + coeff_new * (tilde_two - tilde_one) + coeff_old * (tilde_one - tilde_zero)
    )

    flow_state = jnp.concatenate([band_two, deep[:, band_two.shape[1] :]], axis=1)
    disp_next = jnp.where(shell_flag, disp_three, 0.0)[None]
    residual = jnp.where(shell_flag, resid_two, 0.0)[None]
    flow_final = jnp.where(shell_flag, 0.0, flow_state)[None]
    return (disp_next, residual, flow_final)


def solution(mesh):
    return jax.shard_map(
        body,
        mesh=mesh,
        in_specs=(
            P("side", "slab", None, None),
            P("side", "slab", None, None),
            P("side", "slab", None, None),
            P("slab", None, None),
            P("slab", None),
            P("slab", None),
            P("slab"),
            P("slab", None),
            P("slab"),
        ),
        out_specs=(P("side", "slab", None), P("side", "slab", None), P("side", "slab", None, None)),
        check_vma=False,
    )
```

```python
import jax
import jax.numpy as jnp
from jax import lax
from jax.sharding import PartitionSpec as P

SWEEPS = 4
RELAX = 0.5
PENALTY = 3.0
HALO = SWEEPS
BAND = 2 * SWEEPS


def shift_y(a):
    zero = jnp.zeros_like(a[..., :1])
    return (jnp.concatenate([a[..., 1:], zero], axis=-1), jnp.concatenate([zero, a[..., :-1]], axis=-1))


def stencil(rhs, coef, xp, xm, zp, zm, centre):
    yp, ym = shift_y(centre)
    total = ((((xp + xm) + zp) + zm) + yp) + ym
    return (rhs + total) / (6.0 + coef)


def band_solve(q, rhs, coef, row_ok):
    rows, planes = q.shape[0], q.shape[1]
    for k in range(1, SWEEPS + 1):
        centre = q[1:-1, :-1]
        zm = jnp.concatenate([jnp.zeros_like(centre[:, :1]), centre[:, :-1]], axis=1)
        new = stencil(
            rhs[k : rows - k, : planes - k],
            coef[k : rows - k, : planes - k],
            q[2:, :-1],
            q[:-2, :-1],
            q[1:-1, 1:],
            zm,
            centre,
        )
        q = jnp.where(row_ok[k : rows - k], new, 0.0)
    return q


def ring_pairs(count):
    forward = [(i, i + 1) for i in range(count - 1)]
    return forward, [(t, s) for s, t in forward]


def rims(block, width):
    count = lax.axis_size("slab")
    forward, backward = ring_pairs(count)
    low = lax.ppermute(block[block.shape[0] - width :], "slab", forward)
    high = lax.ppermute(block[:width], "slab", backward)
    return jnp.concatenate([low, block, high], axis=0)


def exchange(items):
    count = lax.axis_size("slab")
    forward, backward = ring_pairs(count)
    cells = items[0][0].shape[-1]
    sizes = [width * (a.size // a.shape[0]) // cells for a, width in items]
    up = jnp.concatenate([a[a.shape[0] - w :].reshape(-1, cells) for a, w in items], axis=0)
    down = jnp.concatenate([a[:w].reshape(-1, cells) for a, w in items], axis=0)
    low = lax.ppermute(up, "slab", forward)
    high = lax.ppermute(down, "slab", backward)
    out, at = [], 0
    for (a, w), n in zip(items, sizes):
        shape = (w,) + a.shape[1:]
        out.append(
            jnp.concatenate([low[at : at + n].reshape(shape), a, high[at : at + n].reshape(shape)], axis=0)
        )
        at += n
    return out


def deep_step(q, rhs, coef, ok):
    centre = q[1:-1]
    zero = jnp.zeros_like(centre[:, :1])
    new = stencil(
        rhs,
        coef,
        q[2:],
        q[:-2],
        jnp.concatenate([centre[:, 1:], zero], axis=1),
        jnp.concatenate([zero, centre[:, :-1]], axis=1),
        centre,
    )
    return jnp.where(ok, new, 0.0)


def deep_solve(q, rhs, coef, row_ok):
    rows = q.shape[0]
    for k in range(1, SWEEPS + 1):
        centre = q[1:-1]
        zero = jnp.zeros_like(centre[:, :1])
        new = stencil(
            rhs[k : rows - k],
            coef[k : rows - k],
            q[2:],
            q[:-2],
            jnp.concatenate([centre[:, 1:], zero], axis=1),
            jnp.concatenate([zero, centre[:, :-1]], axis=1),
            centre,
        )
        q = jnp.where(row_ok[k : rows - k], new, 0.0)
    return q


def allsum_axis(v, axis):
    count = lax.axis_size(axis)
    step = 1
    while step < count:
        v = v + lax.ppermute(v, axis, [(i, i ^ step) for i in range(count)])
        step *= 2
    return v


def shell_sum(v, side_count):
    count = lax.axis_size("slab")
    base = (side_count - 1) * count
    step = 1
    while step < count:
        pairs = [(base + i, base + (i ^ step)) for i in range(count)]
        v = v + lax.ppermute(v, ("side", "slab"), pairs)
        step *= 2
    return v


def fluid_sum(v, side_id, sectors):
    count = lax.axis_size("slab")
    got = [v]
    for k in range(1, sectors):
        pairs = [(s * count + j, ((s + k) % sectors) * count + j) for s in range(sectors) for j in range(count)]
        got.append(lax.ppermute(v, ("side", "slab"), pairs))
    total = None
    for t in range(sectors):
        term = got[0]
        for k in range(1, sectors):
            term = jnp.where(side_id == (t + k) % sectors, got[k], term)
        term = jnp.where(side_id == t, got[0], term)
        total = term if total is None else total + term
    return total


def allsum(v):
    return allsum_axis(allsum_axis(v, "slab"), "side")


def body(
    flow_force, flow_coef, flow_init, compliance, shell_load, disp_init, patch_len, owner, block_row
):
    force_here = flow_force[0]
    coef_here = flow_coef[0]
    start_here = flow_init[0]
    slab_rows, planes, line_cells = force_here.shape
    assert slab_rows >= HALO and planes >= BAND
    side_count = lax.axis_size("side")
    side_id = lax.axis_index("side")
    slab_id = lax.axis_index("slab")
    shell_flag = side_id == side_count - 1
    live = (jnp.arange(line_cells)[None, :] < patch_len[:, None]).astype(jnp.float32)
    own = (owner[:, 0] == side_id).astype(jnp.float32)[:, None]
    own_live = own * live
    onehot = (block_row[None, :] == jnp.arange(slab_rows)[:, None]).astype(jnp.float32) * own[:, 0][None, :]
    pick = (block_row[:, None] == jnp.arange(slab_rows)[None, :]).astype(jnp.float32)

    deep_planes = planes - BAND
    disp_zero = own_live * disp_init
    plane_zero = jnp.sum(onehot[:, :, None] * (live * disp_zero)[None], axis=1)
    packed, plane_zero_rims = exchange(
        [
            (jnp.concatenate([start_here[:, :BAND], force_here[:, :BAND], coef_here[:, :BAND]], axis=1), HALO),
            (plane_zero, HALO),
        ]
    )
    after_band = 0.0 * packed[0, 0, 0]
    init_deep, fc_deep = exchange(
        [
            (start_here[:, BAND:] + after_band, 2),
            (jnp.concatenate([force_here[:, BAND:], coef_here[:, BAND:]], axis=1) + after_band, 1),
        ]
    )
    init_band, force_band, coef_band = (
        packed[:, :BAND],
        packed[:, BAND : 2 * BAND],
        packed[:, 2 * BAND :],
    )
    init_deep = jnp.concatenate([init_band[HALO - 2 : HALO + slab_rows + 2], init_deep], axis=1)
    force_deep = jnp.concatenate(
        [force_band[HALO - 1 : HALO + slab_rows + 1], fc_deep[:, :deep_planes]], axis=1
    )
    coef_deep = jnp.concatenate([coef_band[HALO - 1 : HALO + slab_rows + 1], fc_deep[:, deep_planes:]], axis=1)
    global_row = slab_id * slab_rows + jnp.arange(slab_rows + 2 * HALO) - HALO
    total_rows = slab_rows * lax.axis_size("slab")
    row_ok = ((global_row >= 0) & (global_row < total_rows))[:, None, None]

    ok_one = row_ok[HALO - 1 : HALO + slab_rows + 1]
    ok_two = row_ok[HALO : HALO + slab_rows]

    def plane_of(disp):
        return jnp.sum(onehot[:, :, None] * (live * disp)[None], axis=1)

    def evaluate(disp, plane_rims=None, extra=()):
        if plane_rims is None:
            got = exchange([(plane_of(disp), HALO)] + list(extra))
            plane_rims, extra = got[0], got[1:]
        rhs = force_band.at[:, 0, :].add(plane_rims)
        band = band_solve(init_band, rhs, coef_band, row_ok)
        traction = PENALTY * jnp.sum(pick[:, :, None] * band[:, 0, :][None], axis=1)
        loaded = live * (shell_load - traction)
        tilde = own_live * jnp.sum(compliance * loaded[:, None, :], axis=-1)
        return tilde, band, extra

    tilde_zero, unused, unused_extra = evaluate(disp_zero, plane_zero_rims)
    resid_zero = tilde_zero - disp_zero
    disp_one = disp_zero + RELAX * resid_zero
    tilde_one, unused, unused_extra = evaluate(disp_one)
    init_deep, tilde_one = lax.optimization_barrier((init_deep, tilde_one))
    deep = lax.cond(
        shell_flag,
        lambda: jnp.zeros((slab_rows,) + init_deep.shape[1:], jnp.float32),
        lambda: deep_step(
            deep_step(init_deep, force_deep, coef_deep, ok_one), force_deep[1:-1], coef_deep[1:-1], ok_two
        ),
    )
    resid_one = tilde_one - disp_one
    diff_one = resid_one - resid_zero
    sums = fluid_sum(
        allsum_axis(jnp.stack([jnp.sum(diff_one * diff_one), jnp.sum(diff_one * resid_one)]), "slab"),
        side_id,
        side_count - 1,
    )
    step_one = tilde_one - tilde_zero
    rims_base, rims_step = exchange([(plane_of(tilde_one), HALO), (plane_of(step_one), HALO)])
    band_base = band_solve(init_band, force_band.at[:, 0, :].add(rims_base), coef_band, row_ok)
    band_step = band_solve(
        jnp.zeros_like(init_band), jnp.zeros_like(force_band).at[:, 0, :].set(rims_step), coef_band, row_ok
    )
    both = jnp.stack([band_base[:, 0, :], band_step[:, 0, :]])
    traction = PENALTY * jnp.sum(pick[None, :, :, None] * both[:, None], axis=2)
    loaded = live[None] * (jnp.stack([shell_load, jnp.zeros_like(shell_load)]) - traction)
    applied = own_live[None] * jnp.sum(compliance[None] * loaded[:, :, None, :], axis=-1)
    tilde_base, tilde_step = applied[0], applied[1]
    gram_aa, gram_ab = sums[0], sums[1]
    coeff = -gram_ab / (gram_aa + (0.001 * gram_aa + 1e-06))
    disp_two = tilde_one + coeff * step_one
    (deep,) = exchange([(deep + 0.0 * coeff, 2)])
    tilde_two = tilde_base + coeff * tilde_step
    band_two = band_base + coeff * band_step
    deep = lax.cond(
        shell_flag,
        lambda: jnp.zeros((slab_rows,) + deep.shape[1:], jnp.float32),
        lambda: deep_step(
            deep_step(deep, force_deep, coef_deep, ok_one), force_deep[1:-1], coef_deep[1:-1], ok_two
        ),
    )
    resid_two = tilde_two - disp_two
    newer = resid_two - resid_one
    partial = jnp.stack(
        [
            jnp.sum(newer * newer, axis=0),
            jnp.sum(newer * diff_one, axis=0),
            jnp.sum(newer * resid_two, axis=0),
            jnp.sum(diff_one * resid_two, axis=0),
        ]
    )
    patches_here = tilde_two.shape[0]
    outgoing = jnp.concatenate(
        [
            tilde_two,
            tilde_one,
            tilde_zero,
            resid_two,
            partial,
            jnp.where((jnp.arange(line_cells) == 0) & (side_id == 0), gram_aa, 0.0)[None],
        ],
        axis=0,
    )
    gathered = outgoing
    for source in range(side_count - 1):
        gathered = gathered + lax.ppermute(outgoing, "side", [(source, side_count - 1)])
    sums = shell_sum(jnp.sum(gathered[4 * patches_here : 4 * patches_here + 4], axis=1), side_count)
    gram_aa = gathered[4 * patches_here + 4, 0]
    gram_nn, gram_no, proj_new, proj_old = sums[0], sums[1], sums[2], sums[3]
    tilde_two, tilde_one, tilde_zero, resid_two = (
        gathered[k * patches_here : (k + 1) * patches_here] for k in range(4)
    )

    shift_two = 0.001 * (gram_nn + gram_aa) + 1e-06
    diag_new = gram_nn + shift_two
    diag_old = gram_aa + shift_two
    determ = diag_new * diag_old - gram_no * gram_no
    coeff_new = (-proj_new * diag_old + proj_old * gram_no) / determ
    coeff_old = (-proj_old * diag_new + proj_new * gram_no) / determ
    disp_three = (
        tilde_two + coeff_new * (tilde_two - tilde_one) + coeff_old * (tilde_one - tilde_zero)
    )

    flow_state = jnp.concatenate([band_two, deep[:, band_two.shape[1] :]], axis=1)
    disp_next = jnp.where(shell_flag, disp_three, 0.0)[None]
    residual = jnp.where(shell_flag, resid_two, 0.0)[None]
    flow_final = jnp.where(shell_flag, 0.0, flow_state)[None]
    return (disp_next, residual, flow_final)


def solution(mesh):
    return jax.shard_map(
        body,
        mesh=mesh,
        in_specs=(
            P("side", "slab", None, None),
            P("side", "slab", None, None),
            P("side", "slab", None, None),
            P("slab", None, None),
            P("slab", None),
            P("slab", None),
            P("slab"),
            P("slab", None),
            P("slab"),
        ),
        out_specs=(P("side", "slab", None), P("side", "slab", None), P("side", "slab", None, None)),
        check_vma=False,
    )
```

```python
import jax
import jax.numpy as jnp
from jax import lax
from jax.sharding import PartitionSpec as P

SWEEPS = 4
RELAX = 0.5
PENALTY = 3.0
HALO = SWEEPS
BAND = 2 * SWEEPS


def shift_y(a):
    zero = jnp.zeros_like(a[..., :1])
    return (jnp.concatenate([a[..., 1:], zero], axis=-1), jnp.concatenate([zero, a[..., :-1]], axis=-1))


def stencil(rhs, coef, xp, xm, zp, zm, centre):
    yp, ym = shift_y(centre)
    total = ((((xp + xm) + zp) + zm) + yp) + ym
    return (rhs + total) / (6.0 + coef)


def band_solve(q, rhs, coef, row_ok):
    rows, planes = q.shape[0], q.shape[1]
    for k in range(1, SWEEPS + 1):
        centre = q[1:-1, :-1]
        zm = jnp.concatenate([jnp.zeros_like(centre[:, :1]), centre[:, :-1]], axis=1)
        new = stencil(
            rhs[k : rows - k, : planes - k],
            coef[k : rows - k, : planes - k],
            q[2:, :-1],
            q[:-2, :-1],
            q[1:-1, 1:],
            zm,
            centre,
        )
        q = jnp.where(row_ok[k : rows - k], new, 0.0)
    return q


def ring_pairs(count):
    forward = [(i, i + 1) for i in range(count - 1)]
    return forward, [(t, s) for s, t in forward]


def rims(block, width):
    count = lax.axis_size("slab")
    forward, backward = ring_pairs(count)
    low = lax.ppermute(block[block.shape[0] - width :], "slab", forward)
    high = lax.ppermute(block[:width], "slab", backward)
    return jnp.concatenate([low, block, high], axis=0)


def exchange(items):
    count = lax.axis_size("slab")
    forward, backward = ring_pairs(count)
    cells = items[0][0].shape[-1]
    sizes = [width * (a.size // a.shape[0]) // cells for a, width in items]
    up = jnp.concatenate([a[a.shape[0] - w :].reshape(-1, cells) for a, w in items], axis=0)
    down = jnp.concatenate([a[:w].reshape(-1, cells) for a, w in items], axis=0)
    low = lax.ppermute(up, "slab", forward)
    high = lax.ppermute(down, "slab", backward)
    out, at = [], 0
    for (a, w), n in zip(items, sizes):
        shape = (w,) + a.shape[1:]
        out.append(
            jnp.concatenate([low[at : at + n].reshape(shape), a, high[at : at + n].reshape(shape)], axis=0)
        )
        at += n
    return out


def deep_step(q, rhs, coef, ok):
    centre = q[1:-1]
    zero = jnp.zeros_like(centre[:, :1])
    new = stencil(
        rhs,
        coef,
        q[2:],
        q[:-2],
        jnp.concatenate([centre[:, 1:], zero], axis=1),
        jnp.concatenate([zero, centre[:, :-1]], axis=1),
        centre,
    )
    return jnp.where(ok, new, 0.0)


def deep_solve(q, rhs, coef, row_ok):
    rows = q.shape[0]
    for k in range(1, SWEEPS + 1):
        centre = q[1:-1]
        zero = jnp.zeros_like(centre[:, :1])
        new = stencil(
            rhs[k : rows - k],
            coef[k : rows - k],
            q[2:],
            q[:-2],
            jnp.concatenate([centre[:, 1:], zero], axis=1),
            jnp.concatenate([zero, centre[:, :-1]], axis=1),
            centre,
        )
        q = jnp.where(row_ok[k : rows - k], new, 0.0)
    return q


def allsum_axis(v, axis):
    count = lax.axis_size(axis)
    step = 1
    while step < count:
        v = v + lax.ppermute(v, axis, [(i, i ^ step) for i in range(count)])
        step *= 2
    return v


def shell_sum(v, side_count):
    count = lax.axis_size("slab")
    base = (side_count - 1) * count
    step = 1
    while step < count:
        pairs = [(base + i, base + (i ^ step)) for i in range(count)]
        v = v + lax.ppermute(v, ("side", "slab"), pairs)
        step *= 2
    return v


def fluid_sum(v, side_id, sectors):
    count = lax.axis_size("slab")
    got = [v]
    for k in range(1, sectors):
        pairs = [(s * count + j, ((s + k) % sectors) * count + j) for s in range(sectors) for j in range(count)]
        got.append(lax.ppermute(v, ("side", "slab"), pairs))
    total = None
    for t in range(sectors):
        term = got[0]
        for k in range(1, sectors):
            term = jnp.where(side_id == (t + k) % sectors, got[k], term)
        term = jnp.where(side_id == t, got[0], term)
        total = term if total is None else total + term
    return total


def allsum(v):
    return allsum_axis(allsum_axis(v, "slab"), "side")


def body(
    flow_force, flow_coef, flow_init, compliance, shell_load, disp_init, patch_len, owner, block_row
):
    force_here = flow_force[0]
    coef_here = flow_coef[0]
    start_here = flow_init[0]
    slab_rows, planes, line_cells = force_here.shape
    assert slab_rows >= HALO and planes >= BAND
    side_count = lax.axis_size("side")
    side_id = lax.axis_index("side")
    slab_id = lax.axis_index("slab")
    shell_flag = side_id == side_count - 1
    live = (jnp.arange(line_cells)[None, :] < patch_len[:, None]).astype(jnp.float32)
    own = (owner[:, 0] == side_id).astype(jnp.float32)[:, None]
    own_live = own * live
    onehot = (block_row[None, :] == jnp.arange(slab_rows)[:, None]).astype(jnp.float32) * own[:, 0][None, :]
    pick = (block_row[:, None] == jnp.arange(slab_rows)[None, :]).astype(jnp.float32)

    deep_planes = planes - BAND
    disp_zero = own_live * disp_init
    plane_zero = jnp.sum(onehot[:, :, None] * (live * disp_zero)[None], axis=1)
    packed, plane_zero_rims = exchange(
        [
            (jnp.concatenate([start_here[:, :BAND], force_here[:, :BAND], coef_here[:, :BAND]], axis=1), HALO),
            (plane_zero, HALO),
        ]
    )
    after_band = 0.0 * packed[0, 0, 0]
    init_deep, fc_deep = exchange(
        [
            (start_here[:, BAND:] + after_band, 2),
            (jnp.concatenate([force_here[:, BAND:], coef_here[:, BAND:]], axis=1) + after_band, 1),
        ]
    )
    init_band, force_band, coef_band = (
        packed[:, :BAND],
        packed[:, BAND : 2 * BAND],
        packed[:, 2 * BAND :],
    )
    init_deep = jnp.concatenate([init_band[HALO - 2 : HALO + slab_rows + 2], init_deep], axis=1)
    force_deep = jnp.concatenate(
        [force_band[HALO - 1 : HALO + slab_rows + 1], fc_deep[:, :deep_planes]], axis=1
    )
    coef_deep = jnp.concatenate([coef_band[HALO - 1 : HALO + slab_rows + 1], fc_deep[:, deep_planes:]], axis=1)
    global_row = slab_id * slab_rows + jnp.arange(slab_rows + 2 * HALO) - HALO
    total_rows = slab_rows * lax.axis_size("slab")
    row_ok = ((global_row >= 0) & (global_row < total_rows))[:, None, None]

    ok_one = row_ok[HALO - 1 : HALO + slab_rows + 1]
    ok_two = row_ok[HALO : HALO + slab_rows]

    def plane_of(disp):
        return jnp.sum(onehot[:, :, None] * (live * disp)[None], axis=1)

    def evaluate(disp, plane_rims=None, extra=()):
        if plane_rims is None:
            got = exchange([(plane_of(disp), HALO)] + list(extra))
            plane_rims, extra = got[0], got[1:]
        rhs = force_band.at[:, 0, :].add(plane_rims)
        band = band_solve(init_band, rhs, coef_band, row_ok)
        traction = PENALTY * jnp.sum(pick[:, :, None] * band[:, 0, :][None], axis=1)
        loaded = live * (shell_load - traction)
        tilde = own_live * jnp.sum(compliance * loaded[:, None, :], axis=-1)
        return tilde, band, extra

    tilde_zero, unused, unused_extra = evaluate(disp_zero, plane_zero_rims)
    resid_zero = tilde_zero - disp_zero
    disp_one = disp_zero + RELAX * resid_zero
    tilde_one, unused, unused_extra = evaluate(disp_one)
    init_deep, tilde_one = lax.optimization_barrier((init_deep, tilde_one))
    deep = lax.cond(
        shell_flag,
        lambda: jnp.zeros((slab_rows,) + init_deep.shape[1:], jnp.float32),
        lambda: deep_step(
            deep_step(init_deep, force_deep, coef_deep, ok_one), force_deep[1:-1], coef_deep[1:-1], ok_two
        ),
    )
    resid_one = tilde_one - disp_one
    diff_one = resid_one - resid_zero
    sums = fluid_sum(
        allsum_axis(jnp.stack([jnp.sum(diff_one * diff_one), jnp.sum(diff_one * resid_one)]), "slab"),
        side_id,
        side_count - 1,
    )
    step_one = tilde_one - tilde_zero
    rims_base, rims_step = exchange([(plane_of(tilde_one), HALO), (plane_of(step_one), HALO)])
    band_base = band_solve(init_band, force_band.at[:, 0, :].add(rims_base), coef_band, row_ok)
    band_step = band_solve(
        jnp.zeros_like(init_band), jnp.zeros_like(force_band).at[:, 0, :].set(rims_step), coef_band, row_ok
    )
    both = jnp.stack([band_base[:, 0, :], band_step[:, 0, :]])
    traction = PENALTY * jnp.sum(pick[None, :, :, None] * both[:, None], axis=2)
    loaded = live[None] * (jnp.stack([shell_load, jnp.zeros_like(shell_load)]) - traction)
    applied = own_live[None] * jnp.sum(compliance[None] * loaded[:, :, None, :], axis=-1)
    tilde_base, tilde_step = applied[0], applied[1]
    gram_aa, gram_ab = sums[0], sums[1]
    coeff = -gram_ab / (gram_aa + (0.001 * gram_aa + 1e-06))
    disp_two = tilde_one + coeff * step_one
    (deep,) = exchange([(deep + 0.0 * coeff, 2)])
    faces_in = deep[0, 0, 0]
    tilde_two = tilde_base + coeff * tilde_step
    band_two = band_base + coeff * band_step
    deep = lax.cond(
        shell_flag,
        lambda: jnp.zeros((slab_rows,) + deep.shape[1:], jnp.float32),
        lambda: deep_step(
            deep_step(deep, force_deep, coef_deep, ok_one), force_deep[1:-1], coef_deep[1:-1], ok_two
        ),
    )
    resid_two = tilde_two - disp_two
    newer = resid_two - resid_one
    partial = jnp.stack(
        [
            jnp.sum(newer * newer, axis=0),
            jnp.sum(newer * diff_one, axis=0),
            jnp.sum(newer * resid_two, axis=0),
            jnp.sum(diff_one * resid_two, axis=0),
        ]
    )
    patches_here = tilde_two.shape[0]
    outgoing = jnp.concatenate(
        [
            tilde_two,
            tilde_one,
            tilde_zero,
            resid_two,
            partial,
            jnp.where((jnp.arange(line_cells) == 0) & (side_id == 0), gram_aa, 0.0)[None],
        ],
        axis=0,
    )
    outgoing = outgoing + 0.0 * faces_in
    gathered = outgoing
    for source in range(side_count - 1):
        gathered = gathered + lax.ppermute(outgoing, "side", [(source, side_count - 1)])
    sums = shell_sum(jnp.sum(gathered[4 * patches_here : 4 * patches_here + 4], axis=1), side_count)
    gram_aa = gathered[4 * patches_here + 4, 0]
    gram_nn, gram_no, proj_new, proj_old = sums[0], sums[1], sums[2], sums[3]
    tilde_two, tilde_one, tilde_zero, resid_two = (
        gathered[k * patches_here : (k + 1) * patches_here] for k in range(4)
    )

    shift_two = 0.001 * (gram_nn + gram_aa) + 1e-06
    diag_new = gram_nn + shift_two
    diag_old = gram_aa + shift_two
    determ = diag_new * diag_old - gram_no * gram_no
    coeff_new = (-proj_new * diag_old + proj_old * gram_no) / determ
    coeff_old = (-proj_old * diag_new + proj_new * gram_no) / determ
    disp_three = (
        tilde_two + coeff_new * (tilde_two - tilde_one) + coeff_old * (tilde_one - tilde_zero)
    )

    flow_state = jnp.concatenate([band_two, deep[:, band_two.shape[1] :]], axis=1)
    disp_next = jnp.where(shell_flag, disp_three, 0.0)[None]
    residual = jnp.where(shell_flag, resid_two, 0.0)[None]
    flow_final = jnp.where(shell_flag, 0.0, flow_state)[None]
    return (disp_next, residual, flow_final)


def solution(mesh):
    return jax.shard_map(
        body,
        mesh=mesh,
        in_specs=(
            P("side", "slab", None, None),
            P("side", "slab", None, None),
            P("side", "slab", None, None),
            P("slab", None, None),
            P("slab", None),
            P("slab", None),
            P("slab"),
            P("slab", None),
            P("slab"),
        ),
        out_specs=(P("side", "slab", None), P("side", "slab", None), P("side", "slab", None, None)),
        check_vma=False,
    )
```

```python
import jax
import jax.numpy as jnp
from jax import lax
from jax.sharding import PartitionSpec as P

SWEEPS = 4
RELAX = 0.5
PENALTY = 3.0
HALO = SWEEPS
BAND = 2 * SWEEPS


def shift_y(a):
    zero = jnp.zeros_like(a[..., :1])
    return (jnp.concatenate([a[..., 1:], zero], axis=-1), jnp.concatenate([zero, a[..., :-1]], axis=-1))


def stencil(rhs, coef, xp, xm, zp, zm, centre):
    yp, ym = shift_y(centre)
    total = ((((xp + xm) + zp) + zm) + yp) + ym
    return (rhs + total) / (6.0 + coef)


def band_solve(q, rhs, coef, row_ok):
    rows, planes = q.shape[0], q.shape[1]
    for k in range(1, SWEEPS + 1):
        centre = q[1:-1, :-1]
        zm = jnp.concatenate([jnp.zeros_like(centre[:, :1]), centre[:, :-1]], axis=1)
        new = stencil(
            rhs[k : rows - k, : planes - k],
            coef[k : rows - k, : planes - k],
            q[2:, :-1],
            q[:-2, :-1],
            q[1:-1, 1:],
            zm,
            centre,
        )
        q = jnp.where(row_ok[k : rows - k], new, 0.0)
    return q


def ring_pairs(count):
    forward = [(i, i + 1) for i in range(count - 1)]
    return forward, [(t, s) for s, t in forward]


def rims(block, width):
    count = lax.axis_size("slab")
    forward, backward = ring_pairs(count)
    low = lax.ppermute(block[block.shape[0] - width :], "slab", forward)
    high = lax.ppermute(block[:width], "slab", backward)
    return jnp.concatenate([low, block, high], axis=0)


def exchange(items):
    count = lax.axis_size("slab")
    forward, backward = ring_pairs(count)
    cells = items[0][0].shape[-1]
    sizes = [width * (a.size // a.shape[0]) // cells for a, width in items]
    up = jnp.concatenate([a[a.shape[0] - w :].reshape(-1, cells) for a, w in items], axis=0)
    down = jnp.concatenate([a[:w].reshape(-1, cells) for a, w in items], axis=0)
    low = lax.ppermute(up, "slab", forward)
    high = lax.ppermute(down, "slab", backward)
    out, at = [], 0
    for (a, w), n in zip(items, sizes):
        shape = (w,) + a.shape[1:]
        out.append(
            jnp.concatenate([low[at : at + n].reshape(shape), a, high[at : at + n].reshape(shape)], axis=0)
        )
        at += n
    return out


def deep_step(q, rhs, coef, ok):
    centre = q[1:-1]
    zero = jnp.zeros_like(centre[:, :1])
    new = stencil(
        rhs,
        coef,
        q[2:],
        q[:-2],
        jnp.concatenate([centre[:, 1:], zero], axis=1),
        jnp.concatenate([zero, centre[:, :-1]], axis=1),
        centre,
    )
    return jnp.where(ok, new, 0.0)


def deep_solve(q, rhs, coef, row_ok):
    rows = q.shape[0]
    for k in range(1, SWEEPS + 1):
        centre = q[1:-1]
        zero = jnp.zeros_like(centre[:, :1])
        new = stencil(
            rhs[k : rows - k],
            coef[k : rows - k],
            q[2:],
            q[:-2],
            jnp.concatenate([centre[:, 1:], zero], axis=1),
            jnp.concatenate([zero, centre[:, :-1]], axis=1),
            centre,
        )
        q = jnp.where(row_ok[k : rows - k], new, 0.0)
    return q


def allsum_axis(v, axis):
    count = lax.axis_size(axis)
    step = 1
    while step < count:
        v = v + lax.ppermute(v, axis, [(i, i ^ step) for i in range(count)])
        step *= 2
    return v


def shell_sum(v, side_count):
    count = lax.axis_size("slab")
    base = (side_count - 1) * count
    step = 1
    while step < count:
        pairs = [(base + i, base + (i ^ step)) for i in range(count)]
        v = v + lax.ppermute(v, ("side", "slab"), pairs)
        step *= 2
    return v


def fluid_sum(v, side_id, sectors):
    count = lax.axis_size("slab")
    got = [v]
    for k in range(1, sectors):
        pairs = [(s * count + j, ((s + k) % sectors) * count + j) for s in range(sectors) for j in range(count)]
        got.append(lax.ppermute(v, ("side", "slab"), pairs))
    total = None
    for t in range(sectors):
        term = got[0]
        for k in range(1, sectors):
            term = jnp.where(side_id == (t + k) % sectors, got[k], term)
        term = jnp.where(side_id == t, got[0], term)
        total = term if total is None else total + term
    return total


def allsum(v):
    return allsum_axis(allsum_axis(v, "slab"), "side")


def body(
    flow_force, flow_coef, flow_init, compliance, shell_load, disp_init, patch_len, owner, block_row
):
    force_here = flow_force[0]
    coef_here = flow_coef[0]
    start_here = flow_init[0]
    slab_rows, planes, line_cells = force_here.shape
    assert slab_rows >= HALO and planes >= BAND
    side_count = lax.axis_size("side")
    side_id = lax.axis_index("side")
    slab_id = lax.axis_index("slab")
    shell_flag = side_id == side_count - 1
    live = (jnp.arange(line_cells)[None, :] < patch_len[:, None]).astype(jnp.float32)
    own = (owner[:, 0] == side_id).astype(jnp.float32)[:, None]
    own_live = own * live
    onehot = (block_row[None, :] == jnp.arange(slab_rows)[:, None]).astype(jnp.float32) * own[:, 0][None, :]
    pick = (block_row[:, None] == jnp.arange(slab_rows)[None, :]).astype(jnp.float32)

    deep_planes = planes - BAND
    disp_zero = own_live * disp_init
    plane_zero = jnp.sum(onehot[:, :, None] * (live * disp_zero)[None], axis=1)
    packed, plane_zero_rims = exchange(
        [
            (jnp.concatenate([start_here[:, :BAND], force_here[:, :BAND], coef_here[:, :BAND]], axis=1), HALO),
            (plane_zero, HALO),
        ]
    )
    after_band = 0.0 * packed[0, 0, 0]
    init_deep, fc_deep = exchange(
        [
            (start_here[:, BAND:] + after_band, 2),
            (jnp.concatenate([force_here[:, BAND:], coef_here[:, BAND:]], axis=1) + after_band, 1),
        ]
    )
    init_band, force_band, coef_band = (
        packed[:, :BAND],
        packed[:, BAND : 2 * BAND],
        packed[:, 2 * BAND :],
    )
    init_deep = jnp.concatenate([init_band[HALO - 2 : HALO + slab_rows + 2], init_deep], axis=1)
    force_deep = jnp.concatenate(
        [force_band[HALO - 1 : HALO + slab_rows + 1], fc_deep[:, :deep_planes]], axis=1
    )
    coef_deep = jnp.concatenate([coef_band[HALO - 1 : HALO + slab_rows + 1], fc_deep[:, deep_planes:]], axis=1)
    global_row = slab_id * slab_rows + jnp.arange(slab_rows + 2 * HALO) - HALO
    total_rows = slab_rows * lax.axis_size("slab")
    row_ok = ((global_row >= 0) & (global_row < total_rows))[:, None, None]

    ok_one = row_ok[HALO - 1 : HALO + slab_rows + 1]
    ok_two = row_ok[HALO : HALO + slab_rows]

    def plane_of(disp):
        return jnp.sum(onehot[:, :, None] * (live * disp)[None], axis=1)

    def evaluate(disp, plane_rims=None, extra=()):
        if plane_rims is None:
            got = exchange([(plane_of(disp), HALO)] + list(extra))
            plane_rims, extra = got[0], got[1:]
        rhs = force_band.at[:, 0, :].add(plane_rims)
        band = band_solve(init_band, rhs, coef_band, row_ok)
        traction = PENALTY * jnp.sum(pick[:, :, None] * band[:, 0, :][None], axis=1)
        loaded = live * (shell_load - traction)
        tilde = own_live * jnp.sum(compliance * loaded[:, None, :], axis=-1)
        return tilde, band, extra

    tilde_zero, unused, unused_extra = evaluate(disp_zero, plane_zero_rims)
    resid_zero = tilde_zero - disp_zero
    disp_one = disp_zero + RELAX * resid_zero
    tilde_one, unused, unused_extra = evaluate(disp_one)
    init_deep, tilde_one = lax.optimization_barrier((init_deep, tilde_one))
    deep = lax.cond(
        shell_flag,
        lambda: jnp.zeros((slab_rows,) + init_deep.shape[1:], jnp.float32),
        lambda: deep_step(
            deep_step(init_deep, force_deep, coef_deep, ok_one), force_deep[1:-1], coef_deep[1:-1], ok_two
        ),
    )
    resid_one = tilde_one - disp_one
    diff_one = resid_one - resid_zero
    sums = fluid_sum(
        allsum_axis(jnp.stack([jnp.sum(diff_one * diff_one), jnp.sum(diff_one * resid_one)]), "slab"),
        side_id,
        side_count - 1,
    )
    step_one = tilde_one - tilde_zero
    rims_base, rims_step = exchange([(plane_of(tilde_one), HALO), (plane_of(step_one), HALO)])
    band_base = band_solve(init_band, force_band.at[:, 0, :].add(rims_base), coef_band, row_ok)
    band_step = band_solve(
        jnp.zeros_like(init_band), jnp.zeros_like(force_band).at[:, 0, :].set(rims_step), coef_band, row_ok
    )
    both = jnp.stack([band_base[:, 0, :], band_step[:, 0, :]])
    traction = PENALTY * jnp.sum(pick[None, :, :, None] * both[:, None], axis=2)
    loaded = live[None] * (jnp.stack([shell_load, jnp.zeros_like(shell_load)]) - traction)
    applied = own_live[None] * jnp.sum(compliance[None] * loaded[:, :, None, :], axis=-1)
    tilde_base, tilde_step = applied[0], applied[1]
    gram_aa, gram_ab = sums[0], sums[1]
    coeff = -gram_ab / (gram_aa + (0.001 * gram_aa + 1e-06))
    disp_two = tilde_one + coeff * step_one
    (deep,) = exchange([(deep + 0.0 * coeff, 2)])
    tilde_two = tilde_base + coeff * tilde_step
    band_two = band_base + coeff * band_step
    deep = lax.cond(
        shell_flag,
        lambda: jnp.zeros((slab_rows,) + deep.shape[1:], jnp.float32),
        lambda: jnp.concatenate(
            [
                band_two,
                deep_step(
                    deep_step(deep, force_deep, coef_deep, ok_one), force_deep[1:-1], coef_deep[1:-1], ok_two
                )[:, band_two.shape[1] :],
            ],
            axis=1,
        ),
    )
    resid_two = tilde_two - disp_two
    newer = resid_two - resid_one
    partial = jnp.stack(
        [
            jnp.sum(newer * newer, axis=0),
            jnp.sum(newer * diff_one, axis=0),
            jnp.sum(newer * resid_two, axis=0),
            jnp.sum(diff_one * resid_two, axis=0),
        ]
    )
    patches_here = tilde_two.shape[0]
    outgoing = jnp.concatenate(
        [
            tilde_two,
            tilde_one,
            tilde_zero,
            resid_two,
            partial,
            jnp.where((jnp.arange(line_cells) == 0) & (side_id == 0), gram_aa, 0.0)[None],
        ],
        axis=0,
    )
    gathered = outgoing
    for source in range(side_count - 1):
        gathered = gathered + lax.ppermute(outgoing, "side", [(source, side_count - 1)])
    sums = shell_sum(jnp.sum(gathered[4 * patches_here : 4 * patches_here + 4], axis=1), side_count)
    gram_aa = gathered[4 * patches_here + 4, 0]
    gram_nn, gram_no, proj_new, proj_old = sums[0], sums[1], sums[2], sums[3]
    tilde_two, tilde_one, tilde_zero, resid_two = (
        gathered[k * patches_here : (k + 1) * patches_here] for k in range(4)
    )

    shift_two = 0.001 * (gram_nn + gram_aa) + 1e-06
    diag_new = gram_nn + shift_two
    diag_old = gram_aa + shift_two
    determ = diag_new * diag_old - gram_no * gram_no
    coeff_new = (-proj_new * diag_old + proj_old * gram_no) / determ
    coeff_old = (-proj_old * diag_new + proj_new * gram_no) / determ
    disp_three = (
        tilde_two + coeff_new * (tilde_two - tilde_one) + coeff_old * (tilde_one - tilde_zero)
    )

    disp_next = jnp.where(shell_flag, disp_three, 0.0)[None]
    residual = jnp.where(shell_flag, resid_two, 0.0)[None]
    flow_final = deep[None]
    return (disp_next, residual, flow_final)


def solution(mesh):
    return jax.shard_map(
        body,
        mesh=mesh,
        in_specs=(
            P("side", "slab", None, None),
            P("side", "slab", None, None),
            P("side", "slab", None, None),
            P("slab", None, None),
            P("slab", None),
            P("slab", None),
            P("slab"),
            P("slab", None),
            P("slab"),
        ),
        out_specs=(P("side", "slab", None), P("side", "slab", None), P("side", "slab", None, None)),
        check_vma=False,
    )
```

```python
import jax
import jax.numpy as jnp
from jax import lax
from jax.sharding import PartitionSpec as P

SWEEPS = 4
RELAX = 0.5
PENALTY = 3.0
HALO = SWEEPS
BAND = 2 * SWEEPS


def shift_y(a):
    zero = jnp.zeros_like(a[..., :1])
    return (jnp.concatenate([a[..., 1:], zero], axis=-1), jnp.concatenate([zero, a[..., :-1]], axis=-1))


def stencil(rhs, coef, xp, xm, zp, zm, centre):
    yp, ym = shift_y(centre)
    total = ((((xp + xm) + zp) + zm) + yp) + ym
    return (rhs + total) / (6.0 + coef)


def band_solve(q, rhs, coef, row_ok):
    rows, planes = q.shape[0], q.shape[1]
    for k in range(1, SWEEPS + 1):
        centre = q[1:-1, :-1]
        zm = jnp.concatenate([jnp.zeros_like(centre[:, :1]), centre[:, :-1]], axis=1)
        new = stencil(
            rhs[k : rows - k, : planes - k],
            coef[k : rows - k, : planes - k],
            q[2:, :-1],
            q[:-2, :-1],
            q[1:-1, 1:],
            zm,
            centre,
        )
        q = jnp.where(row_ok[k : rows - k], new, 0.0)
    return q


def ring_pairs(count):
    forward = [(i, i + 1) for i in range(count - 1)]
    return forward, [(t, s) for s, t in forward]


def rims(block, width):
    count = lax.axis_size("slab")
    forward, backward = ring_pairs(count)
    low = lax.ppermute(block[block.shape[0] - width :], "slab", forward)
    high = lax.ppermute(block[:width], "slab", backward)
    return jnp.concatenate([low, block, high], axis=0)


def exchange(items):
    count = lax.axis_size("slab")
    forward, backward = ring_pairs(count)
    cells = items[0][0].shape[-1]
    sizes = [width * (a.size // a.shape[0]) // cells for a, width in items]
    up = jnp.concatenate([a[a.shape[0] - w :].reshape(-1, cells) for a, w in items], axis=0)
    down = jnp.concatenate([a[:w].reshape(-1, cells) for a, w in items], axis=0)
    low = lax.ppermute(up, "slab", forward)
    high = lax.ppermute(down, "slab", backward)
    out, at = [], 0
    for (a, w), n in zip(items, sizes):
        shape = (w,) + a.shape[1:]
        out.append(
            jnp.concatenate([low[at : at + n].reshape(shape), a, high[at : at + n].reshape(shape)], axis=0)
        )
        at += n
    return out


def deep_step(q, rhs, coef, ok):
    centre = q[1:-1]
    zero = jnp.zeros_like(centre[:, :1])
    new = stencil(
        rhs,
        coef,
        q[2:],
        q[:-2],
        jnp.concatenate([centre[:, 1:], zero], axis=1),
        jnp.concatenate([zero, centre[:, :-1]], axis=1),
        centre,
    )
    return jnp.where(ok, new, 0.0)


def deep_solve(q, rhs, coef, row_ok):
    rows = q.shape[0]
    for k in range(1, SWEEPS + 1):
        centre = q[1:-1]
        zero = jnp.zeros_like(centre[:, :1])
        new = stencil(
            rhs[k : rows - k],
            coef[k : rows - k],
            q[2:],
            q[:-2],
            jnp.concatenate([centre[:, 1:], zero], axis=1),
            jnp.concatenate([zero, centre[:, :-1]], axis=1),
            centre,
        )
        q = jnp.where(row_ok[k : rows - k], new, 0.0)
    return q


def allsum_axis(v, axis):
    count = lax.axis_size(axis)
    step = 1
    while step < count:
        v = v + lax.ppermute(v, axis, [(i, i ^ step) for i in range(count)])
        step *= 2
    return v


def shell_sum(v, side_count):
    count = lax.axis_size("slab")
    base = (side_count - 1) * count
    step = 1
    while step < count:
        pairs = [(base + i, base + (i ^ step)) for i in range(count)]
        v = v + lax.ppermute(v, ("side", "slab"), pairs)
        step *= 2
    return v


def fluid_sum(v, side_id, sectors):
    count = lax.axis_size("slab")
    got = [v]
    for k in range(1, sectors):
        pairs = [(s * count + j, ((s + k) % sectors) * count + j) for s in range(sectors) for j in range(count)]
        got.append(lax.ppermute(v, ("side", "slab"), pairs))
    total = None
    for t in range(sectors):
        term = got[0]
        for k in range(1, sectors):
            term = jnp.where(side_id == (t + k) % sectors, got[k], term)
        term = jnp.where(side_id == t, got[0], term)
        total = term if total is None else total + term
    return total


def allsum(v):
    return allsum_axis(allsum_axis(v, "slab"), "side")


def body(
    flow_force, flow_coef, flow_init, compliance, shell_load, disp_init, patch_len, owner, block_row
):
    force_here = flow_force[0]
    coef_here = flow_coef[0]
    start_here = flow_init[0]
    slab_rows, planes, line_cells = force_here.shape
    assert slab_rows >= HALO and planes >= BAND
    side_count = lax.axis_size("side")
    side_id = lax.axis_index("side")
    slab_id = lax.axis_index("slab")
    shell_flag = side_id == side_count - 1
    live = (jnp.arange(line_cells)[None, :] < patch_len[:, None]).astype(jnp.float32)
    own = (owner[:, 0] == side_id).astype(jnp.float32)[:, None]
    own_live = own * live
    onehot = (block_row[None, :] == jnp.arange(slab_rows)[:, None]).astype(jnp.float32) * own[:, 0][None, :]
    pick = (block_row[:, None] == jnp.arange(slab_rows)[None, :]).astype(jnp.float32)

    deep_planes = planes - BAND
    disp_zero = own_live * disp_init
    plane_zero = jnp.sum(onehot[:, :, None] * (live * disp_zero)[None], axis=1)
    packed, plane_zero_rims = exchange(
        [
            (jnp.concatenate([start_here[:, :BAND], force_here[:, :BAND], coef_here[:, :BAND]], axis=1), HALO),
            (plane_zero, HALO),
        ]
    )
    after_band = 0.0 * packed[0, 0, 0]
    init_deep, fc_deep = exchange(
        [
            (start_here[:, BAND:] + after_band, 2),
            (jnp.concatenate([force_here[:, BAND:], coef_here[:, BAND:]], axis=1) + after_band, 1),
        ]
    )
    init_band, force_band, coef_band = (
        packed[:, :BAND],
        packed[:, BAND : 2 * BAND],
        packed[:, 2 * BAND :],
    )
    init_deep = jnp.concatenate([init_band[HALO - 2 : HALO + slab_rows + 2], init_deep], axis=1)
    force_deep = jnp.concatenate(
        [force_band[HALO - 1 : HALO + slab_rows + 1], fc_deep[:, :deep_planes]], axis=1
    )
    coef_deep = jnp.concatenate([coef_band[HALO - 1 : HALO + slab_rows + 1], fc_deep[:, deep_planes:]], axis=1)
    global_row = slab_id * slab_rows + jnp.arange(slab_rows + 2 * HALO) - HALO
    total_rows = slab_rows * lax.axis_size("slab")
    row_ok = ((global_row >= 0) & (global_row < total_rows))[:, None, None]

    ok_one = row_ok[HALO - 1 : HALO + slab_rows + 1]
    ok_two = row_ok[HALO : HALO + slab_rows]

    def plane_of(disp):
        return jnp.sum(onehot[:, :, None] * (live * disp)[None], axis=1)

    def evaluate(disp, plane_rims=None, extra=()):
        if plane_rims is None:
            got = exchange([(plane_of(disp), HALO)] + list(extra))
            plane_rims, extra = got[0], got[1:]
        rhs = force_band.at[:, 0, :].add(plane_rims)
        band = band_solve(init_band, rhs, coef_band, row_ok)
        traction = PENALTY * jnp.sum(pick[:, :, None] * band[:, 0, :][None], axis=1)
        loaded = live * (shell_load - traction)
        tilde = own_live * jnp.sum(compliance * loaded[:, None, :], axis=-1)
        return tilde, band, extra

    tilde_zero, unused, unused_extra = evaluate(disp_zero, plane_zero_rims)
    resid_zero = tilde_zero - disp_zero
    disp_one = disp_zero + RELAX * resid_zero
    tilde_one, unused, unused_extra = evaluate(disp_one)
    init_deep, tilde_one = lax.optimization_barrier((init_deep, tilde_one))
    deep = lax.cond(
        shell_flag,
        lambda: jnp.zeros((slab_rows,) + init_deep.shape[1:], jnp.float32),
        lambda: deep_step(
            deep_step(init_deep, force_deep, coef_deep, ok_one), force_deep[1:-1], coef_deep[1:-1], ok_two
        ),
    )
    resid_one = tilde_one - disp_one
    diff_one = resid_one - resid_zero
    sums = fluid_sum(
        allsum_axis(jnp.stack([jnp.sum(diff_one * diff_one), jnp.sum(diff_one * resid_one)]), "slab"),
        side_id,
        side_count - 1,
    )
    step_one = tilde_one - tilde_zero
    rims_base, rims_step = exchange([(plane_of(tilde_one), HALO), (plane_of(step_one), HALO)])
    band_base = band_solve(init_band, force_band.at[:, 0, :].add(rims_base), coef_band, row_ok)
    band_step = band_solve(
        jnp.zeros_like(init_band), jnp.zeros_like(force_band).at[:, 0, :].set(rims_step), coef_band, row_ok
    )
    both = jnp.stack([band_base[:, 0, :], band_step[:, 0, :]])
    traction = PENALTY * jnp.sum(pick[None, :, :, None] * both[:, None], axis=2)
    loaded = live[None] * (jnp.stack([shell_load, jnp.zeros_like(shell_load)]) - traction)
    applied = own_live[None] * jnp.sum(compliance[None] * loaded[:, :, None, :], axis=-1)
    tilde_base, tilde_step = applied[0], applied[1]
    gram_aa, gram_ab = sums[0], sums[1]
    coeff = -gram_ab / (gram_aa + (0.001 * gram_aa + 1e-06))
    disp_two = tilde_one + coeff * step_one
    (deep,) = exchange([(deep + 0.0 * coeff, 2)])
    tilde_two = tilde_base + coeff * tilde_step
    band_two = band_base + coeff * band_step
    deep = lax.cond(
        shell_flag,
        lambda: jnp.zeros((slab_rows,) + deep.shape[1:], jnp.float32),
        lambda: deep_step(
            deep_step(deep, force_deep, coef_deep, ok_one), force_deep[1:-1], coef_deep[1:-1], ok_two
        ),
    )
    resid_two = tilde_two - disp_two
    newer = resid_two - resid_one
    partial = jnp.stack(
        [
            jnp.sum(newer * newer, axis=0),
            jnp.sum(newer * diff_one, axis=0),
            jnp.sum(newer * resid_two, axis=0),
            jnp.sum(diff_one * resid_two, axis=0),
        ]
    )
    patches_here = tilde_two.shape[0]
    sums_out = jnp.concatenate(
        [partial, jnp.where((jnp.arange(line_cells) == 0) & (side_id == 0), gram_aa, 0.0)[None]], axis=0
    )
    data_out = jnp.concatenate([tilde_two, tilde_one, tilde_zero, resid_two], axis=0)
    sums_in, data_in = sums_out, data_out
    for source in range(side_count - 1):
        sums_in = sums_in + lax.ppermute(sums_out, "side", [(source, side_count - 1)])
    for source in range(side_count - 1):
        data_in = data_in + lax.ppermute(data_out, "side", [(source, side_count - 1)])
    sums = shell_sum(jnp.sum(sums_in[:4], axis=1), side_count)
    gram_aa = sums_in[4, 0]
    gram_nn, gram_no, proj_new, proj_old = sums[0], sums[1], sums[2], sums[3]
    tilde_two, tilde_one, tilde_zero, resid_two = (
        data_in[k * patches_here : (k + 1) * patches_here] for k in range(4)
    )

    shift_two = 0.001 * (gram_nn + gram_aa) + 1e-06
    diag_new = gram_nn + shift_two
    diag_old = gram_aa + shift_two
    determ = diag_new * diag_old - gram_no * gram_no
    coeff_new = (-proj_new * diag_old + proj_old * gram_no) / determ
    coeff_old = (-proj_old * diag_new + proj_new * gram_no) / determ
    disp_three = (
        tilde_two + coeff_new * (tilde_two - tilde_one) + coeff_old * (tilde_one - tilde_zero)
    )

    flow_state = jnp.concatenate([band_two, deep[:, band_two.shape[1] :]], axis=1)
    disp_next = jnp.where(shell_flag, disp_three, 0.0)[None]
    residual = jnp.where(shell_flag, resid_two, 0.0)[None]
    flow_final = jnp.where(shell_flag, 0.0, flow_state)[None]
    return (disp_next, residual, flow_final)


def solution(mesh):
    return jax.shard_map(
        body,
        mesh=mesh,
        in_specs=(
            P("side", "slab", None, None),
            P("side", "slab", None, None),
            P("side", "slab", None, None),
            P("slab", None, None),
            P("slab", None),
            P("slab", None),
            P("slab"),
            P("slab", None),
            P("slab"),
        ),
        out_specs=(P("side", "slab", None), P("side", "slab", None), P("side", "slab", None, None)),
        check_vma=False,
    )
```

```python
import jax
import jax.numpy as jnp
from jax import lax
from jax.sharding import PartitionSpec as P

SWEEPS = 4
RELAX = 0.5
PENALTY = 3.0
HALO = SWEEPS
BAND = 2 * SWEEPS


def shift_y(a):
    zero = jnp.zeros_like(a[..., :1])
    return (jnp.concatenate([a[..., 1:], zero], axis=-1), jnp.concatenate([zero, a[..., :-1]], axis=-1))


def stencil(rhs, coef, xp, xm, zp, zm, centre):
    yp, ym = shift_y(centre)
    total = ((((xp + xm) + zp) + zm) + yp) + ym
    return (rhs + total) / (6.0 + coef)


def band_solve(q, rhs, coef, row_ok):
    rows, planes = q.shape[0], q.shape[1]
    for k in range(1, SWEEPS + 1):
        centre = q[1:-1, :-1]
        zm = jnp.concatenate([jnp.zeros_like(centre[:, :1]), centre[:, :-1]], axis=1)
        new = stencil(
            rhs[k : rows - k, : planes - k],
            coef[k : rows - k, : planes - k],
            q[2:, :-1],
            q[:-2, :-1],
            q[1:-1, 1:],
            zm,
            centre,
        )
        q = jnp.where(row_ok[k : rows - k], new, 0.0)
    return q


def ring_pairs(count):
    forward = [(i, i + 1) for i in range(count - 1)]
    return forward, [(t, s) for s, t in forward]


def rims(block, width):
    count = lax.axis_size("slab")
    forward, backward = ring_pairs(count)
    low = lax.ppermute(block[block.shape[0] - width :], "slab", forward)
    high = lax.ppermute(block[:width], "slab", backward)
    return jnp.concatenate([low, block, high], axis=0)


def exchange(items):
    count = lax.axis_size("slab")
    forward, backward = ring_pairs(count)
    cells = items[0][0].shape[-1]
    sizes = [width * (a.size // a.shape[0]) // cells for a, width in items]
    up = jnp.concatenate([a[a.shape[0] - w :].reshape(-1, cells) for a, w in items], axis=0)
    down = jnp.concatenate([a[:w].reshape(-1, cells) for a, w in items], axis=0)
    low = lax.ppermute(up, "slab", forward)
    high = lax.ppermute(down, "slab", backward)
    out, at = [], 0
    for (a, w), n in zip(items, sizes):
        shape = (w,) + a.shape[1:]
        out.append(
            jnp.concatenate([low[at : at + n].reshape(shape), a, high[at : at + n].reshape(shape)], axis=0)
        )
        at += n
    return out


def deep_step(q, rhs, coef, ok):
    centre = q[1:-1]
    zero = jnp.zeros_like(centre[:, :1])
    new = stencil(
        rhs,
        coef,
        q[2:],
        q[:-2],
        jnp.concatenate([centre[:, 1:], zero], axis=1),
        jnp.concatenate([zero, centre[:, :-1]], axis=1),
        centre,
    )
    return jnp.where(ok, new, 0.0)


def deep_solve(q, rhs, coef, row_ok):
    rows = q.shape[0]
    for k in range(1, SWEEPS + 1):
        centre = q[1:-1]
        zero = jnp.zeros_like(centre[:, :1])
        new = stencil(
            rhs[k : rows - k],
            coef[k : rows - k],
            q[2:],
            q[:-2],
            jnp.concatenate([centre[:, 1:], zero], axis=1),
            jnp.concatenate([zero, centre[:, :-1]], axis=1),
            centre,
        )
        q = jnp.where(row_ok[k : rows - k], new, 0.0)
    return q


def allsum_axis(v, axis):
    count = lax.axis_size(axis)
    step = 1
    while step < count:
        v = v + lax.ppermute(v, axis, [(i, i ^ step) for i in range(count)])
        step *= 2
    return v


def shell_sum(v, side_count):
    count = lax.axis_size("slab")
    base = (side_count - 1) * count
    step = 1
    while step < count:
        pairs = [(base + i, base + (i ^ step)) for i in range(count)]
        v = v + lax.ppermute(v, ("side", "slab"), pairs)
        step *= 2
    return v


def fluid_sum(v, side_id, sectors):
    count = lax.axis_size("slab")
    got = [v]
    for k in range(1, sectors):
        pairs = [(s * count + j, ((s + k) % sectors) * count + j) for s in range(sectors) for j in range(count)]
        got.append(lax.ppermute(v, ("side", "slab"), pairs))
    total = None
    for t in range(sectors):
        term = got[0]
        for k in range(1, sectors):
            term = jnp.where(side_id == (t + k) % sectors, got[k], term)
        term = jnp.where(side_id == t, got[0], term)
        total = term if total is None else total + term
    return total


def allsum(v):
    return allsum_axis(allsum_axis(v, "slab"), "side")


def body(
    flow_force, flow_coef, flow_init, compliance, shell_load, disp_init, patch_len, owner, block_row
):
    force_here = flow_force[0]
    coef_here = flow_coef[0]
    start_here = flow_init[0]
    slab_rows, planes, line_cells = force_here.shape
    assert slab_rows >= HALO and planes >= BAND
    side_count = lax.axis_size("side")
    side_id = lax.axis_index("side")
    slab_id = lax.axis_index("slab")
    shell_flag = side_id == side_count - 1
    live = (jnp.arange(line_cells)[None, :] < patch_len[:, None]).astype(jnp.float32)
    own = (owner[:, 0] == side_id).astype(jnp.float32)[:, None]
    own_live = own * live
    onehot = (block_row[None, :] == jnp.arange(slab_rows)[:, None]).astype(jnp.float32) * own[:, 0][None, :]
    pick = (block_row[:, None] == jnp.arange(slab_rows)[None, :]).astype(jnp.float32)

    deep_planes = planes - BAND
    disp_zero = own_live * disp_init
    plane_zero = jnp.sum(onehot[:, :, None] * (live * disp_zero)[None], axis=1)
    packed, plane_zero_rims = exchange(
        [
            (jnp.concatenate([start_here[:, :BAND], force_here[:, :BAND], coef_here[:, :BAND]], axis=1), HALO),
            (plane_zero, HALO),
        ]
    )
    init_band, force_band, coef_band = (
        packed[:, :BAND],
        packed[:, BAND : 2 * BAND],
        packed[:, 2 * BAND :],
    )
    global_row = slab_id * slab_rows + jnp.arange(slab_rows + 2 * HALO) - HALO
    total_rows = slab_rows * lax.axis_size("slab")
    row_ok = ((global_row >= 0) & (global_row < total_rows))[:, None, None]

    ok_one = row_ok[HALO - 1 : HALO + slab_rows + 1]
    ok_two = row_ok[HALO : HALO + slab_rows]

    def plane_of(disp):
        return jnp.sum(onehot[:, :, None] * (live * disp)[None], axis=1)

    def evaluate(disp, plane_rims=None, extra=()):
        if plane_rims is None:
            got = exchange([(plane_of(disp), HALO)] + list(extra))
            plane_rims, extra = got[0], got[1:]
        rhs = force_band.at[:, 0, :].add(plane_rims)
        band = band_solve(init_band, rhs, coef_band, row_ok)
        traction = PENALTY * jnp.sum(pick[:, :, None] * band[:, 0, :][None], axis=1)
        loaded = live * (shell_load - traction)
        tilde = own_live * jnp.sum(compliance * loaded[:, None, :], axis=-1)
        return tilde, band, extra

    tilde_zero, unused, unused_extra = evaluate(disp_zero, plane_zero_rims)
    resid_zero = tilde_zero - disp_zero
    disp_one = disp_zero + RELAX * resid_zero
    tilde_one, unused, (init_deep, fc_deep) = evaluate(
        disp_one,
        extra=[
            (start_here[:, BAND:], 2),
            (jnp.concatenate([force_here[:, BAND:], coef_here[:, BAND:]], axis=1), 1),
        ],
    )
    init_deep = jnp.concatenate([init_band[HALO - 2 : HALO + slab_rows + 2], init_deep], axis=1)
    force_deep = jnp.concatenate(
        [force_band[HALO - 1 : HALO + slab_rows + 1], fc_deep[:, :deep_planes]], axis=1
    )
    coef_deep = jnp.concatenate([coef_band[HALO - 1 : HALO + slab_rows + 1], fc_deep[:, deep_planes:]], axis=1)
    init_deep, tilde_one = lax.optimization_barrier((init_deep, tilde_one))
    deep = lax.cond(
        shell_flag,
        lambda: jnp.zeros((slab_rows,) + init_deep.shape[1:], jnp.float32),
        lambda: deep_step(
            deep_step(init_deep, force_deep, coef_deep, ok_one), force_deep[1:-1], coef_deep[1:-1], ok_two
        ),
    )
    resid_one = tilde_one - disp_one
    diff_one = resid_one - resid_zero
    sums = fluid_sum(
        allsum_axis(jnp.stack([jnp.sum(diff_one * diff_one), jnp.sum(diff_one * resid_one)]), "slab"),
        side_id,
        side_count - 1,
    )
    step_one = tilde_one - tilde_zero
    rims_base, rims_step = exchange([(plane_of(tilde_one), HALO), (plane_of(step_one), HALO)])
    band_base = band_solve(init_band, force_band.at[:, 0, :].add(rims_base), coef_band, row_ok)
    band_step = band_solve(
        jnp.zeros_like(init_band), jnp.zeros_like(force_band).at[:, 0, :].set(rims_step), coef_band, row_ok
    )
    both = jnp.stack([band_base[:, 0, :], band_step[:, 0, :]])
    traction = PENALTY * jnp.sum(pick[None, :, :, None] * both[:, None], axis=2)
    loaded = live[None] * (jnp.stack([shell_load, jnp.zeros_like(shell_load)]) - traction)
    applied = own_live[None] * jnp.sum(compliance[None] * loaded[:, :, None, :], axis=-1)
    tilde_base, tilde_step = applied[0], applied[1]
    gram_aa, gram_ab = sums[0], sums[1]
    coeff = -gram_ab / (gram_aa + (0.001 * gram_aa + 1e-06))
    disp_two = tilde_one + coeff * step_one
    (deep,) = exchange([(deep + 0.0 * coeff, 2)])
    tilde_two = tilde_base + coeff * tilde_step
    band_two = band_base + coeff * band_step
    deep = lax.cond(
        shell_flag,
        lambda: jnp.zeros((slab_rows,) + deep.shape[1:], jnp.float32),
        lambda: deep_step(
            deep_step(deep, force_deep, coef_deep, ok_one), force_deep[1:-1], coef_deep[1:-1], ok_two
        ),
    )
    resid_two = tilde_two - disp_two
    newer = resid_two - resid_one
    partial = jnp.stack(
        [
            jnp.sum(newer * newer, axis=0),
            jnp.sum(newer * diff_one, axis=0),
            jnp.sum(newer * resid_two, axis=0),
            jnp.sum(diff_one * resid_two, axis=0),
        ]
    )
    patches_here = tilde_two.shape[0]
    outgoing = jnp.concatenate(
        [
            tilde_two,
            tilde_one,
            tilde_zero,
            resid_two,
            partial,
            jnp.where((jnp.arange(line_cells) == 0) & (side_id == 0), gram_aa, 0.0)[None],
        ],
        axis=0,
    )
    gathered = outgoing
    for source in range(side_count - 1):
        gathered = gathered + lax.ppermute(outgoing, "side", [(source, side_count - 1)])
    sums = shell_sum(jnp.sum(gathered[4 * patches_here : 4 * patches_here + 4], axis=1), side_count)
    gram_aa = gathered[4 * patches_here + 4, 0]
    gram_nn, gram_no, proj_new, proj_old = sums[0], sums[1], sums[2], sums[3]
    tilde_two, tilde_one, tilde_zero, resid_two = (
        gathered[k * patches_here : (k + 1) * patches_here] for k in range(4)
    )

    shift_two = 0.001 * (gram_nn + gram_aa) + 1e-06
    diag_new = gram_nn + shift_two
    diag_old = gram_aa + shift_two
    determ = diag_new * diag_old - gram_no * gram_no
    coeff_new = (-proj_new * diag_old + proj_old * gram_no) / determ
    coeff_old = (-proj_old * diag_new + proj_new * gram_no) / determ
    disp_three = (
        tilde_two + coeff_new * (tilde_two - tilde_one) + coeff_old * (tilde_one - tilde_zero)
    )

    flow_state = jnp.concatenate([band_two, deep[:, band_two.shape[1] :]], axis=1)
    disp_next = jnp.where(shell_flag, disp_three, 0.0)[None]
    residual = jnp.where(shell_flag, resid_two, 0.0)[None]
    flow_final = jnp.where(shell_flag, 0.0, flow_state)[None]
    return (disp_next, residual, flow_final)


def solution(mesh):
    return jax.shard_map(
        body,
        mesh=mesh,
        in_specs=(
            P("side", "slab", None, None),
            P("side", "slab", None, None),
            P("side", "slab", None, None),
            P("slab", None, None),
            P("slab", None),
            P("slab", None),
            P("slab"),
            P("slab", None),
            P("slab"),
        ),
        out_specs=(P("side", "slab", None), P("side", "slab", None), P("side", "slab", None, None)),
        check_vma=False,
    )
```
